32 devices in a mesh: grp: 2 (over y), rot: 4 (over z), sub: 2 (over x), ref: 2 (over core).
Axes of the slice: x: 2, y: 2, z: 4, core: 2. Of those that a mesh axis runs over, the one named last changes fastest.
Arguments:
- ligand: bfloat16 [16, 4, 64, 64, 64], P(('grp', 'rot', 'ref'), None, 'sub'), parts along dimension 0, may hold values from -6 to 6
- receptor: float32 [4, 4, 64, 64, 64], P('grp', None, 'rot', 'sub'), parts along dimension 0, may hold values from -6 to 6
- tile_list: int32 [8, 2, 2, 8], P(('grp', 'rot'), 'sub', 'ref'), parts along dimension 0, may hold values from 0 to 255
- tile_owner: int32 [8, 2, 2, 8, 1], P(('grp', 'rot'), 'sub', 'ref'), parts along dimension 0, may hold values from 0 to 7; in each aligned block of 8 rows (0 to 7, 8 to 15, ..., all dimensions but the last counted through in order) at most 2 rows name the same one
- refine_weight: float32 [512, 512], replicated, may hold values from -0.25 to 0.25
Outputs:
- scores: float32 [16, 64, 64, 64], P(('grp', 'rot', 'ref'), 'sub'), parts along dimension 0
- refined: float32 [16, 2, 8, 2, 512], P(('grp', 'rot', 'ref'), 'sub'), parts along dimension 0
The draws below stay inside these ranges and needn't reach their ends.
There are 2 independent parts, one for each index of `grp`. The reference program is written for one: setup_inputs(seed, part) draws one part's arguments, and reference() takes and returns one part's arrays. A program takes and returns all parts, laid end to end along the dimension named above; an argument that names none is the same for every part. Nothing has to cross between parts.
Inputs may be any that keep to these rules, and one draw needn't show every extreme that they name: `tile_owner`: in one device's list no owner is named more than 2 times, and in every draw some device names one owner exactly 2 times.
All inputs are finite; a program needn't handle non-finite values.
Results may differ from the reference program's by a relative error of at most 0.004.
Values may be sent and summed in bfloat16 or wider, within the bound.
No kernel may reach another device: no remote copies, remote signals or barrier semaphores. Data moves between devices by JAX's collectives and lax.ppermute only.
A program may use at most 128 MiB of HBM per device.

```python
import math
import jax
import jax.numpy as jnp
import numpy as np
from jax import lax

GRID = 64
TERMS = 4
ROT_DEV = 1
CAP = 2
TILE = 512
OWNERS = 8
LISTED = 8
ROTATIONS = 8
N_ROT = 4
N_SUB = 2
N_REF = 2


def touch_ends(array, key, smallest, high):
    place = [jax.random.randint(jax.random.fold_in(key, axis), (), 0, length) for axis, length in enumerate(array.shape)]
    longest = array.shape.index(max(array.shape))
    next_to = place[:longest] + [(place[longest] + 1) % array.shape[longest]] + place[longest + 1:]
    return array.at[tuple(place)].set(smallest).at[tuple(next_to)].set(high)


def block_scale(stream_key, dims, pieces, least, top_value):
    gain = 1.0
    for axis_at, blocks in pieces:
        steps = jax.random.uniform(jax.random.fold_in(jax.random.fold_in(stream_key, 6), axis_at), (blocks,), jnp.float32, least / len(pieces), top_value / len(pieces))
        gain = gain * jnp.repeat(jnp.exp(steps), dims[axis_at] // blocks).reshape((-1,) + (1,) * (len(dims) - 1 - axis_at))
    return gain


def routed_block(rng, own, number, rows, count, top, limit, lean):
    order = jax.random.permutation(rng, count)
    heavy_load, ordinary = portions_of(count, rows * top, limit, lean, True), portions_of(count, rows * top, limit, lean, False)
    places = jnp.arange(count)

    def named(sizes, offset_by):
        used = int((sizes > 0).sum())
        fixed = max(1, used // 4)
        shifted = fixed + (places - fixed + offset_by * (used - fixed)) % max(1, count - fixed)
        return jnp.zeros((count,), jnp.int32).at[order[jnp.where(places < fixed, places, shifted)]].set(jnp.asarray(sizes, jnp.int32))

    sizes = jnp.where(number % 4 == 0, named(heavy_load, number // 4), named(ordinary, number - number // 4 - 1))
    mixed = jax.random.permutation(jax.random.fold_in(own, 3), count)
    source_of, sink = mixed[0:count // 2 * 2:2], mixed[1:count // 2 * 2:2]
    margin = jnp.minimum(sizes[source_of] - 1, limit - sizes[sink]) // 2
    margin = jnp.where((source_of == order[0]) | (sink == order[0]) | (sizes[sink] == 0), 0, jnp.maximum(margin, 0))
    shifted = jax.random.randint(jax.random.fold_in(own, 4), (count // 2,), 0, 1 << 20) % (margin + 1)
    sizes = sizes.at[source_of].add(-shifted).at[sink].add(shifted)
    members = jnp.searchsorted(jnp.cumsum(sizes), jnp.arange(rows * top), side="right").astype(jnp.int32)
    table = members.reshape(top, rows).T
    table = table[jax.random.permutation(jax.random.fold_in(own, 1), rows)]
    offset_by = jax.random.randint(jax.random.fold_in(own, 2), (rows, 1), 0, top)
    return jnp.take_along_axis(table, (jnp.arange(top)[None, :] + offset_by) % top, axis=1)


def portions_of(number_of, total, bound, skew, full):
    loads = [(1 << 20) // math.isqrt(standing ** skew) + 1 for standing in range(1, number_of + 1)]
    largest = bound if full else min(bound, max(-(-total // number_of), total * loads[0] // sum(loads)))
    least = 1 if total - largest >= number_of - 1 else 0
    holding, spare = [largest] + [least] * (number_of - 1), total - largest - least * (number_of - 1)
    while spare > 0:
        candidates = [i for i in range(1, number_of) if holding[i] < largest] or [i for i in range(1, number_of) if holding[i] < bound]
        pool, left = sum([loads[i] for i in candidates]), spare
        for i in candidates:
            more = min(bound - holding[i], max(1, left * loads[i] // pool), spare)
            holding[i] = holding[i] + more
            spare = spare - more
    return np.array(holding)


def bell_draw(rng, dims, scale, limit, pieces=(), held_as=jnp.bfloat16):
    gain = block_scale(rng, dims, pieces, -0.22, 0.18) if pieces else 1.0
    result = jax.random.normal(rng, dims, jnp.float32) * scale * gain
    return jnp.minimum(jnp.maximum(result, -limit), limit).astype(held_as)


def setup_inputs(seed: int = 0, part: int = 0) -> dict:
    arg_keys = jax.random.split(jax.random.key(seed), 6)
    part_splits = jax.random.split(jax.random.fold_in(arg_keys[5], part), 6)
    ligand = bell_draw(part_splits[0], (ROTATIONS, TERMS, GRID, GRID, GRID), 1.0, 6.0, ((0, 8), (2, 2)))
    receptor = bell_draw(part_splits[1], (2, TERMS, GRID, GRID, GRID), 1.0, 6.0, ((2, 4), (3, 2)), jnp.float32)
    tile_list = touch_ends(jax.random.randint(part_splits[2], (N_ROT, N_SUB, N_REF, LISTED), 0, ROT_DEV * (GRID // N_SUB) * (GRID // 8)), jax.random.fold_in(part_splits[2], 1), 0, (ROT_DEV * (GRID // N_SUB) * (GRID // 8)) - 1).astype(jnp.int32)
    tile_owner_keys = jax.random.split(jax.random.fold_in(part_splits[3], 1), N_ROT * N_SUB * N_REF * LISTED // LISTED)
    tile_owner_turns = jax.random.permutation(jax.random.fold_in(part_splits[3], 3), N_ROT * N_SUB * N_REF * LISTED // LISTED)
    tile_owner = jax.vmap(lambda own, number: routed_block(jax.random.fold_in(part_splits[3], 2), own, number, LISTED, N_ROT * N_REF, 1, CAP, 2))(tile_owner_keys, tile_owner_turns).reshape((N_ROT, N_SUB, N_REF, LISTED, 1))
    refine_weight = bell_draw(arg_keys[4], (TILE, TILE), TILE ** -0.5, 0.25, (), jnp.float32)
    return dict(ligand=ligand, receptor=receptor, tile_list=tile_list, tile_owner=tile_owner, refine_weight=refine_weight)


def reference(ligand, receptor, tile_list, tile_owner, refine_weight):
    receptor_c = receptor[0] + 1j * receptor[1]

    def one_rotation(volume):
        values = volume.astype(jnp.float32)
        partial_value = jnp.fft.fft2(values, axes=(2, 3))
        p_real, p_imag = lax.optimization_barrier((jnp.real(partial_value).astype(jnp.bfloat16), jnp.imag(partial_value).astype(jnp.bfloat16)))
        partial_value = p_real.astype(jnp.float32) + 1j * p_imag.astype(jnp.float32)
        spectrum = jnp.fft.fft(partial_value, axis=1)
        s_real, s_imag = lax.optimization_barrier((jnp.real(spectrum).astype(jnp.bfloat16), jnp.imag(spectrum).astype(jnp.bfloat16)))
        spectrum = s_real.astype(jnp.float32) + 1j * s_imag.astype(jnp.float32)
        product = jnp.sum(jnp.conj(receptor_c) * spectrum, axis=0)
        return jnp.real(jnp.fft.ifftn(product)).astype(jnp.float32)

    scores = lax.map(one_rotation, ligand)
    slab = GRID // N_SUB
    blocks = GRID // 8
    tiled = scores.reshape(ROTATIONS, GRID, blocks, 8 * GRID)
    rot_index = jnp.arange(N_ROT, dtype=jnp.int32)[:, None, None, None]
    sub_index = jnp.arange(N_SUB, dtype=jnp.int32)[None, :, None, None]
    ref_index = jnp.arange(N_REF, dtype=jnp.int32)[None, None, :, None]
    source = rot_index * N_REF + ref_index
    local_rot = tile_list // (slab * blocks)
    local_x = (tile_list // blocks) % slab
    local_b = tile_list % blocks
    chosen = tiled[(source * ROT_DEV + local_rot).astype(jnp.int32), (sub_index * slab + local_x).astype(jnp.int32), local_b.astype(jnp.int32)]
    owner = tile_owner[..., 0]
    order = jnp.arange(LISTED, dtype=jnp.int32)
    earlier = (owner[..., :, None] == owner[..., None, :]) & (order[None, :] < order[:, None])
    slot = jnp.sum(earlier.astype(jnp.int32), axis=-1).astype(jnp.int32)
    refined_rows = jnp.einsum("abckn,nm->abckm", chosen, refine_weight, precision=lax.Precision.HIGHEST)
    shape = owner.shape
    sub_full = jnp.broadcast_to(sub_index, shape).astype(jnp.int32)
    source_full = jnp.broadcast_to(source, shape).astype(jnp.int32)
    refined = jnp.zeros((OWNERS, N_SUB, OWNERS, CAP, TILE), jnp.float32)
    refined = refined.at[owner, sub_full, source_full, slot].set(refined_rows)
    return scores, refined
```

```python
import math

import jax
import jax.numpy as jnp
from jax import lax
from jax.sharding import PartitionSpec as P

CAP = 2


highest = lax.Precision.HIGHEST


def make_tables(length):
    counter = jnp.arange(length, dtype=jnp.int32)
    phases = counter[:, None] * counter[None, :] % length
    angles = phases.astype(jnp.float32) * (2.0 * math.pi / length)
    return (jnp.cos(angles), jnp.sin(angles))


def forward_table(cos_table, sin_table):
    top = jnp.stack([cos_table, -sin_table], axis=1)
    bottom = jnp.stack([sin_table, cos_table], axis=1)
    return jnp.stack([top, bottom], axis=0)


def inverse_table(cos_table, sin_table):
    top = jnp.stack([cos_table, sin_table], axis=1)
    bottom = jnp.stack([-sin_table, cos_table], axis=1)
    return jnp.stack([top, bottom], axis=0)


def correlate(spectrum, receptor):
    lig_real = spectrum[:, :, 0]
    lig_imag = spectrum[:, :, 1]
    rec_real = receptor[0][None]
    rec_imag = receptor[1][None]
    prod_real = jnp.sum(rec_real * lig_real + rec_imag * lig_imag, axis=1)
    prod_imag = jnp.sum(rec_real * lig_imag - rec_imag * lig_real, axis=1)
    return jnp.stack([prod_real, prod_imag], axis=1)


def gather_receptor(receptor):
    n_ref = lax.axis_size("ref")
    n_rot = lax.axis_size("rot")
    shape = receptor.shape
    share = receptor.astype(jnp.bfloat16).reshape((n_ref, -1))
    mine = lax.dynamic_index_in_dim(share, lax.axis_index("ref"), axis=0, keepdims=False)
    along_rot = lax.all_gather(mine, "rot", axis=0, tiled=False)
    both = lax.all_gather(along_rot, "ref", axis=0, tiled=False)
    both = both.reshape((n_ref, n_rot) + (shape[0] // n_ref,) + shape[1:])
    both = jnp.moveaxis(both, 1, 3).reshape(shape[:2] + (n_rot * shape[2],) + shape[3:])
    return both.astype(jnp.float32)


def local(ligand, receptor, tile_list, tile_owner, refine_weight):
    length = ligand.shape[-1]
    cos_table, sin_table = make_tables(length)
    forward = forward_table(cos_table, sin_table)
    inverse = inverse_table(cos_table, sin_table)
    first_table = jnp.stack([cos_table, -sin_table], axis=1)
    last_table = jnp.stack([cos_table, -sin_table], axis=0)
    values = ligand.astype(jnp.float32)
    along_z = jnp.einsum("rtxyz,zdk->rtdxyk", values, first_table, precision=highest)
    partial_value = jnp.einsum("rtcxyk,cydj->rtdxjk", along_z, forward, precision=highest).astype(
        jnp.bfloat16
    )
    turned = lax.all_to_all(partial_value, "sub", split_axis=4, concat_axis=3, tiled=True).astype(
        jnp.float32
    )
    spectrum = jnp.einsum("rtcxyk,cxdj->rtdjyk", turned, forward, precision=highest).astype(
        jnp.bfloat16
    )
    whole_receptor = gather_receptor(receptor)
    product = correlate(lax.optimization_barrier(spectrum).astype(jnp.float32), whole_receptor)
    back_x = jnp.einsum("rcxyk,cxdj->rdjyk", product, inverse, precision=highest)
    returned = lax.all_to_all(back_x, "sub", split_axis=2, concat_axis=3, tiled=True)
    back_y = jnp.einsum("rcxyk,cydj->rdxjk", returned, inverse, precision=highest)
    scores = jnp.einsum("rcxjk,ckz->rxjz", back_y, last_table, precision=highest) / float(length**3)
    tile_cells = 8 * length
    tile_rows = scores.reshape(-1, tile_cells)
    listing = tile_list.reshape(-1)
    owners = tile_owner.reshape(-1)
    listed = listing.shape[0]
    chosen = tile_rows[listing]
    owner_count = lax.axis_size(("rot", "ref"))
    order = jnp.arange(listed, dtype=jnp.int32)
    earlier = (owners[:, None] == owners[None, :]) & (order[None, :] < order[:, None])
    slot = jnp.sum(earlier.astype(jnp.int32), axis=1)
    target = owners * CAP + slot
    placing = (jnp.arange(owner_count * CAP, dtype=jnp.int32)[:, None] == target[None, :]).astype(
        jnp.float32
    )
    done = jnp.dot(chosen, refine_weight, precision=highest)
    packed = jnp.dot(placing, done, precision=highest).reshape(owner_count, CAP, tile_cells)
    refined = lax.all_to_all(packed, ("rot", "ref"), split_axis=0, concat_axis=0, tiled=True)
    return (scores, refined.reshape(1, 1, owner_count, CAP, tile_cells))


def solution(mesh):
    in_specs = (
        P(("grp", "rot", "ref"), None, "sub", None, None),
        P("grp", None, "rot", "sub", None),
        P(("grp", "rot"), "sub", "ref", None),
        P(("grp", "rot"), "sub", "ref", None, None),
        P(),
    )
    out_specs = (
        P(("grp", "rot", "ref"), "sub", None, None),
        P(("grp", "rot", "ref"), "sub", None, None, None),
    )
    return jax.shard_map(local, mesh=mesh, in_specs=in_specs, out_specs=out_specs, check_vma=False)
```

```python
import math

import jax
import jax.numpy as jnp
from jax import lax
from jax.sharding import PartitionSpec as P

CAP = 2


highest = lax.Precision.HIGHEST


def make_tables(length):
    counter = jnp.arange(length, dtype=jnp.int32)
    phases = counter[:, None] * counter[None, :] % length
    angles = phases.astype(jnp.float32) * (2.0 * math.pi / length)
    return (jnp.cos(angles), jnp.sin(angles))


def forward_table(cos_table, sin_table):
    top = jnp.stack([cos_table, -sin_table], axis=1)
    bottom = jnp.stack([sin_table, cos_table], axis=1)
    return jnp.stack([top, bottom], axis=0)


def inverse_table(cos_table, sin_table):
    top = jnp.stack([cos_table, sin_table], axis=1)
    bottom = jnp.stack([-sin_table, cos_table], axis=1)
    return jnp.stack([top, bottom], axis=0)


def correlate(spectrum, receptor):
    lig_real = spectrum[:, :, 0]
    lig_imag = spectrum[:, :, 1]
    rec_real = receptor[0][None]
    rec_imag = receptor[1][None]
    prod_real = jnp.sum(rec_real * lig_real + rec_imag * lig_imag, axis=1)
    prod_imag = jnp.sum(rec_real * lig_imag - rec_imag * lig_real, axis=1)
    return jnp.stack([prod_real, prod_imag], axis=1)


def gather_by_shifts(piece, axis):
    count = lax.axis_size(axis)
    me = lax.axis_index(axis)
    whole = jnp.zeros((count,) + piece.shape, piece.dtype)
    whole = lax.dynamic_update_index_in_dim(whole, piece, me, axis=0)
    for shift in range(1, count):
        pairs = [(k, (k + shift) % count) for k in range(count)]
        got = lax.ppermute(piece, axis, pairs)
        whole = lax.dynamic_update_index_in_dim(whole, got, (me - shift) % count, axis=0)
    return whole


def gather_receptor(receptor):
    n_ref = lax.axis_size("ref")
    n_rot = lax.axis_size("rot")
    shape = receptor.shape
    share = receptor.astype(jnp.bfloat16).reshape((n_ref, -1))
    mine = lax.dynamic_index_in_dim(share, lax.axis_index("ref"), axis=0, keepdims=False)
    along_rot = gather_by_shifts(mine, "rot")
    both = gather_by_shifts(along_rot, "ref")
    both = both.reshape((n_ref, n_rot) + (shape[0] // n_ref,) + shape[1:])
    both = jnp.moveaxis(both, 1, 3).reshape(shape[:2] + (n_rot * shape[2],) + shape[3:])
    return both.astype(jnp.float32)


def local(ligand, receptor, tile_list, tile_owner, refine_weight):
    length = ligand.shape[-1]
    cos_table, sin_table = make_tables(length)
    forward = forward_table(cos_table, sin_table)
    inverse = inverse_table(cos_table, sin_table)
    first_table = jnp.stack([cos_table, -sin_table], axis=1)
    last_table = jnp.stack([cos_table, -sin_table], axis=0)
    values = ligand.astype(jnp.float32)
    along_z = jnp.einsum("rtxyz,zdk->rtdxyk", values, first_table, precision=highest)
    partial_value = jnp.einsum("rtcxyk,cydj->rtdxjk", along_z, forward, precision=highest).astype(
        jnp.bfloat16
    )
    turned = lax.all_to_all(partial_value, "sub", split_axis=4, concat_axis=3, tiled=True).astype(
        jnp.float32
    )
    spectrum = jnp.einsum("rtcxyk,cxdj->rtdjyk", turned, forward, precision=highest).astype(
        jnp.bfloat16
    )
    whole_receptor = gather_receptor(receptor)
    product = correlate(lax.optimization_barrier(spectrum).astype(jnp.float32), whole_receptor)
    back_x = jnp.einsum("rcxyk,cxdj->rdjyk", product, inverse, precision=highest)
    returned = lax.all_to_all(back_x, "sub", split_axis=2, concat_axis=3, tiled=True)
    back_y = jnp.einsum("rcxyk,cydj->rdxjk", returned, inverse, precision=highest)
    scores = jnp.einsum("rcxjk,ckz->rxjz", back_y, last_table, precision=highest) / float(length**3)
    tile_cells = 8 * length
    tile_rows = scores.reshape(-1, tile_cells)
    listing = tile_list.reshape(-1)
    owners = tile_owner.reshape(-1)
    listed = listing.shape[0]
    chosen = tile_rows[listing]
    owner_count = lax.axis_size(("rot", "ref"))
    order = jnp.arange(listed, dtype=jnp.int32)
    earlier = (owners[:, None] == owners[None, :]) & (order[None, :] < order[:, None])
    slot = jnp.sum(earlier.astype(jnp.int32), axis=1)
    target = owners * CAP + slot
    placing = (jnp.arange(owner_count * CAP, dtype=jnp.int32)[:, None] == target[None, :]).astype(
        jnp.float32
    )
    done = jnp.dot(chosen, refine_weight, precision=highest)
    packed = jnp.dot(placing, done, precision=highest).reshape(owner_count, CAP, tile_cells)
    refined = lax.all_to_all(packed, ("rot", "ref"), split_axis=0, concat_axis=0, tiled=True)
    return (scores, refined.reshape(1, 1, owner_count, CAP, tile_cells))


def solution(mesh):
    in_specs = (
        P(("grp", "rot", "ref"), None, "sub", None, None),
        P("grp", None, "rot", "sub", None),
        P(("grp", "rot"), "sub", "ref", None),
        P(("grp", "rot"), "sub", "ref", None, None),
        P(),
    )
    out_specs = (
        P(("grp", "rot", "ref"), "sub", None, None),
        P(("grp", "rot", "ref"), "sub", None, None, None),
    )
    return jax.shard_map(local, mesh=mesh, in_specs=in_specs, out_specs=out_specs, check_vma=False)
```

```python
import math

import jax
import jax.numpy as jnp
from jax import lax
from jax.sharding import PartitionSpec as P

CAP = 2


highest = lax.Precision.HIGHEST


def make_tables(length):
    counter = jnp.arange(length, dtype=jnp.int32)
    phases = counter[:, None] * counter[None, :] % length
    angles = phases.astype(jnp.float32) * (2.0 * math.pi / length)
    return (jnp.cos(angles), jnp.sin(angles))


def forward_table(cos_table, sin_table):
    top = jnp.stack([cos_table, -sin_table], axis=1)
    bottom = jnp.stack([sin_table, cos_table], axis=1)
    return jnp.stack([top, bottom], axis=0)


def inverse_table(cos_table, sin_table):
    top = jnp.stack([cos_table, sin_table], axis=1)
    bottom = jnp.stack([-sin_table, cos_table], axis=1)
    return jnp.stack([top, bottom], axis=0)


def gather_by_shifts(piece, axis):
    count = lax.axis_size(axis)
    me = lax.axis_index(axis)
    pieces = [piece]
    for shift in range(1, count):
        pairs = [(k, (k + shift) % count) for k in range(count)]
        pieces.append(lax.ppermute(piece, axis, pairs))
    doubled = jnp.stack(pieces[::-1] * 2)
    return lax.dynamic_slice_in_dim(doubled, (count - 1 - me) % count, count, axis=0)


def gather_receptor(receptor):
    shape = receptor.shape
    n_ref = lax.axis_size("ref")
    rows = shape[0] // n_ref
    lanes = 128 if (shape[3] * shape[4]) % 128 == 0 else shape[4]
    share = receptor.reshape((n_ref, rows) + shape[1:])
    mine = lax.dynamic_index_in_dim(share, lax.axis_index("ref"), axis=0, keepdims=False)
    mine = mine.reshape((rows,) + shape[1:3] + (-1, lanes)).astype(jnp.bfloat16)
    along_rot = gather_by_shifts(mine, "rot")
    both = gather_by_shifts(along_rot, "ref")
    both = jnp.moveaxis(both, 2, 1).reshape((n_ref * rows, both.shape[1]) + shape[1:])
    return both.astype(jnp.float32)


def correlate(spectrum, receptor):
    n_rot = receptor.shape[1]
    kx_local = receptor.shape[3]
    spec = spectrum.reshape(spectrum.shape[:3] + (n_rot, kx_local) + spectrum.shape[4:])
    lig_real = spec[:, :, 0]
    lig_imag = spec[:, :, 1]
    rec_real = jnp.swapaxes(receptor[0], 0, 1)[None]
    rec_imag = jnp.swapaxes(receptor[1], 0, 1)[None]
    prod_real = jnp.sum(rec_real * lig_real + rec_imag * lig_imag, axis=1)
    prod_imag = jnp.sum(rec_real * lig_imag - rec_imag * lig_real, axis=1)
    out = jnp.stack([prod_real, prod_imag], axis=1)
    return out.reshape(out.shape[:2] + (n_rot * kx_local,) + out.shape[4:])


def local(ligand, receptor, tile_list, tile_owner, refine_weight):
    length = ligand.shape[-1]
    cos_table, sin_table = make_tables(length)
    forward = forward_table(cos_table, sin_table)
    inverse = inverse_table(cos_table, sin_table)
    first_table = jnp.stack([cos_table, -sin_table], axis=1)
    last_table = jnp.stack([cos_table, -sin_table], axis=0)
    values = ligand.astype(jnp.float32)
    along_z = jnp.einsum("rtxyz,zdk->rtdxyk", values, first_table, precision=highest)
    partial_value = jnp.einsum("rtcxyk,cydj->rtdxjk", along_z, forward, precision=highest).astype(
        jnp.bfloat16
    )
    turned = lax.all_to_all(partial_value, "sub", split_axis=4, concat_axis=3, tiled=True).astype(
        jnp.float32
    )
    spectrum = jnp.einsum("rtcxyk,cxdj->rtdjyk", turned, forward, precision=highest).astype(
        jnp.bfloat16
    )
    whole_receptor = gather_receptor(receptor)
    product = correlate(lax.optimization_barrier(spectrum).astype(jnp.float32), whole_receptor)
    back_x = jnp.einsum("rcxyk,cxdj->rdjyk", product, inverse, precision=highest)
    returned = lax.all_to_all(back_x, "sub", split_axis=2, concat_axis=3, tiled=True)
    back_y = jnp.einsum("rcxyk,cydj->rdxjk", returned, inverse, precision=highest)
    scores = jnp.einsum("rcxjk,ckz->rxjz", back_y, last_table, precision=highest) / float(length**3)
    tile_cells = 8 * length
    tile_rows = scores.reshape(-1, tile_cells)
    listing = tile_list.reshape(-1)
    owners = tile_owner.reshape(-1)
    listed = listing.shape[0]
    chosen = tile_rows[listing]
    owner_count = lax.axis_size(("rot", "ref"))
    order = jnp.arange(listed, dtype=jnp.int32)
    earlier = (owners[:, None] == owners[None, :]) & (order[None, :] < order[:, None])
    slot = jnp.sum(earlier.astype(jnp.int32), axis=1)
    target = owners * CAP + slot
    placing = (jnp.arange(owner_count * CAP, dtype=jnp.int32)[:, None] == target[None, :]).astype(
        jnp.float32
    )
    done = jnp.dot(chosen, refine_weight, precision=highest)
    packed = jnp.dot(placing, done, precision=highest).reshape(owner_count, CAP, tile_cells)
    refined = lax.all_to_all(packed, ("rot", "ref"), split_axis=0, concat_axis=0, tiled=True)
    return (scores, refined.reshape(1, 1, owner_count, CAP, tile_cells))


def solution(mesh):
    in_specs = (
        P(("grp", "rot", "ref"), None, "sub", None, None),
        P("grp", None, "rot", "sub", None),
        P(("grp", "rot"), "sub", "ref", None),
        P(("grp", "rot"), "sub", "ref", None, None),
        P(),
    )
    out_specs = (
        P(("grp", "rot", "ref"), "sub", None, None),
        P(("grp", "rot", "ref"), "sub", None, None, None),
    )
    return jax.shard_map(local, mesh=mesh, in_specs=in_specs, out_specs=out_specs, check_vma=False)
```

```python
import math

import jax
import jax.numpy as jnp
from jax import lax
from jax.sharding import PartitionSpec as P

CAP = 2


highest = lax.Precision.HIGHEST


def make_tables(length):
    counter = jnp.arange(length, dtype=jnp.int32)
    phases = counter[:, None] * counter[None, :] % length
    angles = phases.astype(jnp.float32) * (2.0 * math.pi / length)
    return (jnp.cos(angles), jnp.sin(angles))


def swap_halves(values):
    half = values.shape[-1] // 2
    return jnp.concatenate([values[..., half:], values[..., :half]], axis=-1)


def half_signs(length, first, second):
    return jnp.concatenate(
        [jnp.full((length,), first, jnp.float32), jnp.full((length,), second, jnp.float32)]
    )


def combine(stacked, axis, signs):
    cos_part = lax.index_in_dim(stacked, 0, axis, keepdims=False)
    sin_part = lax.index_in_dim(stacked, 1, axis, keepdims=False)
    return cos_part + swap_halves(sin_part) * signs


def gather_by_shifts(piece, axis):
    count = lax.axis_size(axis)
    me = lax.axis_index(axis)
    pieces = [piece]
    for shift in range(1, count):
        pairs = [(k, (k + shift) % count) for k in range(count)]
        pieces.append(lax.ppermute(piece, axis, pairs))
    doubled = jnp.stack(pieces[::-1] * 2)
    return lax.dynamic_slice_in_dim(doubled, (count - 1 - me) % count, count, axis=0)


def gather_receptor(receptor):
    _, terms, kx_local, ky_local, kz = receptor.shape
    n_ref = lax.axis_size("ref")
    n_rot = lax.axis_size("rot")
    rows = ky_local // n_ref
    block = lax.dynamic_slice_in_dim(receptor, lax.axis_index("ref") * rows, rows, axis=3)
    mine = jnp.concatenate([block[0], block[1]], axis=-1).astype(jnp.bfloat16)
    along_rot = gather_by_shifts(mine, "rot")
    both = gather_by_shifts(along_rot, "ref")
    both = jnp.transpose(both, (2, 1, 3, 0, 4, 5))
    return both.reshape(terms, n_rot * kx_local, ky_local, 2 * kz)


def local(ligand, receptor, tile_list, tile_owner, refine_weight):
    rots, terms, x_local, ny, nz = ligand.shape
    length = nz
    n_sub = lax.axis_size("sub")
    y_local = ny // n_sub
    cos_table, sin_table = make_tables(length)
    forward_signs = half_signs(length, 1.0, -1.0)
    inverse_signs = half_signs(length, -1.0, 1.0)
    pair = jnp.stack([cos_table, sin_table])

    along_z = jnp.einsum(
        "rtxyz,zl->rtxyl",
        ligand.astype(jnp.float32),
        jnp.concatenate([cos_table, -sin_table], axis=1),
        precision=highest,
    )
    along_y = jnp.einsum("ejy,rtxyl->rtxejl", pair, along_z, precision=highest)
    partial_value = combine(along_y, 3, forward_signs).astype(jnp.bfloat16)
    sending = jnp.moveaxis(
        partial_value.reshape(rots, terms, x_local, n_sub, y_local, 2 * length), 3, 0
    )
    turned = lax.all_to_all(sending, "sub", split_axis=0, concat_axis=0, tiled=True)
    turned = turned.astype(jnp.float32)
    pair_x = pair.reshape(2, length, n_sub, x_local)
    along_x = sum(
        jnp.einsum("ekx,rtxjl->rtekjl", pair_x[:, :, s], turned[s], precision=highest)
        for s in range(n_sub)
    )
    spectrum = combine(along_x, 2, forward_signs).astype(jnp.bfloat16)
    spectrum = lax.optimization_barrier(spectrum).astype(jnp.float32)

    whole_receptor = gather_receptor(receptor).astype(jnp.float32)
    half = length
    rec_real = jnp.concatenate([whole_receptor[..., :half]] * 2, axis=-1)
    rec_imag = jnp.concatenate([whole_receptor[..., half:], -whole_receptor[..., half:]], axis=-1)
    product = jnp.sum(rec_real[None] * spectrum + rec_imag[None] * swap_halves(spectrum), axis=1)

    back_x = jnp.einsum("exk,rkjl->exrjl", pair, product, precision=highest)
    back_x = combine(back_x, 0, inverse_signs)
    back_x = back_x.reshape(n_sub, x_local, rots, y_local, 2 * length)
    returned = lax.all_to_all(back_x, "sub", split_axis=0, concat_axis=0, tiled=True)
    pair_y = pair.reshape(2, length, n_sub, y_local)
    back_y = sum(
        jnp.einsum("eyj,xrjl->rxeyl", pair_y[:, :, s], returned[s], precision=highest)
        for s in range(n_sub)
    )
    back_y = combine(back_y, 2, inverse_signs)
    last_table = jnp.concatenate([cos_table, -sin_table], axis=0)
    scores = jnp.einsum("rxyl,lz->rxyz", back_y, last_table, precision=highest) / float(length**3)

    tile_cells = 8 * length
    tile_rows = scores.reshape(-1, tile_cells)
    listing = tile_list.reshape(-1)
    owners = tile_owner.reshape(-1)
    listed = listing.shape[0]
    chosen = tile_rows[listing]
    owner_count = lax.axis_size(("rot", "ref"))
    order = jnp.arange(listed, dtype=jnp.int32)
    earlier = (owners[:, None] == owners[None, :]) & (order[None, :] < order[:, None])
    slot = jnp.sum(earlier.astype(jnp.int32), axis=1)
    target = owners * CAP + slot
    placing = (jnp.arange(owner_count * CAP, dtype=jnp.int32)[:, None] == target[None, :]).astype(
        jnp.float32
    )
    done = jnp.dot(chosen, refine_weight, precision=highest)
    packed = jnp.dot(placing, done, precision=highest).reshape(owner_count, CAP, tile_cells)
    refined = lax.all_to_all(packed, ("rot", "ref"), split_axis=0, concat_axis=0, tiled=True)
    return (scores, refined.reshape(1, 1, owner_count, CAP, tile_cells))


def solution(mesh):
    in_specs = (
        P(("grp", "rot", "ref"), None, "sub", None, None),
        P("grp", None, "rot", "sub", None),
        P(("grp", "rot"), "sub", "ref", None),
        P(("grp", "rot"), "sub", "ref", None, None),
        P(),
    )
    out_specs = (
        P(("grp", "rot", "ref"), "sub", None, None),
        P(("grp", "rot", "ref"), "sub", None, None, None),
    )
    return jax.shard_map(local, mesh=mesh, in_specs=in_specs, out_specs=out_specs, check_vma=False)
```

```python
import math

import jax
import jax.numpy as jnp
from jax import lax
from jax.experimental import pallas as pl
from jax.experimental.pallas import tpu as pltpu
from jax.sharding import PartitionSpec as P

CAP = 2


highest = lax.Precision.HIGHEST


def make_tables(length):
    counter = jnp.arange(length, dtype=jnp.int32)
    phases = counter[:, None] * counter[None, :] % length
    angles = phases.astype(jnp.float32) * (2.0 * math.pi / length)
    return (jnp.cos(angles), jnp.sin(angles))


def swap_halves(values):
    half = values.shape[-1] // 2
    return jnp.concatenate([values[..., half:], values[..., :half]], axis=-1)


def half_signs(length, first, second):
    return jnp.concatenate(
        [jnp.full((length,), first, jnp.float32), jnp.full((length,), second, jnp.float32)]
    )


def combine(stacked, axis, signs):
    cos_part = lax.index_in_dim(stacked, 0, axis, keepdims=False)
    sin_part = lax.index_in_dim(stacked, 1, axis, keepdims=False)
    return cos_part + swap_halves(sin_part) * signs


def gather_by_shifts(piece, axis):
    count = lax.axis_size(axis)
    me = lax.axis_index(axis)
    pieces = [piece]
    for shift in range(1, count):
        pairs = [(k, (k + shift) % count) for k in range(count)]
        pieces.append(lax.ppermute(piece, axis, pairs))
    doubled = jnp.stack(pieces[::-1] * 2)
    return lax.dynamic_slice_in_dim(doubled, (count - 1 - me) % count, count, axis=0)


def gather_receptor(receptor):
    _, terms, kx_local, ky_local, kz = receptor.shape
    n_ref = lax.axis_size("ref")
    n_rot = lax.axis_size("rot")
    rows = ky_local // n_ref
    block = lax.dynamic_slice_in_dim(receptor, lax.axis_index("ref") * rows, rows, axis=3)
    mine = jnp.concatenate([block[0], block[1]], axis=-1).astype(jnp.bfloat16)
    along_rot = gather_by_shifts(mine, "rot")
    both = gather_by_shifts(along_rot, "ref")
    both = jnp.transpose(both, (2, 1, 3, 0, 4, 5))
    return both.reshape(terms, n_rot * kx_local, ky_local, 2 * kz)


def product_kernel(spec_ref, rec_ref, out_ref):
    lanes = out_ref.shape[-1]
    half = lanes // 2
    total = None
    for term in range(spec_ref.shape[0]):
        spec = spec_ref[term].astype(jnp.float32)
        rec = rec_ref[term].astype(jnp.float32)
        low = lax.broadcasted_iota(jnp.int32, rec.shape, 1) < half
        rec_turned = pltpu.roll(rec, half, 1)
        rec_real = jnp.where(low, rec, rec_turned)
        rec_imag = jnp.where(low, rec_turned, -rec)
        part = rec_real * spec + rec_imag * pltpu.roll(spec, half, 1)
        total = part if total is None else total + part
    out_ref[...] = total


def correlate(spectrum, receptor):
    rots, terms, kx, ky, lanes = spectrum.shape
    rows = kx * ky
    block = min(rows, 512)
    spec = spectrum.reshape(rots, terms, rows, lanes)
    rec = receptor.reshape(terms, rows, lanes)
    out = pl.pallas_call(
        product_kernel,
        grid=(rots, rows // block),
        in_specs=[
            pl.BlockSpec((None, terms, block, lanes), lambda r, i: (r, 0, i, 0)),
            pl.BlockSpec((terms, block, lanes), lambda r, i: (0, i, 0)),
        ],
        out_specs=pl.BlockSpec((None, block, lanes), lambda r, i: (r, i, 0)),
        out_shape=jax.ShapeDtypeStruct((rots, rows, lanes), jnp.float32),
        cost_estimate=pl.CostEstimate(
            flops=8 * rots * terms * rows * lanes,
            bytes_accessed=2 * (rots + 1) * terms * rows * lanes + 4 * rots * rows * lanes,
            transcendentals=0,
        ),
    )(spec, rec)
    return out.reshape(rots, kx, ky, lanes)


def local(ligand, receptor, tile_list, tile_owner, refine_weight):
    rots, terms, x_local, ny, nz = ligand.shape
    length = nz
    n_sub = lax.axis_size("sub")
    y_local = ny // n_sub
    cos_table, sin_table = make_tables(length)
    forward_signs = half_signs(length, 1.0, -1.0)
    inverse_signs = half_signs(length, -1.0, 1.0)
    pair = jnp.stack([cos_table, sin_table])

    along_z = jnp.einsum(
        "rtxyz,zl->rtxyl",
        ligand.astype(jnp.float32),
        jnp.concatenate([cos_table, -sin_table], axis=1),
        precision=highest,
    )
    along_y = jnp.einsum("ejy,rtxyl->rtxejl", pair, along_z, precision=highest)
    partial_value = combine(along_y, 3, forward_signs).astype(jnp.bfloat16)
    sending = jnp.moveaxis(
        partial_value.reshape(rots, terms, x_local, n_sub, y_local, 2 * length), 3, 0
    )
    turned = lax.all_to_all(sending, "sub", split_axis=0, concat_axis=0, tiled=True)
    turned = turned.astype(jnp.float32)
    pair_x = pair.reshape(2, length, n_sub, x_local)
    along_x = sum(
        jnp.einsum("ekx,rtxjl->rtekjl", pair_x[:, :, s], turned[s], precision=highest)
        for s in range(n_sub)
    )
    spectrum = combine(along_x, 2, forward_signs).astype(jnp.bfloat16)

    whole_receptor = gather_receptor(receptor)
    product = correlate(spectrum, whole_receptor)

    back_x = jnp.einsum("exk,rkjl->exrjl", pair, product, precision=highest)
    back_x = combine(back_x, 0, inverse_signs)
    back_x = back_x.reshape(n_sub, x_local, rots, y_local, 2 * length)
    returned = lax.all_to_all(back_x, "sub", split_axis=0, concat_axis=0, tiled=True)
    pair_y = pair.reshape(2, length, n_sub, y_local)
    back_y = sum(
        jnp.einsum("eyj,xrjl->rxeyl", pair_y[:, :, s], returned[s], precision=highest)
        for s in range(n_sub)
    )
    back_y = combine(back_y, 2, inverse_signs)
    last_table = jnp.concatenate([cos_table, -sin_table], axis=0)
    scores = jnp.einsum("rxyl,lz->rxyz", back_y, last_table, precision=highest) / float(length**3)

    tile_cells = 8 * length
    tile_rows = scores.reshape(-1, tile_cells)
    listing = tile_list.reshape(-1)
    owners = tile_owner.reshape(-1)
    listed = listing.shape[0]
    chosen = tile_rows[listing]
    owner_count = lax.axis_size(("rot", "ref"))
    order = jnp.arange(listed, dtype=jnp.int32)
    earlier = (owners[:, None] == owners[None, :]) & (order[None, :] < order[:, None])
    slot = jnp.sum(earlier.astype(jnp.int32), axis=1)
    target = owners * CAP + slot
    placing = (jnp.arange(owner_count * CAP, dtype=jnp.int32)[:, None] == target[None, :]).astype(
        jnp.float32
    )
    done = jnp.dot(chosen, refine_weight, precision=highest)
    packed = jnp.dot(placing, done, precision=highest).reshape(owner_count, CAP, tile_cells)
    refined = lax.all_to_all(packed, ("rot", "ref"), split_axis=0, concat_axis=0, tiled=True)
    return (scores, refined.reshape(1, 1, owner_count, CAP, tile_cells))


def solution(mesh):
    in_specs = (
        P(("grp", "rot", "ref"), None, "sub", None, None),
        P("grp", None, "rot", "sub", None),
        P(("grp", "rot"), "sub", "ref", None),
        P(("grp", "rot"), "sub", "ref", None, None),
        P(),
    )
    out_specs = (
        P(("grp", "rot", "ref"), "sub", None, None),
        P(("grp", "rot", "ref"), "sub", None, None, None),
    )
    return jax.shard_map(local, mesh=mesh, in_specs=in_specs, out_specs=out_specs, check_vma=False)
```

```python
import math

import jax
import jax.numpy as jnp
from jax import lax
from jax.experimental import pallas as pl
from jax.experimental.pallas import tpu as pltpu
from jax.sharding import PartitionSpec as P

CAP = 2


highest = lax.Precision.HIGH


def make_tables(length):
    counter = jnp.arange(length, dtype=jnp.int32)
    phases = counter[:, None] * counter[None, :] % length
    angles = phases.astype(jnp.float32) * (2.0 * math.pi / length)
    return (jnp.cos(angles), jnp.sin(angles))


def swap_halves(values):
    half = values.shape[-1] // 2
    return jnp.concatenate([values[..., half:], values[..., :half]], axis=-1)


def half_signs(length, first, second):
    return jnp.concatenate(
        [jnp.full((length,), first, jnp.float32), jnp.full((length,), second, jnp.float32)]
    )


def combine(stacked, axis, signs):
    cos_part = lax.index_in_dim(stacked, 0, axis, keepdims=False)
    sin_part = lax.index_in_dim(stacked, 1, axis, keepdims=False)
    return cos_part + swap_halves(sin_part) * signs


def gather_by_shifts(piece, axis):
    count = lax.axis_size(axis)
    me = lax.axis_index(axis)
    pieces = [piece]
    for shift in range(1, count):
        pairs = [(k, (k + shift) % count) for k in range(count)]
        pieces.append(lax.ppermute(piece, axis, pairs))
    doubled = jnp.stack(pieces[::-1] * 2)
    return lax.dynamic_slice_in_dim(doubled, (count - 1 - me) % count, count, axis=0)


def gather_receptor(receptor):
    _, terms, kx_local, ky_local, kz = receptor.shape
    n_ref = lax.axis_size("ref")
    n_rot = lax.axis_size("rot")
    rows = ky_local // n_ref
    block = lax.dynamic_slice_in_dim(receptor, lax.axis_index("ref") * rows, rows, axis=3)
    mine = jnp.concatenate([block[0], block[1]], axis=-1).astype(jnp.bfloat16)
    along_rot = gather_by_shifts(mine, "rot")
    both = gather_by_shifts(along_rot, "ref")
    both = jnp.transpose(both, (2, 1, 3, 0, 4, 5))
    return both.reshape(terms, n_rot * kx_local, ky_local, 2 * kz)


def product_kernel(spec_ref, rec_ref, out_ref):
    lanes = out_ref.shape[-1]
    half = lanes // 2
    total = None
    for term in range(spec_ref.shape[0]):
        spec = spec_ref[term].astype(jnp.float32)
        rec = rec_ref[term].astype(jnp.float32)
        low = lax.broadcasted_iota(jnp.int32, rec.shape, 1) < half
        rec_turned = pltpu.roll(rec, half, 1)
        rec_real = jnp.where(low, rec, rec_turned)
        rec_imag = jnp.where(low, rec_turned, -rec)
        part = rec_real * spec + rec_imag * pltpu.roll(spec, half, 1)
        total = part if total is None else total + part
    out_ref[...] = total


def correlate(spectrum, receptor):
    rots, terms, kx, ky, lanes = spectrum.shape
    rows = kx * ky
    block = min(rows, 512)
    spec = spectrum.reshape(rots, terms, rows, lanes)
    rec = receptor.reshape(terms, rows, lanes)
    out = pl.pallas_call(
        product_kernel,
        grid=(rots, rows // block),
        in_specs=[
            pl.BlockSpec((None, terms, block, lanes), lambda r, i: (r, 0, i, 0)),
            pl.BlockSpec((terms, block, lanes), lambda r, i: (0, i, 0)),
        ],
        out_specs=pl.BlockSpec((None, block, lanes), lambda r, i: (r, i, 0)),
        out_shape=jax.ShapeDtypeStruct((rots, rows, lanes), jnp.float32),
        cost_estimate=pl.CostEstimate(
            flops=8 * rots * terms * rows * lanes,
            bytes_accessed=2 * (rots + 1) * terms * rows * lanes + 4 * rots * rows * lanes,
            transcendentals=0,
        ),
    )(spec, rec)
    return out.reshape(rots, kx, ky, lanes)


def local(ligand, receptor, tile_list, tile_owner, refine_weight):
    rots, terms, x_local, ny, nz = ligand.shape
    length = nz
    n_sub = lax.axis_size("sub")
    y_local = ny // n_sub
    cos_table, sin_table = make_tables(length)
    forward_signs = half_signs(length, 1.0, -1.0)
    inverse_signs = half_signs(length, -1.0, 1.0)
    pair = jnp.stack([cos_table, sin_table])

    along_z = jnp.einsum(
        "rtxyz,zl->rtxyl",
        ligand.astype(jnp.float32),
        jnp.concatenate([cos_table, -sin_table], axis=1),
        precision=highest,
    )
    along_y = jnp.einsum("ejy,rtxyl->rtxejl", pair, along_z, precision=highest)
    partial_value = combine(along_y, 3, forward_signs).astype(jnp.bfloat16)
    sending = jnp.moveaxis(
        partial_value.reshape(rots, terms, x_local, n_sub, y_local, 2 * length), 3, 0
    )
    turned = lax.all_to_all(sending, "sub", split_axis=0, concat_axis=0, tiled=True)
    turned = turned.astype(jnp.float32)
    pair_x = pair.reshape(2, length, n_sub, x_local)
    along_x = sum(
        jnp.einsum("ekx,rtxjl->rtekjl", pair_x[:, :, s], turned[s], precision=highest)
        for s in range(n_sub)
    )
    spectrum = combine(along_x, 2, forward_signs).astype(jnp.bfloat16)

    whole_receptor = gather_receptor(receptor)
    product = correlate(spectrum, whole_receptor)

    back_x = jnp.einsum("exk,rkjl->exrjl", pair, product, precision=highest)
    back_x = combine(back_x, 0, inverse_signs)
    back_x = back_x.reshape(n_sub, x_local, rots, y_local, 2 * length)
    returned = lax.all_to_all(back_x, "sub", split_axis=0, concat_axis=0, tiled=True)
    pair_y = pair.reshape(2, length, n_sub, y_local)
    back_y = sum(
        jnp.einsum("eyj,xrjl->rxeyl", pair_y[:, :, s], returned[s], precision=highest)
        for s in range(n_sub)
    )
    back_y = combine(back_y, 2, inverse_signs)
    last_table = jnp.concatenate([cos_table, -sin_table], axis=0)
    scores = jnp.einsum("rxyl,lz->rxyz", back_y, last_table, precision=highest) / float(length**3)

    tile_cells = 8 * length
    tile_rows = scores.reshape(-1, tile_cells)
    listing = tile_list.reshape(-1)
    owners = tile_owner.reshape(-1)
    listed = listing.shape[0]
    chosen = tile_rows[listing]
    owner_count = lax.axis_size(("rot", "ref"))
    order = jnp.arange(listed, dtype=jnp.int32)
    earlier = (owners[:, None] == owners[None, :]) & (order[None, :] < order[:, None])
    slot = jnp.sum(earlier.astype(jnp.int32), axis=1)
    target = owners * CAP + slot
    placing = (jnp.arange(owner_count * CAP, dtype=jnp.int32)[:, None] == target[None, :]).astype(
        jnp.float32
    )
    done = jnp.dot(chosen, refine_weight, precision=highest)
    packed = jnp.dot(placing, done, precision=highest).reshape(owner_count, CAP, tile_cells)
    refined = lax.all_to_all(packed, ("rot", "ref"), split_axis=0, concat_axis=0, tiled=True)
    return (scores, refined.reshape(1, 1, owner_count, CAP, tile_cells))


def solution(mesh):
    in_specs = (
        P(("grp", "rot", "ref"), None, "sub", None, None),
        P("grp", None, "rot", "sub", None),
        P(("grp", "rot"), "sub", "ref", None),
        P(("grp", "rot"), "sub", "ref", None, None),
        P(),
    )
    out_specs = (
        P(("grp", "rot", "ref"), "sub", None, None),
        P(("grp", "rot", "ref"), "sub", None, None, None),
    )
    return jax.shard_map(local, mesh=mesh, in_specs=in_specs, out_specs=out_specs, check_vma=False)
```

```python
import math

import jax
import jax.numpy as jnp
from jax import lax
from jax.experimental import pallas as pl
from jax.experimental.pallas import tpu as pltpu
from jax.sharding import PartitionSpec as P

CAP = 2


highest = lax.Precision.HIGH


def make_tables(length):
    counter = jnp.arange(length, dtype=jnp.int32)
    phases = counter[:, None] * counter[None, :] % length
    angles = phases.astype(jnp.float32) * (2.0 * math.pi / length)
    return (jnp.cos(angles), jnp.sin(angles))


def swap_halves(values):
    half = values.shape[-1] // 2
    return jnp.concatenate([values[..., half:], values[..., :half]], axis=-1)


def half_signs(length, first, second):
    return jnp.concatenate(
        [jnp.full((length,), first, jnp.float32), jnp.full((length,), second, jnp.float32)]
    )


def combine(stacked, axis, signs):
    cos_part = lax.index_in_dim(stacked, 0, axis, keepdims=False)
    sin_part = lax.index_in_dim(stacked, 1, axis, keepdims=False)
    return cos_part + swap_halves(sin_part) * signs


def gather_by_shifts(piece, axis):
    count = lax.axis_size(axis)
    me = lax.axis_index(axis)
    pieces = [piece]
    for shift in range(1, count):
        pairs = [(k, (k + shift) % count) for k in range(count)]
        pieces.append(lax.ppermute(piece, axis, pairs))
    doubled = jnp.stack(pieces[::-1] * 2)
    return lax.dynamic_slice_in_dim(doubled, (count - 1 - me) % count, count, axis=0)


def gather_receptor(receptor):
    _, terms, kx_local, ky_local, kz = receptor.shape
    n_ref = lax.axis_size("ref")
    n_rot = lax.axis_size("rot")
    rows = ky_local // n_ref
    block = lax.dynamic_slice_in_dim(receptor, lax.axis_index("ref") * rows, rows, axis=3)
    mine = jnp.concatenate([block[0], block[1]], axis=-1).astype(jnp.bfloat16)
    along_rot = gather_by_shifts(mine, "rot")
    both = gather_by_shifts(along_rot, "ref")
    both = jnp.transpose(both, (2, 1, 3, 0, 4, 5))
    return both.reshape(terms, n_rot * kx_local, ky_local, 2 * kz)


def product_kernel(*refs):
    *spec_refs, rec_ref, out_ref = refs
    lanes = out_ref.shape[-1]
    half = lanes // 2
    total = None
    term = 0
    for spec_ref in spec_refs:
        for inner in range(spec_ref.shape[0]):
            spec = spec_ref[inner].astype(jnp.float32)
            rec = rec_ref[term].astype(jnp.float32)
            term += 1
            low = lax.broadcasted_iota(jnp.int32, rec.shape, 1) < half
            rec_turned = pltpu.roll(rec, half, 1)
            rec_real = jnp.where(low, rec, rec_turned)
            rec_imag = jnp.where(low, rec_turned, -rec)
            part = rec_real * spec + rec_imag * pltpu.roll(spec, half, 1)
            total = part if total is None else total + part
    out_ref[...] = total


def correlate(spectra, receptor):
    rots, _, kx, ky, lanes = spectra[0].shape
    terms = receptor.shape[0]
    rows = kx * ky
    block = min(rows, 512)
    specs = [part.reshape(rots, part.shape[1], rows, lanes) for part in spectra]
    rec = receptor.reshape(terms, rows, lanes)
    out = pl.pallas_call(
        product_kernel,
        grid=(rots, rows // block),
        in_specs=[
            pl.BlockSpec((None, part.shape[1], block, lanes), lambda r, i: (r, 0, i, 0))
            for part in specs
        ]
        + [pl.BlockSpec((terms, block, lanes), lambda r, i: (0, i, 0))],
        out_specs=pl.BlockSpec((None, block, lanes), lambda r, i: (r, i, 0)),
        out_shape=jax.ShapeDtypeStruct((rots, rows, lanes), jnp.float32),
        cost_estimate=pl.CostEstimate(
            flops=8 * rots * terms * rows * lanes,
            bytes_accessed=2 * (rots + 1) * terms * rows * lanes + 4 * rots * rows * lanes,
            transcendentals=0,
        ),
    )(*specs, rec)
    return out.reshape(rots, kx, ky, lanes)


def local(ligand, receptor, tile_list, tile_owner, refine_weight):
    rots, terms, x_local, ny, nz = ligand.shape
    length = nz
    n_sub = lax.axis_size("sub")
    y_local = ny // n_sub
    cos_table, sin_table = make_tables(length)
    forward_signs = half_signs(length, 1.0, -1.0)
    inverse_signs = half_signs(length, -1.0, 1.0)
    pair = jnp.stack([cos_table, sin_table])

    chunks = 2 if terms % 2 == 0 else 1
    part_terms = terms // chunks
    pair_x = pair.reshape(2, length, n_sub, x_local)
    z_table = jnp.concatenate([cos_table, -sin_table], axis=1)
    values = ligand.astype(jnp.float32)
    spectra = []
    for chunk in range(chunks):
        part = values[:, chunk * part_terms:(chunk + 1) * part_terms]
        along_z = jnp.einsum("rtxyz,zl->rtxyl", part, z_table, precision=highest)
        along_y = jnp.einsum("ejy,rtxyl->rtxejl", pair, along_z, precision=highest)
        partial_value = combine(along_y, 3, forward_signs).astype(jnp.bfloat16)
        sending = jnp.moveaxis(
            partial_value.reshape(rots, part_terms, x_local, n_sub, y_local, 2 * length), 3, 0
        )
        turned = lax.all_to_all(sending, "sub", split_axis=0, concat_axis=0, tiled=True)
        turned = turned.astype(jnp.float32)
        along_x = sum(
            jnp.einsum("ekx,rtxjl->rtekjl", pair_x[:, :, s], turned[s], precision=highest)
            for s in range(n_sub)
        )
        spectra.append(combine(along_x, 2, forward_signs).astype(jnp.bfloat16))

    whole_receptor = gather_receptor(receptor)
    product = correlate(spectra, whole_receptor)

    back_x = jnp.einsum("exk,rkjl->exrjl", pair, product, precision=highest)
    back_x = combine(back_x, 0, inverse_signs)
    back_x = back_x.reshape(n_sub, x_local, rots, y_local, 2 * length)
    returned = lax.all_to_all(back_x, "sub", split_axis=0, concat_axis=0, tiled=True)
    pair_y = pair.reshape(2, length, n_sub, y_local)
    back_y = sum(
        jnp.einsum("eyj,xrjl->rxeyl", pair_y[:, :, s], returned[s], precision=highest)
        for s in range(n_sub)
    )
    back_y = combine(back_y, 2, inverse_signs)
    last_table = jnp.concatenate([cos_table, -sin_table], axis=0)
    scores = jnp.einsum("rxyl,lz->rxyz", back_y, last_table, precision=highest) / float(length**3)

    tile_cells = 8 * length
    tile_rows = scores.reshape(-1, tile_cells)
    listing = tile_list.reshape(-1)
    owners = tile_owner.reshape(-1)
    listed = listing.shape[0]
    chosen = tile_rows[listing]
    owner_count = lax.axis_size(("rot", "ref"))
    order = jnp.arange(listed, dtype=jnp.int32)
    earlier = (owners[:, None] == owners[None, :]) & (order[None, :] < order[:, None])
    slot = jnp.sum(earlier.astype(jnp.int32), axis=1)
    target = owners * CAP + slot
    placing = (jnp.arange(owner_count * CAP, dtype=jnp.int32)[:, None] == target[None, :]).astype(
        jnp.float32
    )
    done = jnp.dot(chosen, refine_weight, precision=highest)
    packed = jnp.dot(placing, done, precision=highest).reshape(owner_count, CAP, tile_cells)
    refined = lax.all_to_all(packed, ("rot", "ref"), split_axis=0, concat_axis=0, tiled=True)
    return (scores, refined.reshape(1, 1, owner_count, CAP, tile_cells))


def solution(mesh):
    in_specs = (
        P(("grp", "rot", "ref"), None, "sub", None, None),
        P("grp", None, "rot", "sub", None),
        P(("grp", "rot"), "sub", "ref", None),
        P(("grp", "rot"), "sub", "ref", None, None),
        P(),
    )
    out_specs = (
        P(("grp", "rot", "ref"), "sub", None, None),
        P(("grp", "rot", "ref"), "sub", None, None, None),
    )
    return jax.shard_map(local, mesh=mesh, in_specs=in_specs, out_specs=out_specs, check_vma=False)
```

```python
import functools
import math

import jax
import jax.numpy as jnp
from jax import lax
from jax.experimental import pallas as pl
from jax.experimental.pallas import tpu as pltpu
from jax.sharding import PartitionSpec as P

CAP = 2


highest = lax.Precision.HIGH


def make_tables(length):
    counter = jnp.arange(length, dtype=jnp.int32)
    phases = counter[:, None] * counter[None, :] % length
    angles = phases.astype(jnp.float32) * (2.0 * math.pi / length)
    return (jnp.cos(angles), jnp.sin(angles))


def combine_kernel(in_ref, out_ref, *, first, second):
    batch, _, rows, lanes = in_ref.shape
    split = out_ref.shape[0]
    part = rows // split
    half = lanes // 2
    cos_part = in_ref[:, 0].reshape(batch * rows, lanes)
    sin_part = in_ref[:, 1].reshape(batch * rows, lanes)
    low = lax.broadcasted_iota(jnp.int32, cos_part.shape, 1) < half
    signs = jnp.where(low, first, second).astype(jnp.float32)
    result = (cos_part + pltpu.roll(sin_part, half, 1) * signs).reshape(batch, rows, lanes)
    for piece in range(split):
        out_ref[piece] = result[:, piece * part:(piece + 1) * part].astype(out_ref.dtype)


def combine_call(stacked, first, second, split, dtype):
    batch, _, rows, lanes = stacked.shape
    block = max(b for b in range(1, 17) if batch % b == 0)
    part = rows // split
    return pl.pallas_call(
        functools.partial(combine_kernel, first=first, second=second),
        grid=(batch // block,),
        in_specs=[pl.BlockSpec((block, 2, rows, lanes), lambda i: (i, 0, 0, 0))],
        out_specs=pl.BlockSpec((split, block, part, lanes), lambda i: (0, i, 0, 0)),
        out_shape=jax.ShapeDtypeStruct((split, batch, part, lanes), dtype),
        cost_estimate=pl.CostEstimate(
            flops=3 * batch * rows * lanes,
            bytes_accessed=(8 + jnp.dtype(dtype).itemsize) * batch * rows * lanes,
            transcendentals=0,
        ),
    )(stacked)


def gather_by_shifts(piece, axis):
    count = lax.axis_size(axis)
    me = lax.axis_index(axis)
    pieces = [piece]
    for shift in range(1, count):
        pairs = [(k, (k + shift) % count) for k in range(count)]
        pieces.append(lax.ppermute(piece, axis, pairs))
    doubled = jnp.stack(pieces[::-1] * 2)
    return lax.dynamic_slice_in_dim(doubled, (count - 1 - me) % count, count, axis=0)


def gather_receptor(receptor):
    _, terms, kx_local, ky_local, kz = receptor.shape
    n_ref = lax.axis_size("ref")
    n_rot = lax.axis_size("rot")
    rows = ky_local // n_ref
    block = lax.dynamic_slice_in_dim(receptor, lax.axis_index("ref") * rows, rows, axis=3)
    mine = jnp.concatenate([block[0], block[1]], axis=-1).astype(jnp.bfloat16)
    mine = jnp.swapaxes(mine, 1, 2)
    along_rot = gather_by_shifts(mine, "rot")
    both = gather_by_shifts(along_rot, "ref")
    both = jnp.transpose(both, (2, 0, 3, 1, 4, 5))
    return both.reshape(terms, ky_local, n_rot * kx_local, 2 * kz)


def product_kernel(*refs):
    *spec_refs, rec_ref, out_ref = refs
    lanes = out_ref.shape[-1]
    half = lanes // 2
    total = None
    term = 0
    for spec_ref in spec_refs:
        for inner in range(spec_ref.shape[0]):
            spec = spec_ref[inner].astype(jnp.float32)
            rec = rec_ref[term].astype(jnp.float32)
            term += 1
            low = lax.broadcasted_iota(jnp.int32, rec.shape, 1) < half
            rec_turned = pltpu.roll(rec, half, 1)
            rec_real = jnp.where(low, rec, rec_turned)
            rec_imag = jnp.where(low, rec_turned, -rec)
            part = rec_real * spec + rec_imag * pltpu.roll(spec, half, 1)
            total = part if total is None else total + part
    out_ref[...] = total


def correlate(spectra, receptor):
    rots, _, kx, ky, lanes = spectra[0].shape
    terms = receptor.shape[0]
    rows = kx * ky
    block = min(rows, 512)
    specs = [part.reshape(rots, part.shape[1], rows, lanes) for part in spectra]
    rec = receptor.reshape(terms, rows, lanes)
    out = pl.pallas_call(
        product_kernel,
        grid=(rots, rows // block),
        in_specs=[
            pl.BlockSpec((None, part.shape[1], block, lanes), lambda r, i: (r, 0, i, 0))
            for part in specs
        ]
        + [pl.BlockSpec((terms, block, lanes), lambda r, i: (0, i, 0))],
        out_specs=pl.BlockSpec((None, block, lanes), lambda r, i: (r, i, 0)),
        out_shape=jax.ShapeDtypeStruct((rots, rows, lanes), jnp.float32),
        cost_estimate=pl.CostEstimate(
            flops=8 * rots * terms * rows * lanes,
            bytes_accessed=2 * (rots + 1) * terms * rows * lanes + 4 * rots * rows * lanes,
            transcendentals=0,
        ),
    )(*specs, rec)
    return out.reshape(rots, kx, ky, lanes)


def local(ligand, receptor, tile_list, tile_owner, refine_weight):
    rots, terms, x_local, ny, nz = ligand.shape
    length = nz
    n_sub = lax.axis_size("sub")
    y_local = ny // n_sub
    cos_table, sin_table = make_tables(length)
    pair = jnp.stack([cos_table, sin_table])

    chunks = 2 if terms % 2 == 0 else 1
    part_terms = terms // chunks
    pair_x = pair.reshape(2, length, n_sub, x_local)
    z_table = jnp.concatenate([cos_table, -sin_table], axis=1)
    values = ligand.astype(jnp.float32)
    spectra = []
    for chunk in range(chunks):
        part = values[:, chunk * part_terms:(chunk + 1) * part_terms]
        along_z = jnp.einsum("rtxyz,zl->rtxyl", part, z_table, precision=highest)
        along_y = jnp.einsum("ejy,rtxyl->rtxejl", pair, along_z, precision=highest)
        sending = combine_call(
            along_y.reshape(-1, 2, ny, 2 * length), 1.0, -1.0, n_sub, jnp.bfloat16
        ).reshape(n_sub, rots, part_terms, x_local, y_local, 2 * length)
        turned = lax.all_to_all(sending, "sub", split_axis=0, concat_axis=0, tiled=True)
        turned = turned.astype(jnp.float32)
        along_x = sum(
            jnp.einsum("ekx,rtxjl->rtjekl", pair_x[:, :, s], turned[s], precision=highest)
            for s in range(n_sub)
        )
        spectrum = combine_call(
            along_x.reshape(-1, 2, length, 2 * length), 1.0, -1.0, 1, jnp.bfloat16
        )
        spectra.append(spectrum.reshape(rots, part_terms, y_local, length, 2 * length))

    whole_receptor = gather_receptor(receptor)
    product = correlate(spectra, whole_receptor)

    back_x = jnp.einsum("exk,rjkl->xrejl", pair, product, precision=highest)
    back_x = combine_call(back_x.reshape(-1, 2, y_local, 2 * length), -1.0, 1.0, 1, jnp.float32)
    back_x = back_x.reshape(n_sub, x_local, rots, y_local, 2 * length)
    returned = lax.all_to_all(back_x, "sub", split_axis=0, concat_axis=0, tiled=True)
    pair_y = pair.reshape(2, length, n_sub, y_local)
    back_y = sum(
        jnp.einsum("eyj,xrjl->rxeyl", pair_y[:, :, s], returned[s], precision=highest)
        for s in range(n_sub)
    )
    back_y = combine_call(back_y.reshape(-1, 2, ny, 2 * length), -1.0, 1.0, 1, jnp.float32)
    back_y = back_y.reshape(rots, x_local, ny, 2 * length)
    last_table = jnp.concatenate([cos_table, -sin_table], axis=0)
    scores = jnp.einsum("rxyl,lz->rxyz", back_y, last_table, precision=highest) / float(length**3)

    tile_cells = 8 * length
    tile_rows = scores.reshape(-1, tile_cells)
    listing = tile_list.reshape(-1)
    owners = tile_owner.reshape(-1)
    listed = listing.shape[0]
    chosen = tile_rows[listing]
    owner_count = lax.axis_size(("rot", "ref"))
    order = jnp.arange(listed, dtype=jnp.int32)
    earlier = (owners[:, None] == owners[None, :]) & (order[None, :] < order[:, None])
    slot = jnp.sum(earlier.astype(jnp.int32), axis=1)
    target = owners * CAP + slot
    placing = (jnp.arange(owner_count * CAP, dtype=jnp.int32)[:, None] == target[None, :]).astype(
        jnp.float32
    )
    done = jnp.dot(chosen, refine_weight, precision=highest)
    packed = jnp.dot(placing, done, precision=highest).reshape(owner_count, CAP, tile_cells)
    refined = lax.all_to_all(packed, ("rot", "ref"), split_axis=0, concat_axis=0, tiled=True)
    return (scores, refined.reshape(1, 1, owner_count, CAP, tile_cells))


def solution(mesh):
    in_specs = (
        P(("grp", "rot", "ref"), None, "sub", None, None),
        P("grp", None, "rot", "sub", None),
        P(("grp", "rot"), "sub", "ref", None),
        P(("grp", "rot"), "sub", "ref", None, None),
        P(),
    )
    out_specs = (
        P(("grp", "rot", "ref"), "sub", None, None),
        P(("grp", "rot", "ref"), "sub", None, None, None),
    )
    return jax.shard_map(local, mesh=mesh, in_specs=in_specs, out_specs=out_specs, check_vma=False)
```

```python
import functools
import math

import jax
import jax.numpy as jnp
from jax import lax
from jax.experimental import pallas as pl
from jax.experimental.pallas import tpu as pltpu
from jax.sharding import PartitionSpec as P

CAP = 2


highest = lax.Precision.HIGH


def make_tables(length):
    counter = jnp.arange(length, dtype=jnp.int32)
    phases = counter[:, None] * counter[None, :] % length
    angles = phases.astype(jnp.float32) * (2.0 * math.pi / length)
    return (jnp.cos(angles), jnp.sin(angles))


def combine_kernel(in_ref, out_ref, *, first, second):
    batch, _, rows, lanes = in_ref.shape
    split = out_ref.shape[0]
    part = rows // split
    half = lanes // 2
    cos_part = in_ref[:, 0].reshape(batch * rows, lanes)
    sin_part = in_ref[:, 1].reshape(batch * rows, lanes)
    low = lax.broadcasted_iota(jnp.int32, (1, lanes), 1) < half
    signs = jnp.where(low, first, second).astype(jnp.float32)
    result = (cos_part + pltpu.roll(sin_part, half, 1) * signs).reshape(batch, rows, lanes)
    for piece in range(split):
        out_ref[piece] = result[:, piece * part:(piece + 1) * part].astype(out_ref.dtype)


def combine_call(stacked, first, second, split, dtype):
    batch, _, rows, lanes = stacked.shape
    block = max(b for b in range(1, 33) if batch % b == 0)
    part = rows // split
    return pl.pallas_call(
        functools.partial(combine_kernel, first=first, second=second),
        grid=(batch // block,),
        in_specs=[pl.BlockSpec((block, 2, rows, lanes), lambda i: (i, 0, 0, 0))],
        out_specs=pl.BlockSpec((split, block, part, lanes), lambda i: (0, i, 0, 0)),
        out_shape=jax.ShapeDtypeStruct((split, batch, part, lanes), dtype),
        cost_estimate=pl.CostEstimate(
            flops=3 * batch * rows * lanes,
            bytes_accessed=(8 + jnp.dtype(dtype).itemsize) * batch * rows * lanes,
            transcendentals=0,
        ),
    )(stacked)


def gather_by_shifts(piece, axis):
    count = lax.axis_size(axis)
    me = lax.axis_index(axis)
    pieces = [piece]
    for shift in range(1, count):
        pairs = [(k, (k + shift) % count) for k in range(count)]
        pieces.append(lax.ppermute(piece, axis, pairs))
    doubled = jnp.stack(pieces[::-1] * 2)
    return lax.dynamic_slice_in_dim(doubled, (count - 1 - me) % count, count, axis=0)


def gather_receptor(receptor):
    _, terms, kx_local, ky_local, kz = receptor.shape
    n_ref = lax.axis_size("ref")
    n_rot = lax.axis_size("rot")
    rows = ky_local // n_ref
    block = lax.dynamic_slice_in_dim(receptor, lax.axis_index("ref") * rows, rows, axis=3)
    mine = jnp.concatenate([block[0], block[1]], axis=-1).astype(jnp.bfloat16)
    mine = jnp.swapaxes(mine, 1, 2)
    along_rot = gather_by_shifts(mine, "rot")
    both = gather_by_shifts(along_rot, "ref")
    both = jnp.transpose(both, (2, 0, 3, 1, 4, 5))
    return both.reshape(terms, ky_local, n_rot * kx_local, 2 * kz)


def product_kernel(*refs):
    *spec_refs, rec_ref, out_ref = refs
    lanes = out_ref.shape[-1]
    half = lanes // 2
    total = None
    term = 0
    for spec_ref in spec_refs:
        for inner in range(spec_ref.shape[0]):
            spec = spec_ref[inner].astype(jnp.float32)
            rec = rec_ref[term].astype(jnp.float32)
            term += 1
            low = lax.broadcasted_iota(jnp.int32, (1, lanes), 1) < half
            rec_turned = pltpu.roll(rec, half, 1)
            rec_real = jnp.where(low, rec, rec_turned)
            rec_imag = jnp.where(low, rec_turned, -rec)
            part = rec_real * spec + rec_imag * pltpu.roll(spec, half, 1)
            total = part if total is None else total + part
    out_ref[...] = total


def correlate(spectra, receptor):
    rots, _, kx, ky, lanes = spectra[0].shape
    terms = receptor.shape[0]
    rows = kx * ky
    block = min(rows, 512)
    specs = [part.reshape(rots, part.shape[1], rows, lanes) for part in spectra]
    rec = receptor.reshape(terms, rows, lanes)
    out = pl.pallas_call(
        product_kernel,
        grid=(rots, rows // block),
        in_specs=[
            pl.BlockSpec((None, part.shape[1], block, lanes), lambda r, i: (r, 0, i, 0))
            for part in specs
        ]
        + [pl.BlockSpec((terms, block, lanes), lambda r, i: (0, i, 0))],
        out_specs=pl.BlockSpec((None, block, lanes), lambda r, i: (r, i, 0)),
        out_shape=jax.ShapeDtypeStruct((rots, rows, lanes), jnp.float32),
        cost_estimate=pl.CostEstimate(
            flops=8 * rots * terms * rows * lanes,
            bytes_accessed=2 * (rots + 1) * terms * rows * lanes + 4 * rots * rows * lanes,
            transcendentals=0,
        ),
    )(*specs, rec)
    return out.reshape(rots, kx, ky, lanes)


def local(ligand, receptor, tile_list, tile_owner, refine_weight):
    rots, terms, x_local, ny, nz = ligand.shape
    length = nz
    n_sub = lax.axis_size("sub")
    y_local = ny // n_sub
    cos_table, sin_table = make_tables(length)
    pair = jnp.stack([cos_table, sin_table])

    chunks = 2 if terms % 2 == 0 else 1
    part_terms = terms // chunks
    pair_x = pair.reshape(2, length, n_sub, x_local)
    z_table = jnp.concatenate([cos_table, -sin_table], axis=1)
    values = ligand.astype(jnp.float32)
    spectra = []
    for chunk in range(chunks):
        part = values[:, chunk * part_terms:(chunk + 1) * part_terms]
        along_z = jnp.einsum("rtxyz,zl->rtxyl", part, z_table, precision=highest)
        along_y = jnp.einsum("ejy,rtxyl->rtxejl", pair, along_z, precision=highest)
        sending = combine_call(
            along_y.reshape(-1, 2, ny, 2 * length), 1.0, -1.0, n_sub, jnp.bfloat16
        ).reshape(n_sub, rots, part_terms, x_local, y_local, 2 * length)
        turned = lax.all_to_all(sending, "sub", split_axis=0, concat_axis=0, tiled=True)
        turned = turned.astype(jnp.float32)
        along_x = sum(
            jnp.einsum("ekx,rtxjl->rtjekl", pair_x[:, :, s], turned[s], precision=highest)
            for s in range(n_sub)
        )
        spectrum = combine_call(
            along_x.reshape(-1, 2, length, 2 * length), 1.0, -1.0, 1, jnp.bfloat16
        )
        spectra.append(spectrum.reshape(rots, part_terms, y_local, length, 2 * length))

    whole_receptor = gather_receptor(receptor)
    product = correlate(spectra, whole_receptor)

    back_x = jnp.einsum("exk,rjkl->xrejl", pair, product, precision=highest)
    back_x = combine_call(back_x.reshape(-1, 2, y_local, 2 * length), -1.0, 1.0, 1, jnp.float32)
    back_x = back_x.reshape(n_sub, x_local, rots, y_local, 2 * length)
    returned = lax.all_to_all(back_x, "sub", split_axis=0, concat_axis=0, tiled=True)
    pair_y = pair.reshape(2, length, n_sub, y_local)
    back_y = sum(
        jnp.einsum("eyj,xrjl->rxeyl", pair_y[:, :, s], returned[s], precision=highest)
        for s in range(n_sub)
    )
    back_y = combine_call(back_y.reshape(-1, 2, ny, 2 * length), -1.0, 1.0, 1, jnp.float32)
    back_y = back_y.reshape(rots, x_local, ny, 2 * length)
    last_table = jnp.concatenate([cos_table, -sin_table], axis=0)
    scores = jnp.einsum("rxyl,lz->rxyz", back_y, last_table, precision=highest) / float(length**3)

    tile_cells = 8 * length
    tile_rows = scores.reshape(-1, tile_cells)
    listing = tile_list.reshape(-1)
    owners = tile_owner.reshape(-1)
    listed = listing.shape[0]
    chosen = tile_rows[listing]
    owner_count = lax.axis_size(("rot", "ref"))
    order = jnp.arange(listed, dtype=jnp.int32)
    earlier = (owners[:, None] == owners[None, :]) & (order[None, :] < order[:, None])
    slot = jnp.sum(earlier.astype(jnp.int32), axis=1)
    target = owners * CAP + slot
    placing = (jnp.arange(owner_count * CAP, dtype=jnp.int32)[:, None] == target[None, :]).astype(
        jnp.float32
    )
    done = jnp.dot(chosen, refine_weight, precision=highest)
    packed = jnp.dot(placing, done, precision=highest).reshape(owner_count, CAP, tile_cells)
    refined = lax.all_to_all(packed, ("rot", "ref"), split_axis=0, concat_axis=0, tiled=True)
    return (scores, refined.reshape(1, 1, owner_count, CAP, tile_cells))


def solution(mesh):
    in_specs = (
        P(("grp", "rot", "ref"), None, "sub", None, None),
        P("grp", None, "rot", "sub", None),
        P(("grp", "rot"), "sub", "ref", None),
        P(("grp", "rot"), "sub", "ref", None, None),
        P(),
    )
    out_specs = (
        P(("grp", "rot", "ref"), "sub", None, None),
        P(("grp", "rot", "ref"), "sub", None, None, None),
    )
    return jax.shard_map(local, mesh=mesh, in_specs=in_specs, out_specs=out_specs, check_vma=False)
```

```python
import functools
import math

import jax
import jax.numpy as jnp
from jax import lax
from jax.experimental import pallas as pl
from jax.experimental.pallas import tpu as pltpu
from jax.sharding import PartitionSpec as P

CAP = 2


highest = lax.Precision.HIGH


def make_tables(length):
    counter = jnp.arange(length, dtype=jnp.int32)
    phases = counter[:, None] * counter[None, :] % length
    angles = phases.astype(jnp.float32) * (2.0 * math.pi / length)
    return (jnp.cos(angles), jnp.sin(angles))


def combine_kernel(in_ref, out_ref, *, first, second):
    batch, _, rows, lanes = in_ref.shape
    split = out_ref.shape[0]
    part = rows // split
    half = lanes // 2
    cos_part = in_ref[:, 0].reshape(batch * rows, lanes)
    sin_part = in_ref[:, 1].reshape(batch * rows, lanes)
    low = lax.broadcasted_iota(jnp.int32, (1, lanes), 1) < half
    signs = jnp.where(low, first, second).astype(jnp.float32)
    result = (cos_part + pltpu.roll(sin_part, half, 1) * signs).reshape(batch, rows, lanes)
    for piece in range(split):
        out_ref[piece] = result[:, piece * part:(piece + 1) * part].astype(out_ref.dtype)


def combine_call(stacked, first, second, split, dtype):
    batch, _, rows, lanes = stacked.shape
    block = max(b for b in range(1, 33) if batch % b == 0)
    part = rows // split
    return pl.pallas_call(
        functools.partial(combine_kernel, first=first, second=second),
        grid=(batch // block,),
        in_specs=[pl.BlockSpec((block, 2, rows, lanes), lambda i: (i, 0, 0, 0))],
        out_specs=pl.BlockSpec((split, block, part, lanes), lambda i: (0, i, 0, 0)),
        out_shape=jax.ShapeDtypeStruct((split, batch, part, lanes), dtype),
        cost_estimate=pl.CostEstimate(
            flops=3 * batch * rows * lanes,
            bytes_accessed=(8 + jnp.dtype(dtype).itemsize) * batch * rows * lanes,
            transcendentals=0,
        ),
    )(stacked)


def gather_by_shifts(piece, axis):
    count = lax.axis_size(axis)
    me = lax.axis_index(axis)
    pieces = [piece]
    for shift in range(1, count):
        pairs = [(k, (k + shift) % count) for k in range(count)]
        pieces.append(lax.ppermute(piece, axis, pairs))
    doubled = jnp.stack(pieces[::-1] * 2)
    return lax.dynamic_slice_in_dim(doubled, (count - 1 - me) % count, count, axis=0)


def gather_receptor(receptor):
    _, terms, kx_local, ky_local, kz = receptor.shape
    n_ref = lax.axis_size("ref")
    n_rot = lax.axis_size("rot")
    rows = ky_local // n_ref
    block = lax.dynamic_slice_in_dim(receptor, lax.axis_index("ref") * rows, rows, axis=3)
    mine = jnp.concatenate([block[0], block[1]], axis=-1).astype(jnp.bfloat16)
    mine = jnp.swapaxes(mine, 1, 2)
    along_rot = gather_by_shifts(mine, "rot")
    both = gather_by_shifts(along_rot, "ref")
    both = jnp.transpose(both, (2, 0, 3, 1, 4, 5))
    return both.reshape(terms, ky_local, n_rot * kx_local, 2 * kz)


def product_kernel(*refs):
    *spec_refs, rec_ref, out_ref = refs
    lanes = out_ref.shape[-1]
    half = lanes // 2
    total = None
    term = 0
    for spec_ref in spec_refs:
        for inner in range(spec_ref.shape[0]):
            spec = spec_ref[inner].astype(jnp.float32)
            rec = rec_ref[term].astype(jnp.float32)
            term += 1
            low = lax.broadcasted_iota(jnp.int32, (1, lanes), 1) < half
            rec_turned = pltpu.roll(rec, half, 1)
            rec_real = jnp.where(low, rec, rec_turned)
            rec_imag = jnp.where(low, rec_turned, -rec)
            part = rec_real * spec + rec_imag * pltpu.roll(spec, half, 1)
            total = part if total is None else total + part
    out_ref[...] = total


def correlate(spectra, receptor):
    rots, _, kx, ky, lanes = spectra[0].shape
    terms = receptor.shape[0]
    rows = kx * ky
    block = min(rows, 512)
    specs = [part.reshape(rots, part.shape[1], rows, lanes) for part in spectra]
    rec = receptor.reshape(terms, rows, lanes)
    out = pl.pallas_call(
        product_kernel,
        grid=(rots, rows // block),
        in_specs=[
            pl.BlockSpec((None, part.shape[1], block, lanes), lambda r, i: (r, 0, i, 0))
            for part in specs
        ]
        + [pl.BlockSpec((terms, block, lanes), lambda r, i: (0, i, 0))],
        out_specs=pl.BlockSpec((None, block, lanes), lambda r, i: (r, i, 0)),
        out_shape=jax.ShapeDtypeStruct((rots, rows, lanes), jnp.float32),
        cost_estimate=pl.CostEstimate(
            flops=8 * rots * terms * rows * lanes,
            bytes_accessed=2 * (rots + 1) * terms * rows * lanes + 4 * rots * rows * lanes,
            transcendentals=0,
        ),
    )(*specs, rec)
    return out.reshape(rots, kx, ky, lanes)


def local(ligand, receptor, tile_list, tile_owner, refine_weight):
    rots, terms, x_local, ny, nz = ligand.shape
    length = nz
    n_sub = lax.axis_size("sub")
    y_local = ny // n_sub
    cos_table, sin_table = make_tables(length)
    pair = jnp.stack([cos_table, sin_table])

    chunks = 2 if terms % 2 == 0 else 1
    part_terms = terms // chunks
    pair_x = pair.reshape(2, length, n_sub, x_local)
    z_table = jnp.concatenate([cos_table, -sin_table], axis=1)
    values = ligand.astype(jnp.float32)
    spectra = []
    for chunk in range(chunks):
        part = values[:, chunk * part_terms:(chunk + 1) * part_terms]
        along_z = jnp.einsum("rtxyz,zl->rtxyl", part, z_table, precision=highest)
        along_y = jnp.einsum("ejy,rtxyl->rtxejl", pair, along_z, precision=highest)
        sending = combine_call(
            along_y.reshape(-1, 2, ny, 2 * length), 1.0, -1.0, n_sub, jnp.bfloat16
        ).reshape(n_sub, rots, part_terms, x_local, y_local, 2 * length)
        turned = lax.all_to_all(sending, "sub", split_axis=0, concat_axis=0, tiled=True)
        turned = turned.astype(jnp.float32)
        along_x = sum(
            jnp.einsum("ekx,rtxjl->rtjekl", pair_x[:, :, s], turned[s], precision=highest)
            for s in range(n_sub)
        )
        spectrum = combine_call(
            along_x.reshape(-1, 2, length, 2 * length), 1.0, -1.0, 1, jnp.bfloat16
        )
        spectra.append(spectrum.reshape(rots, part_terms, y_local, length, 2 * length))

    whole_receptor = gather_receptor(receptor)
    product = correlate(spectra, whole_receptor)

    halves = 2 if y_local % 16 == 0 else 1
    rows_half = y_local // halves
    pair_y = pair.reshape(2, length, n_sub, y_local)
    back_y = 0.0
    for h in range(halves):
        rows = slice(h * rows_half, (h + 1) * rows_half)
        back_x = jnp.einsum("exk,rjkl->xrejl", pair, product[:, rows], precision=highest)
        back_x = combine_call(
            back_x.reshape(-1, 2, rows_half, 2 * length), -1.0, 1.0, 1, jnp.float32
        )
        back_x = back_x.reshape(n_sub, x_local, rots, rows_half, 2 * length)
        returned = lax.all_to_all(back_x, "sub", split_axis=0, concat_axis=0, tiled=True)
        back_y = back_y + sum(
            jnp.einsum("eyj,xrjl->rxeyl", pair_y[:, :, s, rows], returned[s], precision=highest)
            for s in range(n_sub)
        )
    back_y = combine_call(back_y.reshape(-1, 2, ny, 2 * length), -1.0, 1.0, 1, jnp.float32)
    back_y = back_y.reshape(rots, x_local, ny, 2 * length)
    last_table = jnp.concatenate([cos_table, -sin_table], axis=0)
    scores = jnp.einsum("rxyl,lz->rxyz", back_y, last_table, precision=highest) / float(length**3)

    tile_cells = 8 * length
    tile_rows = scores.reshape(-1, tile_cells)
    listing = tile_list.reshape(-1)
    owners = tile_owner.reshape(-1)
    listed = listing.shape[0]
    chosen = tile_rows[listing]
    owner_count = lax.axis_size(("rot", "ref"))
    order = jnp.arange(listed, dtype=jnp.int32)
    earlier = (owners[:, None] == owners[None, :]) & (order[None, :] < order[:, None])
    slot = jnp.sum(earlier.astype(jnp.int32), axis=1)
    target = owners * CAP + slot
    placing = (jnp.arange(owner_count * CAP, dtype=jnp.int32)[:, None] == target[None, :]).astype(
        jnp.float32
    )
    done = jnp.dot(chosen, refine_weight, precision=highest)
    packed = jnp.dot(placing, done, precision=highest).reshape(owner_count, CAP, tile_cells)
    refined = lax.all_to_all(packed, ("rot", "ref"), split_axis=0, concat_axis=0, tiled=True)
    return (scores, refined.reshape(1, 1, owner_count, CAP, tile_cells))


def solution(mesh):
    in_specs = (
        P(("grp", "rot", "ref"), None, "sub", None, None),
        P("grp", None, "rot", "sub", None),
        P(("grp", "rot"), "sub", "ref", None),
        P(("grp", "rot"), "sub", "ref", None, None),
        P(),
    )
    out_specs = (
        P(("grp", "rot", "ref"), "sub", None, None),
        P(("grp", "rot", "ref"), "sub", None, None, None),
    )
    return jax.shard_map(local, mesh=mesh, in_specs=in_specs, out_specs=out_specs, check_vma=False)
```

```python
import functools
import math

import jax
import jax.numpy as jnp
from jax import lax
from jax.experimental import pallas as pl
from jax.experimental.pallas import tpu as pltpu
from jax.sharding import PartitionSpec as P

CAP = 2


highest = lax.Precision.HIGH


def make_tables(length):
    counter = jnp.arange(length, dtype=jnp.int32)
    phases = counter[:, None] * counter[None, :] % length
    angles = phases.astype(jnp.float32) * (2.0 * math.pi / length)
    return (jnp.cos(angles), jnp.sin(angles))


def combine_kernel(in_ref, out_ref, *, first, second):
    batch, _, rows, lanes = in_ref.shape
    split = out_ref.shape[0]
    part = rows // split
    half = lanes // 2
    cos_part = in_ref[:, 0].reshape(batch * rows, lanes)
    sin_part = in_ref[:, 1].reshape(batch * rows, lanes)
    low = lax.broadcasted_iota(jnp.int32, (1, lanes), 1) < half
    signs = jnp.where(low, first, second).astype(jnp.float32)
    result = (cos_part + pltpu.roll(sin_part, half, 1) * signs).reshape(batch, rows, lanes)
    for piece in range(split):
        out_ref[piece] = result[:, piece * part:(piece + 1) * part].astype(out_ref.dtype)


def combine_call(stacked, first, second, split, dtype):
    batch, _, rows, lanes = stacked.shape
    block = max(b for b in range(1, 33) if batch % b == 0)
    part = rows // split
    return pl.pallas_call(
        functools.partial(combine_kernel, first=first, second=second),
        grid=(batch // block,),
        in_specs=[pl.BlockSpec((block, 2, rows, lanes), lambda i: (i, 0, 0, 0))],
        out_specs=pl.BlockSpec((split, block, part, lanes), lambda i: (0, i, 0, 0)),
        out_shape=jax.ShapeDtypeStruct((split, batch, part, lanes), dtype),
        cost_estimate=pl.CostEstimate(
            flops=3 * batch * rows * lanes,
            bytes_accessed=(8 + jnp.dtype(dtype).itemsize) * batch * rows * lanes,
            transcendentals=0,
        ),
    )(stacked)


def gather_by_shifts(piece, axis):
    count = lax.axis_size(axis)
    me = lax.axis_index(axis)
    pieces = [piece]
    for shift in range(1, count):
        pairs = [(k, (k + shift) % count) for k in range(count)]
        pieces.append(lax.ppermute(piece, axis, pairs))
    doubled = jnp.stack(pieces[::-1] * 2)
    return lax.dynamic_slice_in_dim(doubled, (count - 1 - me) % count, count, axis=0)


def exchange(sending, axis):
    count = lax.axis_size(axis)
    me = lax.axis_index(axis)
    pieces = [(me, lax.dynamic_index_in_dim(sending, me, axis=0, keepdims=False))]
    for shift in range(1, count):
        piece = lax.dynamic_index_in_dim(sending, (me + shift) % count, axis=0, keepdims=False)
        pairs = [(k, (k + shift) % count) for k in range(count)]
        pieces.append(((me - shift) % count, lax.ppermute(piece, axis, pairs)))
    return pieces


def gather_receptor(receptor):
    _, terms, kx_local, ky_local, kz = receptor.shape
    n_ref = lax.axis_size("ref")
    n_rot = lax.axis_size("rot")
    rows = ky_local // n_ref
    block = lax.dynamic_slice_in_dim(receptor, lax.axis_index("ref") * rows, rows, axis=3)
    mine = jnp.concatenate([block[0], block[1]], axis=-1).astype(jnp.bfloat16)
    mine = jnp.swapaxes(mine, 1, 2)
    along_rot = gather_by_shifts(mine, "rot")
    both = gather_by_shifts(along_rot, "ref")
    both = jnp.transpose(both, (2, 0, 3, 1, 4, 5))
    return both.reshape(terms, ky_local, n_rot * kx_local, 2 * kz)


def product_kernel(*refs):
    *spec_refs, rec_ref, out_ref = refs
    lanes = out_ref.shape[-1]
    half = lanes // 2
    total = None
    term = 0
    for spec_ref in spec_refs:
        for inner in range(spec_ref.shape[0]):
            spec = spec_ref[inner].astype(jnp.float32)
            rec = rec_ref[term].astype(jnp.float32)
            term += 1
            low = lax.broadcasted_iota(jnp.int32, (1, lanes), 1) < half
            rec_turned = pltpu.roll(rec, half, 1)
            rec_real = jnp.where(low, rec, rec_turned)
            rec_imag = jnp.where(low, rec_turned, -rec)
            part = rec_real * spec + rec_imag * pltpu.roll(spec, half, 1)
            total = part if total is None else total + part
    out_ref[...] = total


def correlate(spectra, receptor):
    rots, _, kx, ky, lanes = spectra[0].shape
    terms = receptor.shape[0]
    rows = kx * ky
    block = min(rows, 512)
    specs = [part.reshape(rots, part.shape[1], rows, lanes) for part in spectra]
    rec = receptor.reshape(terms, rows, lanes)
    out = pl.pallas_call(
        product_kernel,
        grid=(rots, rows // block),
        in_specs=[
            pl.BlockSpec((None, part.shape[1], block, lanes), lambda r, i: (r, 0, i, 0))
            for part in specs
        ]
        + [pl.BlockSpec((terms, block, lanes), lambda r, i: (0, i, 0))],
        out_specs=pl.BlockSpec((None, block, lanes), lambda r, i: (r, i, 0)),
        out_shape=jax.ShapeDtypeStruct((rots, rows, lanes), jnp.float32),
        cost_estimate=pl.CostEstimate(
            flops=8 * rots * terms * rows * lanes,
            bytes_accessed=2 * (rots + 1) * terms * rows * lanes + 4 * rots * rows * lanes,
            transcendentals=0,
        ),
    )(*specs, rec)
    return out.reshape(rots, kx, ky, lanes)


def local(ligand, receptor, tile_list, tile_owner, refine_weight):
    rots, terms, x_local, ny, nz = ligand.shape
    length = nz
    n_sub = lax.axis_size("sub")
    y_local = ny // n_sub
    cos_table, sin_table = make_tables(length)
    pair = jnp.stack([cos_table, sin_table])

    chunks = 2 if terms % 2 == 0 else 1
    part_terms = terms // chunks
    pair_x = pair.reshape(2, length, n_sub, x_local)
    z_table = jnp.concatenate([cos_table, -sin_table], axis=1)
    values = ligand.astype(jnp.float32)
    spectra = []
    for chunk in range(chunks):
        part = values[:, chunk * part_terms:(chunk + 1) * part_terms]
        along_z = jnp.einsum("rtxyz,zl->rtxyl", part, z_table, precision=highest)
        along_y = jnp.einsum("ejy,rtxyl->rtxejl", pair, along_z, precision=highest)
        sending = combine_call(
            along_y.reshape(-1, 2, ny, 2 * length), 1.0, -1.0, n_sub, jnp.bfloat16
        ).reshape(n_sub, rots, part_terms, x_local, y_local, 2 * length)
        along_x = sum(
            jnp.einsum(
                "ekx,rtxjl->rtjekl",
                lax.dynamic_index_in_dim(pair_x, source, axis=2, keepdims=False),
                piece.astype(jnp.float32),
                precision=highest,
            )
            for source, piece in exchange(sending, "sub")
        )
        spectrum = combine_call(
            along_x.reshape(-1, 2, length, 2 * length), 1.0, -1.0, 1, jnp.bfloat16
        )
        spectra.append(spectrum.reshape(rots, part_terms, y_local, length, 2 * length))

    whole_receptor = gather_receptor(receptor)
    product = correlate(spectra, whole_receptor)

    back_x = jnp.einsum("exk,rjkl->xrejl", pair, product, precision=highest)
    back_x = combine_call(back_x.reshape(-1, 2, y_local, 2 * length), -1.0, 1.0, 1, jnp.float32)
    back_x = back_x.reshape(n_sub, x_local, rots, y_local, 2 * length)
    pair_y = pair.reshape(2, length, n_sub, y_local)
    back_y = sum(
        jnp.einsum(
            "eyj,xrjl->rxeyl",
            lax.dynamic_index_in_dim(pair_y, source, axis=2, keepdims=False),
            piece,
            precision=highest,
        )
        for source, piece in exchange(back_x, "sub")
    )
    back_y = combine_call(back_y.reshape(-1, 2, ny, 2 * length), -1.0, 1.0, 1, jnp.float32)
    back_y = back_y.reshape(rots, x_local, ny, 2 * length)
    last_table = jnp.concatenate([cos_table, -sin_table], axis=0)
    scores = jnp.einsum("rxyl,lz->rxyz", back_y, last_table, precision=highest) / float(length**3)

    tile_cells = 8 * length
    tile_rows = scores.reshape(-1, tile_cells)
    listing = tile_list.reshape(-1)
    owners = tile_owner.reshape(-1)
    listed = listing.shape[0]
    chosen = tile_rows[listing]
    owner_count = lax.axis_size(("rot", "ref"))
    order = jnp.arange(listed, dtype=jnp.int32)
    earlier = (owners[:, None] == owners[None, :]) & (order[None, :] < order[:, None])
    slot = jnp.sum(earlier.astype(jnp.int32), axis=1)
    target = owners * CAP + slot
    placing = (jnp.arange(owner_count * CAP, dtype=jnp.int32)[:, None] == target[None, :]).astype(
        jnp.float32
    )
    done = jnp.dot(chosen, refine_weight, precision=highest)
    packed = jnp.dot(placing, done, precision=highest).reshape(owner_count, CAP, tile_cells)
    refined = lax.all_to_all(packed, ("rot", "ref"), split_axis=0, concat_axis=0, tiled=True)
    return (scores, refined.reshape(1, 1, owner_count, CAP, tile_cells))


def solution(mesh):
    in_specs = (
        P(("grp", "rot", "ref"), None, "sub", None, None),
        P("grp", None, "rot", "sub", None),
        P(("grp", "rot"), "sub", "ref", None),
        P(("grp", "rot"), "sub", "ref", None, None),
        P(),
    )
    out_specs = (
        P(("grp", "rot", "ref"), "sub", None, None),
        P(("grp", "rot", "ref"), "sub", None, None, None),
    )
    return jax.shard_map(local, mesh=mesh, in_specs=in_specs, out_specs=out_specs, check_vma=False)
```

```python
import functools
import math

import jax
import jax.numpy as jnp
from jax import lax
from jax.experimental import pallas as pl
from jax.experimental.pallas import tpu as pltpu
from jax.sharding import PartitionSpec as P

CAP = 2


highest = lax.Precision.HIGH


def make_tables(length):
    counter = jnp.arange(length, dtype=jnp.int32)
    phases = counter[:, None] * counter[None, :] % length
    angles = phases.astype(jnp.float32) * (2.0 * math.pi / length)
    return (jnp.cos(angles), jnp.sin(angles))


def combine_kernel(in_ref, out_ref, *, first, second):
    batch, _, rows, lanes = in_ref.shape
    split = out_ref.shape[0]
    part = rows // split
    half = lanes // 2
    cos_part = in_ref[:, 0].reshape(batch * rows, lanes)
    sin_part = in_ref[:, 1].reshape(batch * rows, lanes)
    low = lax.broadcasted_iota(jnp.int32, (1, lanes), 1) < half
    signs = jnp.where(low, first, second).astype(jnp.float32)
    result = (cos_part + pltpu.roll(sin_part, half, 1) * signs).reshape(batch, rows, lanes)
    for piece in range(split):
        out_ref[piece] = result[:, piece * part:(piece + 1) * part].astype(out_ref.dtype)


def combine_call(stacked, first, second, split, dtype):
    batch, _, rows, lanes = stacked.shape
    block = max(b for b in range(1, 33) if batch % b == 0)
    part = rows // split
    return pl.pallas_call(
        functools.partial(combine_kernel, first=first, second=second),
        grid=(batch // block,),
        in_specs=[pl.BlockSpec((block, 2, rows, lanes), lambda i: (i, 0, 0, 0))],
        out_specs=pl.BlockSpec((split, block, part, lanes), lambda i: (0, i, 0, 0)),
        out_shape=jax.ShapeDtypeStruct((split, batch, part, lanes), dtype),
        cost_estimate=pl.CostEstimate(
            flops=3 * batch * rows * lanes,
            bytes_accessed=(8 + jnp.dtype(dtype).itemsize) * batch * rows * lanes,
            transcendentals=0,
        ),
    )(stacked)


def gather_by_shifts(piece, axis):
    count = lax.axis_size(axis)
    me = lax.axis_index(axis)
    pieces = [piece]
    for shift in range(1, count):
        pairs = [(k, (k + shift) % count) for k in range(count)]
        pieces.append(lax.ppermute(piece, axis, pairs))
    doubled = jnp.stack(pieces[::-1] * 2)
    return lax.dynamic_slice_in_dim(doubled, (count - 1 - me) % count, count, axis=0)


def exchange(sending, axis):
    count = lax.axis_size(axis)
    me = lax.axis_index(axis)
    pieces = [(me, lax.dynamic_index_in_dim(sending, me, axis=0, keepdims=False))]
    for shift in range(1, count):
        piece = lax.dynamic_index_in_dim(sending, (me + shift) % count, axis=0, keepdims=False)
        pairs = [(k, (k + shift) % count) for k in range(count)]
        pieces.append(((me - shift) % count, lax.ppermute(piece, axis, pairs)))
    return pieces


def gather_receptor(receptor):
    _, terms, kx_local, ky_local, kz = receptor.shape
    n_ref = lax.axis_size("ref")
    n_rot = lax.axis_size("rot")
    rows = ky_local // n_ref
    block = lax.dynamic_slice_in_dim(receptor, lax.axis_index("ref") * rows, rows, axis=3)
    mine = jnp.concatenate([block[0], block[1]], axis=-1).astype(jnp.bfloat16)
    mine = jnp.swapaxes(mine, 1, 2)
    along_rot = gather_by_shifts(mine, "rot")
    both = gather_by_shifts(along_rot, "ref")
    both = jnp.transpose(both, (2, 0, 3, 1, 4, 5))
    return both.reshape(terms, ky_local, n_rot * kx_local, 2 * kz)


def product_kernel(*refs):
    *spec_refs, rec_ref, out_ref = refs
    lanes = out_ref.shape[-1]
    half = lanes // 2
    total = None
    term = 0
    for spec_ref in spec_refs:
        for inner in range(spec_ref.shape[0]):
            spec = spec_ref[inner].astype(jnp.float32)
            rec = rec_ref[term].astype(jnp.float32)
            term += 1
            low = lax.broadcasted_iota(jnp.int32, (1, lanes), 1) < half
            rec_turned = pltpu.roll(rec, half, 1)
            rec_real = jnp.where(low, rec, rec_turned)
            rec_imag = jnp.where(low, rec_turned, -rec)
            part = rec_real * spec + rec_imag * pltpu.roll(spec, half, 1)
            total = part if total is None else total + part
    out_ref[...] = total


def correlate(spectra, receptor):
    rots, _, kx, ky, lanes = spectra[0].shape
    terms = receptor.shape[0]
    rows = kx * ky
    block = min(rows, 512)
    specs = [part.reshape(rots, part.shape[1], rows, lanes) for part in spectra]
    rec = receptor.reshape(terms, rows, lanes)
    out = pl.pallas_call(
        product_kernel,
        grid=(rots, rows // block),
        in_specs=[
            pl.BlockSpec((None, part.shape[1], block, lanes), lambda r, i: (r, 0, i, 0))
            for part in specs
        ]
        + [pl.BlockSpec((terms, block, lanes), lambda r, i: (0, i, 0))],
        out_specs=pl.BlockSpec((None, block, lanes), lambda r, i: (r, i, 0)),
        out_shape=jax.ShapeDtypeStruct((rots, rows, lanes), jnp.float32),
        cost_estimate=pl.CostEstimate(
            flops=8 * rots * terms * rows * lanes,
            bytes_accessed=2 * (rots + 1) * terms * rows * lanes + 4 * rots * rows * lanes,
            transcendentals=0,
        ),
    )(*specs, rec)
    return out.reshape(rots, kx, ky, lanes)


def local(ligand, receptor, tile_list, tile_owner, refine_weight):
    rots, terms, x_local, ny, nz = ligand.shape
    length = nz
    n_sub = lax.axis_size("sub")
    y_local = ny // n_sub
    cos_table, sin_table = make_tables(length)
    pair = jnp.stack([cos_table, sin_table])

    chunks = 2 if terms % 2 == 0 else 1
    part_terms = terms // chunks
    pair_x = pair.reshape(2, length, n_sub, x_local)
    z_table = jnp.concatenate([cos_table, -sin_table], axis=1)
    values = ligand.astype(jnp.float32)
    spectra = []
    for chunk in range(chunks):
        part = values[:, chunk * part_terms:(chunk + 1) * part_terms]
        along_z = jnp.einsum("rtxyz,zl->rtxyl", part, z_table, precision=highest)
        along_y = jnp.einsum("ejy,rtxyl->rtxejl", pair, along_z, precision=highest)
        sending = combine_call(
            along_y.reshape(-1, 2, ny, 2 * length), 1.0, -1.0, n_sub, jnp.bfloat16
        ).reshape(n_sub, rots, part_terms, x_local, y_local, 2 * length)
        along_x = sum(
            jnp.einsum(
                "ekx,rtxjl->rtjekl",
                lax.dynamic_index_in_dim(pair_x, source, axis=2, keepdims=False),
                piece.astype(jnp.float32),
                precision=highest,
            )
            for source, piece in exchange(sending, "sub")
        )
        spectrum = combine_call(
            along_x.reshape(-1, 2, length, 2 * length), 1.0, -1.0, 1, jnp.bfloat16
        )
        spectra.append(spectrum.reshape(rots, part_terms, y_local, length, 2 * length))

    whole_receptor = gather_receptor(receptor)
    product = correlate(spectra, whole_receptor)

    back_x = jnp.einsum("exk,rjkl->xrejl", pair, product, precision=highest)
    back_x = combine_call(back_x.reshape(-1, 2, y_local, 2 * length), -1.0, 1.0, 1, jnp.float32)
    back_x = back_x.reshape(n_sub, x_local, rots, y_local, 2 * length)
    pair_y = pair.reshape(2, length, n_sub, y_local)
    back_y = sum(
        jnp.einsum(
            "eyj,xrjl->rxeyl",
            lax.dynamic_index_in_dim(pair_y, source, axis=2, keepdims=False),
            piece,
            precision=highest,
        )
        for source, piece in exchange(back_x, "sub")
    )
    back_y = combine_call(back_y.reshape(-1, 2, ny, 2 * length), -1.0, 1.0, 1, jnp.float32)
    back_y = back_y.reshape(rots, x_local, ny, 2 * length)
    last_table = jnp.concatenate([cos_table, -sin_table], axis=0)
    scores = jnp.einsum("rxyl,lz->rxyz", back_y, last_table, precision=highest) / float(length**3)

    tile_cells = 8 * length
    tile_rows = scores.reshape(-1, tile_cells)
    listing = tile_list.reshape(-1)
    owners = tile_owner.reshape(-1)
    listed = listing.shape[0]
    chosen = tile_rows[listing]
    owner_count = lax.axis_size(("rot", "ref"))
    order = jnp.arange(listed, dtype=jnp.int32)
    earlier = (owners[:, None] == owners[None, :]) & (order[None, :] < order[:, None])
    slot = jnp.sum(earlier.astype(jnp.int32), axis=1)
    target = owners * CAP + slot
    placing = (jnp.arange(owner_count * CAP, dtype=jnp.int32)[:, None] == target[None, :]).astype(
        jnp.float32
    )
    done = jnp.dot(chosen, refine_weight, precision=highest)
    packed = jnp.dot(placing, done, precision=highest).reshape(owner_count, CAP, tile_cells)
    owner_axes = ("rot", "ref")
    arrived = [piece for _, piece in exchange(packed, owner_axes)]
    me = lax.axis_index(owner_axes)
    doubled = jnp.stack(arrived[::-1] * 2)
    refined = lax.dynamic_slice_in_dim(doubled, (owner_count - 1 - me) % owner_count, owner_count)
    return (scores, refined.reshape(1, 1, owner_count, CAP, tile_cells))


def solution(mesh):
    in_specs = (
        P(("grp", "rot", "ref"), None, "sub", None, None),
        P("grp", None, "rot", "sub", None),
        P(("grp", "rot"), "sub", "ref", None),
        P(("grp", "rot"), "sub", "ref", None, None),
        P(),
    )
    out_specs = (
        P(("grp", "rot", "ref"), "sub", None, None),
        P(("grp", "rot", "ref"), "sub", None, None, None),
    )
    return jax.shard_map(local, mesh=mesh, in_specs=in_specs, out_specs=out_specs, check_vma=False)
```

```python
import functools
import math

import jax
import jax.numpy as jnp
from jax import lax
from jax.experimental import pallas as pl
from jax.experimental.pallas import tpu as pltpu
from jax.sharding import PartitionSpec as P

CAP = 2


highest = lax.Precision.HIGH


def make_tables(length):
    counter = jnp.arange(length, dtype=jnp.int32)
    phases = counter[:, None] * counter[None, :] % length
    angles = phases.astype(jnp.float32) * (2.0 * math.pi / length)
    return (jnp.cos(angles), jnp.sin(angles))


def combine_kernel(in_ref, out_ref, *, first, second):
    batch, _, rows, lanes = in_ref.shape
    split = out_ref.shape[0]
    part = rows // split
    half = lanes // 2
    cos_part = in_ref[:, 0].reshape(batch * rows, lanes)
    sin_part = in_ref[:, 1].reshape(batch * rows, lanes)
    low = lax.broadcasted_iota(jnp.int32, (1, lanes), 1) < half
    signs = jnp.where(low, first, second).astype(jnp.float32)
    result = (cos_part + pltpu.roll(sin_part, half, 1) * signs).reshape(batch, rows, lanes)
    for piece in range(split):
        out_ref[piece] = result[:, piece * part:(piece + 1) * part].astype(out_ref.dtype)


def combine_call(stacked, first, second, split, dtype):
    batch, _, rows, lanes = stacked.shape
    block = max(b for b in range(1, 33) if batch % b == 0)
    part = rows // split
    return pl.pallas_call(
        functools.partial(combine_kernel, first=first, second=second),
        grid=(batch // block,),
        in_specs=[pl.BlockSpec((block, 2, rows, lanes), lambda i: (i, 0, 0, 0))],
        out_specs=pl.BlockSpec((split, block, part, lanes), lambda i: (0, i, 0, 0)),
        out_shape=jax.ShapeDtypeStruct((split, batch, part, lanes), dtype),
        cost_estimate=pl.CostEstimate(
            flops=3 * batch * rows * lanes,
            bytes_accessed=(8 + jnp.dtype(dtype).itemsize) * batch * rows * lanes,
            transcendentals=0,
        ),
    )(stacked)


def gather_by_shifts(piece, axis):
    count = lax.axis_size(axis)
    me = lax.axis_index(axis)
    pieces = [piece]
    for shift in range(1, count):
        pairs = [(k, (k + shift) % count) for k in range(count)]
        pieces.append(lax.ppermute(piece, axis, pairs))
    doubled = jnp.stack(pieces[::-1] * 2)
    return lax.dynamic_slice_in_dim(doubled, (count - 1 - me) % count, count, axis=0)


def exchange(sending, axis):
    count = lax.axis_size(axis)
    me = lax.axis_index(axis)
    pieces = [(me, lax.dynamic_index_in_dim(sending, me, axis=0, keepdims=False))]
    for shift in range(1, count):
        piece = lax.dynamic_index_in_dim(sending, (me + shift) % count, axis=0, keepdims=False)
        pairs = [(k, (k + shift) % count) for k in range(count)]
        pieces.append(((me - shift) % count, lax.ppermute(piece, axis, pairs)))
    return pieces


def gather_receptor(receptor):
    _, terms, kx_local, ky_local, kz = receptor.shape
    n_ref = lax.axis_size("ref")
    n_rot = lax.axis_size("rot")
    rows = ky_local // n_ref
    block = lax.dynamic_slice_in_dim(receptor, lax.axis_index("ref") * rows, rows, axis=3)
    mine = jnp.concatenate([block[0], block[1]], axis=-1).astype(jnp.bfloat16)
    mine = jnp.swapaxes(mine, 1, 2)
    along_rot = gather_by_shifts(mine, "rot")
    both = gather_by_shifts(along_rot, "ref")
    both = jnp.transpose(both, (2, 0, 3, 1, 4, 5))
    return both.reshape(terms, ky_local, n_rot * kx_local, 2 * kz)


def product_kernel(*refs):
    *spec_refs, rec_ref, out_ref = refs
    lanes = out_ref.shape[-1]
    half = lanes // 2
    total = None
    term = 0
    for spec_ref in spec_refs:
        for inner in range(spec_ref.shape[0]):
            spec = spec_ref[inner].astype(jnp.float32)
            rec = rec_ref[term].astype(jnp.float32)
            term += 1
            low = lax.broadcasted_iota(jnp.int32, (1, lanes), 1) < half
            rec_turned = pltpu.roll(rec, half, 1)
            rec_real = jnp.where(low, rec, rec_turned)
            rec_imag = jnp.where(low, rec_turned, -rec)
            part = rec_real * spec + rec_imag * pltpu.roll(spec, half, 1)
            total = part if total is None else total + part
    out_ref[...] = total


def correlate(spectra, receptor):
    rots, _, kx, ky, lanes = spectra[0].shape
    terms = receptor.shape[0]
    rows = kx * ky
    block = min(rows, 512)
    specs = [part.reshape(rots, part.shape[1], rows, lanes) for part in spectra]
    rec = receptor.reshape(terms, rows, lanes)
    out = pl.pallas_call(
        product_kernel,
        grid=(rots, rows // block),
        in_specs=[
            pl.BlockSpec((None, part.shape[1], block, lanes), lambda r, i: (r, 0, i, 0))
            for part in specs
        ]
        + [pl.BlockSpec((terms, block, lanes), lambda r, i: (0, i, 0))],
        out_specs=pl.BlockSpec((None, block, lanes), lambda r, i: (r, i, 0)),
        out_shape=jax.ShapeDtypeStruct((rots, rows, lanes), jnp.float32),
        cost_estimate=pl.CostEstimate(
            flops=8 * rots * terms * rows * lanes,
            bytes_accessed=2 * (rots + 1) * terms * rows * lanes + 4 * rots * rows * lanes,
            transcendentals=0,
        ),
    )(*specs, rec)
    return out.reshape(rots, kx, ky, lanes)


def local(ligand, receptor, tile_list, tile_owner, refine_weight):
    rots, terms, x_local, ny, nz = ligand.shape
    length = nz
    n_sub = lax.axis_size("sub")
    y_local = ny // n_sub
    cos_table, sin_table = make_tables(length)
    pair = jnp.stack([cos_table, sin_table])

    chunks = 2 if terms % 2 == 0 else 1
    part_terms = terms // chunks
    pair_x = pair.reshape(2, length, n_sub, x_local)
    z_table = jnp.concatenate([cos_table, -sin_table], axis=1)
    values = ligand.astype(jnp.float32)
    spectra = []
    for chunk in range(chunks):
        part = values[:, chunk * part_terms:(chunk + 1) * part_terms]
        along_z = jnp.einsum("rtxyz,zl->rtxyl", part, z_table, precision=highest)
        along_y = jnp.einsum("ejy,rtxyl->rtxejl", pair, along_z, precision=highest)
        sending = combine_call(
            along_y.reshape(-1, 2, ny, 2 * length), 1.0, -1.0, n_sub, jnp.bfloat16
        ).reshape(n_sub, rots, part_terms, x_local, y_local, 2 * length)
        along_x = sum(
            jnp.einsum(
                "ekx,rtxjl->rtjekl",
                lax.dynamic_index_in_dim(pair_x, source, axis=2, keepdims=False),
                piece.astype(jnp.float32),
                precision=highest,
            )
            for source, piece in exchange(sending, "sub")
        )
        spectrum = combine_call(
            along_x.reshape(-1, 2, length, 2 * length), 1.0, -1.0, 1, jnp.bfloat16
        )
        spectra.append(spectrum.reshape(rots, part_terms, y_local, length, 2 * length))

    whole_receptor = gather_receptor(receptor)
    product = correlate(spectra, whole_receptor)

    halves = 2 if y_local % 16 == 0 else 1
    rows_half = y_local // halves
    pair_y = pair.reshape(2, length, n_sub, y_local)
    back_y = 0.0
    for h in range(halves):
        rows = slice(h * rows_half, (h + 1) * rows_half)
        back_x = jnp.einsum("exk,rjkl->xrejl", pair, product[:, rows], precision=highest)
        back_x = combine_call(
            back_x.reshape(-1, 2, rows_half, 2 * length), -1.0, 1.0, 1, jnp.float32
        )
        back_x = back_x.reshape(n_sub, x_local, rots, rows_half, 2 * length)
        back_y = back_y + sum(
            jnp.einsum(
                "eyj,xrjl->rxeyl",
                lax.dynamic_index_in_dim(pair_y[..., rows], source, axis=2, keepdims=False),
                piece,
                precision=highest,
            )
            for source, piece in exchange(back_x, "sub")
        )
    back_y = combine_call(back_y.reshape(-1, 2, ny, 2 * length), -1.0, 1.0, 1, jnp.float32)
    back_y = back_y.reshape(rots, x_local, ny, 2 * length)
    last_table = jnp.concatenate([cos_table, -sin_table], axis=0)
    scores = jnp.einsum("rxyl,lz->rxyz", back_y, last_table, precision=highest) / float(length**3)

    tile_cells = 8 * length
    tile_rows = scores.reshape(-1, tile_cells)
    listing = tile_list.reshape(-1)
    owners = tile_owner.reshape(-1)
    listed = listing.shape[0]
    chosen = tile_rows[listing]
    owner_count = lax.axis_size(("rot", "ref"))
    order = jnp.arange(listed, dtype=jnp.int32)
    earlier = (owners[:, None] == owners[None, :]) & (order[None, :] < order[:, None])
    slot = jnp.sum(earlier.astype(jnp.int32), axis=1)
    target = owners * CAP + slot
    placing = (jnp.arange(owner_count * CAP, dtype=jnp.int32)[:, None] == target[None, :]).astype(
        jnp.float32
    )
    done = jnp.dot(chosen, refine_weight, precision=highest)
    packed = jnp.dot(placing, done, precision=highest).reshape(owner_count, CAP, tile_cells)
    refined = lax.all_to_all(packed, ("rot", "ref"), split_axis=0, concat_axis=0, tiled=True)
    return (scores, refined.reshape(1, 1, owner_count, CAP, tile_cells))


def solution(mesh):
    in_specs = (
        P(("grp", "rot", "ref"), None, "sub", None, None),
        P("grp", None, "rot", "sub", None),
        P(("grp", "rot"), "sub", "ref", None),
        P(("grp", "rot"), "sub", "ref", None, None),
        P(),
    )
    out_specs = (
        P(("grp", "rot", "ref"), "sub", None, None),
        P(("grp", "rot", "ref"), "sub", None, None, None),
    )
    return jax.shard_map(local, mesh=mesh, in_specs=in_specs, out_specs=out_specs, check_vma=False)
```

```python
import functools
import math

import jax
import jax.numpy as jnp
from jax import lax
from jax.experimental import pallas as pl
from jax.experimental.pallas import tpu as pltpu
from jax.sharding import PartitionSpec as P

CAP = 2


highest = lax.Precision.HIGH


def make_tables(length):
    counter = jnp.arange(length, dtype=jnp.int32)
    phases = counter[:, None] * counter[None, :] % length
    angles = phases.astype(jnp.float32) * (2.0 * math.pi / length)
    return (jnp.cos(angles), jnp.sin(angles))


def combine_kernel(in_ref, out_ref, *, first, second):
    batch, _, rows, lanes = in_ref.shape
    split = out_ref.shape[0]
    part = rows // split
    half = lanes // 2
    cos_part = in_ref[:, 0].reshape(batch * rows, lanes)
    sin_part = in_ref[:, 1].reshape(batch * rows, lanes)
    low = lax.broadcasted_iota(jnp.int32, (1, lanes), 1) < half
    signs = jnp.where(low, first, second).astype(jnp.float32)
    result = (cos_part + pltpu.roll(sin_part, half, 1) * signs).reshape(batch, rows, lanes)
    for piece in range(split):
        out_ref[piece] = result[:, piece * part:(piece + 1) * part].astype(out_ref.dtype)


def combine_call(stacked, first, second, split, dtype):
    batch, _, rows, lanes = stacked.shape
    block = max(b for b in range(1, 33) if batch % b == 0)
    part = rows // split
    return pl.pallas_call(
        functools.partial(combine_kernel, first=first, second=second),
        grid=(batch // block,),
        in_specs=[pl.BlockSpec((block, 2, rows, lanes), lambda i: (i, 0, 0, 0))],
        out_specs=pl.BlockSpec((split, block, part, lanes), lambda i: (0, i, 0, 0)),
        out_shape=jax.ShapeDtypeStruct((split, batch, part, lanes), dtype),
        cost_estimate=pl.CostEstimate(
            flops=3 * batch * rows * lanes,
            bytes_accessed=(8 + jnp.dtype(dtype).itemsize) * batch * rows * lanes,
            transcendentals=0,
        ),
    )(stacked)


def gather_by_shifts(piece, axis):
    count = lax.axis_size(axis)
    me = lax.axis_index(axis)
    pieces = [piece]
    for shift in range(1, count):
        pairs = [(k, (k + shift) % count) for k in range(count)]
        pieces.append(lax.ppermute(piece, axis, pairs))
    doubled = jnp.stack(pieces[::-1] * 2)
    return lax.dynamic_slice_in_dim(doubled, (count - 1 - me) % count, count, axis=0)


def exchange(sending, axis):
    count = lax.axis_size(axis)
    me = lax.axis_index(axis)
    pieces = [(me, lax.dynamic_index_in_dim(sending, me, axis=0, keepdims=False))]
    for shift in range(1, count):
        piece = lax.dynamic_index_in_dim(sending, (me + shift) % count, axis=0, keepdims=False)
        pairs = [(k, (k + shift) % count) for k in range(count)]
        pieces.append(((me - shift) % count, lax.ppermute(piece, axis, pairs)))
    return pieces


def table_for(tables, source):
    chosen = tables[:, :, 0]
    for index in range(1, tables.shape[2]):
        chosen = jnp.where(source == index, tables[:, :, index], chosen)
    return chosen


def gather_receptor(receptor):
    _, terms, kx_local, ky_local, kz = receptor.shape
    n_ref = lax.axis_size("ref")
    n_rot = lax.axis_size("rot")
    rows = ky_local // n_ref
    block = lax.dynamic_slice_in_dim(receptor, lax.axis_index("ref") * rows, rows, axis=3)
    mine = jnp.concatenate([block[0], block[1]], axis=-1).astype(jnp.bfloat16)
    mine = jnp.swapaxes(mine, 1, 2)
    along_rot = gather_by_shifts(mine, "rot")
    both = gather_by_shifts(along_rot, "ref")
    both = jnp.transpose(both, (2, 0, 3, 1, 4, 5))
    return both.reshape(terms, ky_local, n_rot * kx_local, 2 * kz)


def product_kernel(*refs):
    *spec_refs, rec_ref, out_ref = refs
    lanes = out_ref.shape[-1]
    half = lanes // 2
    total = None
    term = 0
    for spec_ref in spec_refs:
        for inner in range(spec_ref.shape[0]):
            spec = spec_ref[inner].astype(jnp.float32)
            rec = rec_ref[term].astype(jnp.float32)
            term += 1
            low = lax.broadcasted_iota(jnp.int32, (1, lanes), 1) < half
            rec_turned = pltpu.roll(rec, half, 1)
            rec_real = jnp.where(low, rec, rec_turned)
            rec_imag = jnp.where(low, rec_turned, -rec)
            part = rec_real * spec + rec_imag * pltpu.roll(spec, half, 1)
            total = part if total is None else total + part
    out_ref[...] = total


def correlate(spectra, receptor):
    rots, _, kx, ky, lanes = spectra[0].shape
    terms = receptor.shape[0]
    rows = kx * ky
    block = min(rows, 512)
    specs = [part.reshape(rots, part.shape[1], rows, lanes) for part in spectra]
    rec = receptor.reshape(terms, rows, lanes)
    out = pl.pallas_call(
        product_kernel,
        grid=(rots, rows // block),
        in_specs=[
            pl.BlockSpec((None, part.shape[1], block, lanes), lambda r, i: (r, 0, i, 0))
            for part in specs
        ]
        + [pl.BlockSpec((terms, block, lanes), lambda r, i: (0, i, 0))],
        out_specs=pl.BlockSpec((None, block, lanes), lambda r, i: (r, i, 0)),
        out_shape=jax.ShapeDtypeStruct((rots, rows, lanes), jnp.float32),
        cost_estimate=pl.CostEstimate(
            flops=8 * rots * terms * rows * lanes,
            bytes_accessed=2 * (rots + 1) * terms * rows * lanes + 4 * rots * rows * lanes,
            transcendentals=0,
        ),
    )(*specs, rec)
    return out.reshape(rots, kx, ky, lanes)


def local(ligand, receptor, tile_list, tile_owner, refine_weight):
    rots, terms, x_local, ny, nz = ligand.shape
    length = nz
    n_sub = lax.axis_size("sub")
    y_local = ny // n_sub
    cos_table, sin_table = make_tables(length)
    pair = jnp.stack([cos_table, sin_table])

    chunks = 2 if terms % 2 == 0 else 1
    part_terms = terms // chunks
    pair_x = pair.reshape(2, length, n_sub, x_local)
    z_table = jnp.concatenate([cos_table, -sin_table], axis=1)
    values = ligand.astype(jnp.float32)
    spectra = []
    for chunk in range(chunks):
        part = values[:, chunk * part_terms:(chunk + 1) * part_terms]
        along_z = jnp.einsum("rtxyz,zl->rtxyl", part, z_table, precision=highest)
        along_y = jnp.einsum("ejy,rtxyl->rtxejl", pair, along_z, precision=highest)
        sending = combine_call(
            along_y.reshape(-1, 2, ny, 2 * length), 1.0, -1.0, n_sub, jnp.bfloat16
        ).reshape(n_sub, rots, part_terms, x_local, y_local, 2 * length)
        along_x = sum(
            jnp.einsum(
                "ekx,rtxjl->rtjekl",
                table_for(pair_x, source),
                piece.astype(jnp.float32),
                precision=highest,
            )
            for source, piece in exchange(sending, "sub")
        )
        spectrum = combine_call(
            along_x.reshape(-1, 2, length, 2 * length), 1.0, -1.0, 1, jnp.bfloat16
        )
        spectra.append(spectrum.reshape(rots, part_terms, y_local, length, 2 * length))

    whole_receptor = gather_receptor(receptor)
    product = correlate(spectra, whole_receptor)

    back_x = jnp.einsum("exk,rjkl->xrejl", pair, product, precision=highest)
    back_x = combine_call(back_x.reshape(-1, 2, y_local, 2 * length), -1.0, 1.0, 1, jnp.float32)
    back_x = back_x.reshape(n_sub, x_local, rots, y_local, 2 * length)
    pair_y = pair.reshape(2, length, n_sub, y_local)
    back_y = sum(
        jnp.einsum(
            "eyj,xrjl->rxeyl",
            table_for(pair_y, source),
            piece,
            precision=highest,
        )
        for source, piece in exchange(back_x, "sub")
    )
    back_y = combine_call(back_y.reshape(-1, 2, ny, 2 * length), -1.0, 1.0, 1, jnp.float32)
    back_y = back_y.reshape(rots, x_local, ny, 2 * length)
    last_table = jnp.concatenate([cos_table, -sin_table], axis=0)
    scores = jnp.einsum("rxyl,lz->rxyz", back_y, last_table, precision=highest) / float(length**3)

    tile_cells = 8 * length
    tile_rows = scores.reshape(-1, tile_cells)
    listing = tile_list.reshape(-1)
    owners = tile_owner.reshape(-1)
    listed = listing.shape[0]
    chosen = tile_rows[listing]
    owner_count = lax.axis_size(("rot", "ref"))
    order = jnp.arange(listed, dtype=jnp.int32)
    earlier = (owners[:, None] == owners[None, :]) & (order[None, :] < order[:, None])
    slot = jnp.sum(earlier.astype(jnp.int32), axis=1)
    target = owners * CAP + slot
    placing = (jnp.arange(owner_count * CAP, dtype=jnp.int32)[:, None] == target[None, :]).astype(
        jnp.float32
    )
    done = jnp.dot(chosen, refine_weight, precision=highest)
    packed = jnp.dot(placing, done, precision=highest).reshape(owner_count, CAP, tile_cells)
    refined = lax.all_to_all(packed, ("rot", "ref"), split_axis=0, concat_axis=0, tiled=True)
    return (scores, refined.reshape(1, 1, owner_count, CAP, tile_cells))


def solution(mesh):
    in_specs = (
        P(("grp", "rot", "ref"), None, "sub", None, None),
        P("grp", None, "rot", "sub", None),
        P(("grp", "rot"), "sub", "ref", None),
        P(("grp", "rot"), "sub", "ref", None, None),
        P(),
    )
    out_specs = (
        P(("grp", "rot", "ref"), "sub", None, None),
        P(("grp", "rot", "ref"), "sub", None, None, None),
    )
    return jax.shard_map(local, mesh=mesh, in_specs=in_specs, out_specs=out_specs, check_vma=False)
```

```python
import functools
import math

import jax
import jax.numpy as jnp
from jax import lax
from jax.experimental import pallas as pl
from jax.experimental.pallas import tpu as pltpu
from jax.sharding import PartitionSpec as P

CAP = 2


highest = lax.Precision.HIGH


def make_tables(length):
    counter = jnp.arange(length, dtype=jnp.int32)
    phases = counter[:, None] * counter[None, :] % length
    angles = phases.astype(jnp.float32) * (2.0 * math.pi / length)
    return (jnp.cos(angles), jnp.sin(angles))


def combine_kernel(me_ref, in_ref, out_ref, *, first, second):
    batch, _, rows, lanes = in_ref.shape
    split = out_ref.shape[0]
    part = rows // split
    half = lanes // 2
    low = lax.broadcasted_iota(jnp.int32, (1, lanes), 1) < half
    signs = jnp.where(low, first, second).astype(jnp.float32)
    me = me_ref[0]
    for piece in range(split):
        start = pl.multiple_of(((me + piece) % split) * part, 8)
        cos_part = in_ref[:, 0, pl.ds(start, part), :].reshape(batch * part, lanes)
        sin_part = in_ref[:, 1, pl.ds(start, part), :].reshape(batch * part, lanes)
        result = cos_part + pltpu.roll(sin_part, half, 1) * signs
        out_ref[piece] = result.reshape(batch, part, lanes).astype(out_ref.dtype)


def combine_call(stacked, first, second, split, dtype, me=0):
    batch, _, rows, lanes = stacked.shape
    block = max(b for b in range(1, 33) if batch % b == 0)
    part = rows // split
    return pl.pallas_call(
        functools.partial(combine_kernel, first=first, second=second),
        grid_spec=pltpu.PrefetchScalarGridSpec(
            num_scalar_prefetch=1,
            grid=(batch // block,),
            in_specs=[pl.BlockSpec((block, 2, rows, lanes), lambda i, me: (i, 0, 0, 0))],
            out_specs=pl.BlockSpec((split, block, part, lanes), lambda i, me: (0, i, 0, 0)),
        ),
        out_shape=jax.ShapeDtypeStruct((split, batch, part, lanes), dtype),
        cost_estimate=pl.CostEstimate(
            flops=3 * batch * rows * lanes,
            bytes_accessed=(8 + jnp.dtype(dtype).itemsize) * batch * rows * lanes,
            transcendentals=0,
        ),
    )(jnp.reshape(jnp.asarray(me, jnp.int32), (1,)), stacked)


def gather_by_shifts(piece, axis):
    count = lax.axis_size(axis)
    me = lax.axis_index(axis)
    pieces = [piece]
    for shift in range(1, count):
        pairs = [(k, (k + shift) % count) for k in range(count)]
        pieces.append(lax.ppermute(piece, axis, pairs))
    doubled = jnp.stack(pieces[::-1] * 2)
    return lax.dynamic_slice_in_dim(doubled, (count - 1 - me) % count, count, axis=0)


def exchange(sending, axis, rotated=False):
    count = lax.axis_size(axis)
    me = lax.axis_index(axis)

    def entry(shift):
        if rotated:
            return sending[shift]
        return lax.dynamic_index_in_dim(sending, (me + shift) % count, axis=0, keepdims=False)

    pieces = [(me, entry(0))]
    for shift in range(1, count):
        pairs = [(k, (k + shift) % count) for k in range(count)]
        pieces.append(((me - shift) % count, lax.ppermute(entry(shift), axis, pairs)))
    return pieces


def table_for(tables, source):
    chosen = tables[:, :, 0]
    for index in range(1, tables.shape[2]):
        chosen = jnp.where(source == index, tables[:, :, index], chosen)
    return chosen


def gather_receptor(receptor):
    _, terms, kx_local, ky_local, kz = receptor.shape
    n_ref = lax.axis_size("ref")
    n_rot = lax.axis_size("rot")
    rows = ky_local // n_ref
    block = lax.dynamic_slice_in_dim(receptor, lax.axis_index("ref") * rows, rows, axis=3)
    mine = jnp.concatenate([block[0], block[1]], axis=-1).astype(jnp.bfloat16)
    mine = jnp.swapaxes(mine, 1, 2)
    along_rot = gather_by_shifts(mine, "rot")
    both = gather_by_shifts(along_rot, "ref")
    both = jnp.transpose(both, (2, 0, 3, 1, 4, 5))
    return both.reshape(terms, ky_local, n_rot * kx_local, 2 * kz)


def product_kernel(*refs):
    *spec_refs, rec_ref, out_ref = refs
    lanes = out_ref.shape[-1]
    half = lanes // 2
    total = None
    term = 0
    for spec_ref in spec_refs:
        for inner in range(spec_ref.shape[0]):
            spec = spec_ref[inner].astype(jnp.float32)
            rec = rec_ref[term].astype(jnp.float32)
            term += 1
            low = lax.broadcasted_iota(jnp.int32, (1, lanes), 1) < half
            rec_turned = pltpu.roll(rec, half, 1)
            rec_real = jnp.where(low, rec, rec_turned)
            rec_imag = jnp.where(low, rec_turned, -rec)
            part = rec_real * spec + rec_imag * pltpu.roll(spec, half, 1)
            total = part if total is None else total + part
    out_ref[...] = total


def correlate(spectra, receptor):
    rots, _, kx, ky, lanes = spectra[0].shape
    terms = receptor.shape[0]
    rows = kx * ky
    block = min(rows, 512)
    specs = [part.reshape(rots, part.shape[1], rows, lanes) for part in spectra]
    rec = receptor.reshape(terms, rows, lanes)
    out = pl.pallas_call(
        product_kernel,
        grid=(rots, rows // block),
        in_specs=[
            pl.BlockSpec((None, part.shape[1], block, lanes), lambda r, i: (r, 0, i, 0))
            for part in specs
        ]
        + [pl.BlockSpec((terms, block, lanes), lambda r, i: (0, i, 0))],
        out_specs=pl.BlockSpec((None, block, lanes), lambda r, i: (r, i, 0)),
        out_shape=jax.ShapeDtypeStruct((rots, rows, lanes), jnp.float32),
        cost_estimate=pl.CostEstimate(
            flops=8 * rots * terms * rows * lanes,
            bytes_accessed=2 * (rots + 1) * terms * rows * lanes + 4 * rots * rows * lanes,
            transcendentals=0,
        ),
    )(*specs, rec)
    return out.reshape(rots, kx, ky, lanes)


def local(ligand, receptor, tile_list, tile_owner, refine_weight):
    rots, terms, x_local, ny, nz = ligand.shape
    length = nz
    n_sub = lax.axis_size("sub")
    y_local = ny // n_sub
    cos_table, sin_table = make_tables(length)
    pair = jnp.stack([cos_table, sin_table])

    chunks = 2 if terms % 2 == 0 else 1
    part_terms = terms // chunks
    pair_x = pair.reshape(2, length, n_sub, x_local)
    z_table = jnp.concatenate([cos_table, -sin_table], axis=1)
    values = ligand.astype(jnp.float32)
    spectra = []
    for chunk in range(chunks):
        part = values[:, chunk * part_terms:(chunk + 1) * part_terms]
        along_z = jnp.einsum("rtxyz,zl->rtxyl", part, z_table, precision=highest)
        along_y = jnp.einsum("ejy,rtxyl->rtxejl", pair, along_z, precision=highest)
        sending = combine_call(
            along_y.reshape(-1, 2, ny, 2 * length), 1.0, -1.0, n_sub, jnp.bfloat16,
            lax.axis_index("sub"),
        ).reshape(n_sub, rots, part_terms, x_local, y_local, 2 * length)
        along_x = sum(
            jnp.einsum(
                "ekx,rtxjl->rtjekl",
                table_for(pair_x, source),
                piece.astype(jnp.float32),
                precision=highest,
            )
            for source, piece in exchange(sending, "sub", rotated=True)
        )
        spectrum = combine_call(
            along_x.reshape(-1, 2, length, 2 * length), 1.0, -1.0, 1, jnp.bfloat16
        )
        spectra.append(spectrum.reshape(rots, part_terms, y_local, length, 2 * length))

    whole_receptor = gather_receptor(receptor)
    product = correlate(spectra, whole_receptor)

    back_x = jnp.einsum("exk,rjkl->xrejl", pair, product, precision=highest)
    back_x = combine_call(back_x.reshape(-1, 2, y_local, 2 * length), -1.0, 1.0, 1, jnp.float32)
    back_x = back_x.reshape(n_sub, x_local, rots, y_local, 2 * length)
    pair_y = pair.reshape(2, length, n_sub, y_local)
    back_y = sum(
        jnp.einsum(
            "eyj,xrjl->rxeyl",
            table_for(pair_y, source),
            piece,
            precision=highest,
        )
        for source, piece in exchange(back_x, "sub")
    )
    back_y = combine_call(back_y.reshape(-1, 2, ny, 2 * length), -1.0, 1.0, 1, jnp.float32)
    back_y = back_y.reshape(rots, x_local, ny, 2 * length)
    last_table = jnp.concatenate([cos_table, -sin_table], axis=0)
    scores = jnp.einsum("rxyl,lz->rxyz", back_y, last_table, precision=highest) / float(length**3)

    tile_cells = 8 * length
    tile_rows = scores.reshape(-1, tile_cells)
    listing = tile_list.reshape(-1)
    owners = tile_owner.reshape(-1)
    listed = listing.shape[0]
    chosen = tile_rows[listing]
    owner_count = lax.axis_size(("rot", "ref"))
    order = jnp.arange(listed, dtype=jnp.int32)
    earlier = (owners[:, None] == owners[None, :]) & (order[None, :] < order[:, None])
    slot = jnp.sum(earlier.astype(jnp.int32), axis=1)
    target = owners * CAP + slot
    placing = (jnp.arange(owner_count * CAP, dtype=jnp.int32)[:, None] == target[None, :]).astype(
        jnp.float32
    )
    done = jnp.dot(chosen, refine_weight, precision=highest)
    packed = jnp.dot(placing, done, precision=highest).reshape(owner_count, CAP, tile_cells)
    refined = lax.all_to_all(packed, ("rot", "ref"), split_axis=0, concat_axis=0, tiled=True)
    return (scores, refined.reshape(1, 1, owner_count, CAP, tile_cells))


def solution(mesh):
    in_specs = (
        P(("grp", "rot", "ref"), None, "sub", None, None),
        P("grp", None, "rot", "sub", None),
        P(("grp", "rot"), "sub", "ref", None),
        P(("grp", "rot"), "sub", "ref", None, None),
        P(),
    )
    out_specs = (
        P(("grp", "rot", "ref"), "sub", None, None),
        P(("grp", "rot", "ref"), "sub", None, None, None),
    )
    return jax.shard_map(local, mesh=mesh, in_specs=in_specs, out_specs=out_specs, check_vma=False)
```

```python
import functools
import math

import jax
import jax.numpy as jnp
from jax import lax
from jax.experimental import pallas as pl
from jax.experimental.pallas import tpu as pltpu
from jax.sharding import PartitionSpec as P

CAP = 2


highest = lax.Precision.HIGH


def make_tables(length):
    counter = jnp.arange(length, dtype=jnp.int32)
    phases = counter[:, None] * counter[None, :] % length
    angles = phases.astype(jnp.float32) * (2.0 * math.pi / length)
    return (jnp.cos(angles), jnp.sin(angles))


def combine_kernel(me_ref, in_ref, out_ref, *, first, second):
    batch, _, rows, lanes = in_ref.shape
    split = out_ref.shape[0]
    part = rows // split
    half = lanes // 2
    low = lax.broadcasted_iota(jnp.int32, (1, lanes), 1) < half
    signs = jnp.where(low, first, second).astype(jnp.float32)
    me = me_ref[0]
    for piece in range(split):
        start = pl.multiple_of(((me + piece) % split) * part, 8)
        cos_part = in_ref[:, 0, pl.ds(start, part), :].reshape(batch * part, lanes)
        sin_part = in_ref[:, 1, pl.ds(start, part), :].reshape(batch * part, lanes)
        result = cos_part + pltpu.roll(sin_part, half, 1) * signs
        out_ref[piece] = result.reshape(batch, part, lanes).astype(out_ref.dtype)


def combine_call(stacked, first, second, split, dtype, me=0):
    batch, _, rows, lanes = stacked.shape
    block = max(b for b in range(1, 33) if batch % b == 0)
    part = rows // split
    return pl.pallas_call(
        functools.partial(combine_kernel, first=first, second=second),
        grid_spec=pltpu.PrefetchScalarGridSpec(
            num_scalar_prefetch=1,
            grid=(batch // block,),
            in_specs=[pl.BlockSpec((block, 2, rows, lanes), lambda i, me: (i, 0, 0, 0))],
            out_specs=pl.BlockSpec((split, block, part, lanes), lambda i, me: (0, i, 0, 0)),
        ),
        out_shape=jax.ShapeDtypeStruct((split, batch, part, lanes), dtype),
        cost_estimate=pl.CostEstimate(
            flops=3 * batch * rows * lanes,
            bytes_accessed=(8 + jnp.dtype(dtype).itemsize) * batch * rows * lanes,
            transcendentals=0,
        ),
    )(jnp.reshape(jnp.asarray(me, jnp.int32), (1,)), stacked)


def gather_by_shifts(piece, axis):
    count = lax.axis_size(axis)
    me = lax.axis_index(axis)
    pieces = [piece]
    for shift in range(1, count):
        pairs = [(k, (k + shift) % count) for k in range(count)]
        pieces.append(lax.ppermute(piece, axis, pairs))
    doubled = jnp.stack(pieces[::-1] * 2)
    return lax.dynamic_slice_in_dim(doubled, (count - 1 - me) % count, count, axis=0)


def exchange(sending, axis, rotated=False):
    count = lax.axis_size(axis)
    me = lax.axis_index(axis)

    def entry(shift):
        if rotated:
            return sending[shift]
        return lax.dynamic_index_in_dim(sending, (me + shift) % count, axis=0, keepdims=False)

    pieces = [(me, entry(0))]
    for shift in range(1, count):
        pairs = [(k, (k + shift) % count) for k in range(count)]
        pieces.append(((me - shift) % count, lax.ppermute(entry(shift), axis, pairs)))
    return pieces


def by_source(pieces):
    ordered = []
    for source in range(len(pieces)):
        chosen = pieces[0][1]
        for index, piece in pieces[1:]:
            chosen = jnp.where(index == source, piece, chosen)
        ordered.append(chosen)
    return ordered


def gather_receptor(receptor):
    _, terms, kx_local, ky_local, kz = receptor.shape
    n_ref = lax.axis_size("ref")
    n_rot = lax.axis_size("rot")
    rows = ky_local // n_ref
    block = lax.dynamic_slice_in_dim(receptor, lax.axis_index("ref") * rows, rows, axis=3)
    mine = jnp.concatenate([block[0], block[1]], axis=-1).astype(jnp.bfloat16)
    mine = jnp.swapaxes(mine, 1, 2)
    along_rot = gather_by_shifts(mine, "rot")
    both = gather_by_shifts(along_rot, "ref")
    both = jnp.transpose(both, (2, 0, 3, 1, 4, 5))
    return both.reshape(terms, ky_local, n_rot * kx_local, 2 * kz)


def product_kernel(*refs):
    *spec_refs, rec_ref, out_ref = refs
    lanes = out_ref.shape[-1]
    half = lanes // 2
    total = None
    term = 0
    for spec_ref in spec_refs:
        for inner in range(spec_ref.shape[0]):
            spec = spec_ref[inner].astype(jnp.float32)
            rec = rec_ref[term].astype(jnp.float32)
            term += 1
            low = lax.broadcasted_iota(jnp.int32, (1, lanes), 1) < half
            rec_turned = pltpu.roll(rec, half, 1)
            rec_real = jnp.where(low, rec, rec_turned)
            rec_imag = jnp.where(low, rec_turned, -rec)
            part = rec_real * spec + rec_imag * pltpu.roll(spec, half, 1)
            total = part if total is None else total + part
    out_ref[...] = total


def correlate(spectra, receptor):
    rots, _, kx, ky, lanes = spectra[0].shape
    terms = receptor.shape[0]
    rows = kx * ky
    block = min(rows, 512)
    specs = [part.reshape(rots, part.shape[1], rows, lanes) for part in spectra]
    rec = receptor.reshape(terms, rows, lanes)
    out = pl.pallas_call(
        product_kernel,
        grid=(rots, rows // block),
        in_specs=[
            pl.BlockSpec((None, part.shape[1], block, lanes), lambda r, i: (r, 0, i, 0))
            for part in specs
        ]
        + [pl.BlockSpec((terms, block, lanes), lambda r, i: (0, i, 0))],
        out_specs=pl.BlockSpec((None, block, lanes), lambda r, i: (r, i, 0)),
        out_shape=jax.ShapeDtypeStruct((rots, rows, lanes), jnp.float32),
        cost_estimate=pl.CostEstimate(
            flops=8 * rots * terms * rows * lanes,
            bytes_accessed=2 * (rots + 1) * terms * rows * lanes + 4 * rots * rows * lanes,
            transcendentals=0,
        ),
    )(*specs, rec)
    return out.reshape(rots, kx, ky, lanes)


def local(ligand, receptor, tile_list, tile_owner, refine_weight):
    rots, terms, x_local, ny, nz = ligand.shape
    length = nz
    n_sub = lax.axis_size("sub")
    y_local = ny // n_sub
    cos_table, sin_table = make_tables(length)
    pair = jnp.stack([cos_table, sin_table])

    chunks = 2 if terms % 2 == 0 else 1
    part_terms = terms // chunks
    pair_x = pair.reshape(2, length, n_sub, x_local)
    z_table = jnp.concatenate([cos_table, -sin_table], axis=1)
    values = ligand.astype(jnp.float32)
    spectra = []
    for chunk in range(chunks):
        part = values[:, chunk * part_terms:(chunk + 1) * part_terms]
        along_z = jnp.einsum("rtxyz,zl->rtxyl", part, z_table, precision=highest)
        along_y = jnp.einsum("ejy,rtxyl->rtxejl", pair, along_z, precision=highest)
        sending = combine_call(
            along_y.reshape(-1, 2, ny, 2 * length), 1.0, -1.0, n_sub, jnp.bfloat16,
            lax.axis_index("sub"),
        ).reshape(n_sub, rots, part_terms, x_local, y_local, 2 * length)
        along_x = sum(
            jnp.einsum(
                "ekx,rtxjl->rtjekl", pair_x[:, :, source], piece.astype(jnp.float32),
                precision=highest,
            )
            for source, piece in enumerate(by_source(exchange(sending, "sub", rotated=True)))
        )
        spectrum = combine_call(
            along_x.reshape(-1, 2, length, 2 * length), 1.0, -1.0, 1, jnp.bfloat16
        )
        spectra.append(spectrum.reshape(rots, part_terms, y_local, length, 2 * length))

    whole_receptor = gather_receptor(receptor)
    product = correlate(spectra, whole_receptor)

    back_x = jnp.einsum("exk,rjkl->xrejl", pair, product, precision=highest)
    back_x = combine_call(back_x.reshape(-1, 2, y_local, 2 * length), -1.0, 1.0, 1, jnp.float32)
    back_x = back_x.reshape(n_sub, x_local, rots, y_local, 2 * length)
    pair_y = pair.reshape(2, length, n_sub, y_local)
    back_y = sum(
        jnp.einsum("eyj,xrjl->rxeyl", pair_y[:, :, source], piece, precision=highest)
        for source, piece in enumerate(by_source(exchange(back_x, "sub")))
    )
    back_y = combine_call(back_y.reshape(-1, 2, ny, 2 * length), -1.0, 1.0, 1, jnp.float32)
    back_y = back_y.reshape(rots, x_local, ny, 2 * length)
    last_table = jnp.concatenate([cos_table, -sin_table], axis=0)
    scores = jnp.einsum("rxyl,lz->rxyz", back_y, last_table, precision=highest) / float(length**3)

    tile_cells = 8 * length
    tile_rows = scores.reshape(-1, tile_cells)
    listing = tile_list.reshape(-1)
    owners = tile_owner.reshape(-1)
    listed = listing.shape[0]
    chosen = tile_rows[listing]
    owner_count = lax.axis_size(("rot", "ref"))
    order = jnp.arange(listed, dtype=jnp.int32)
    earlier = (owners[:, None] == owners[None, :]) & (order[None, :] < order[:, None])
    slot = jnp.sum(earlier.astype(jnp.int32), axis=1)
    target = owners * CAP + slot
    placing = (jnp.arange(owner_count * CAP, dtype=jnp.int32)[:, None] == target[None, :]).astype(
        jnp.float32
    )
    done = jnp.dot(chosen, refine_weight, precision=highest)
    packed = jnp.dot(placing, done, precision=highest).reshape(owner_count, CAP, tile_cells)
    refined = lax.all_to_all(packed, ("rot", "ref"), split_axis=0, concat_axis=0, tiled=True)
    return (scores, refined.reshape(1, 1, owner_count, CAP, tile_cells))


def solution(mesh):
    in_specs = (
        P(("grp", "rot", "ref"), None, "sub", None, None),
        P("grp", None, "rot", "sub", None),
        P(("grp", "rot"), "sub", "ref", None),
        P(("grp", "rot"), "sub", "ref", None, None),
        P(),
    )
    out_specs = (
        P(("grp", "rot", "ref"), "sub", None, None),
        P(("grp", "rot", "ref"), "sub", None, None, None),
    )
    return jax.shard_map(local, mesh=mesh, in_specs=in_specs, out_specs=out_specs, check_vma=False)
```

```python
import functools
import math

import jax
import jax.numpy as jnp
from jax import lax
from jax.experimental import pallas as pl
from jax.experimental.pallas import tpu as pltpu
from jax.sharding import PartitionSpec as P

CAP = 2


highest = lax.Precision.HIGH


def make_tables(length):
    counter = jnp.arange(length, dtype=jnp.int32)
    phases = counter[:, None] * counter[None, :] % length
    angles = phases.astype(jnp.float32) * (2.0 * math.pi / length)
    return (jnp.cos(angles), jnp.sin(angles))


def combine_kernel(me_ref, in_ref, out_ref, *, first, second):
    batch, _, rows, lanes = in_ref.shape
    split = out_ref.shape[0]
    part = rows // split
    half = lanes // 2
    low = lax.broadcasted_iota(jnp.int32, (1, lanes), 1) < half
    signs = jnp.where(low, first, second).astype(jnp.float32)
    me = me_ref[0]
    for piece in range(split):
        start = pl.multiple_of(((me + piece) % split) * part, 8)
        cos_part = in_ref[:, 0, pl.ds(start, part), :].reshape(batch * part, lanes)
        sin_part = in_ref[:, 1, pl.ds(start, part), :].reshape(batch * part, lanes)
        result = cos_part + pltpu.roll(sin_part, half, 1) * signs
        out_ref[piece] = result.reshape(batch, part, lanes).astype(out_ref.dtype)


def combine_call(stacked, first, second, split, dtype, me=0):
    batch, _, rows, lanes = stacked.shape
    block = max(b for b in range(1, 33) if batch % b == 0)
    part = rows // split
    return pl.pallas_call(
        functools.partial(combine_kernel, first=first, second=second),
        grid_spec=pltpu.PrefetchScalarGridSpec(
            num_scalar_prefetch=1,
            grid=(batch // block,),
            in_specs=[pl.BlockSpec((block, 2, rows, lanes), lambda i, me: (i, 0, 0, 0))],
            out_specs=pl.BlockSpec((split, block, part, lanes), lambda i, me: (0, i, 0, 0)),
        ),
        out_shape=jax.ShapeDtypeStruct((split, batch, part, lanes), dtype),
        cost_estimate=pl.CostEstimate(
            flops=3 * batch * rows * lanes,
            bytes_accessed=(8 + jnp.dtype(dtype).itemsize) * batch * rows * lanes,
            transcendentals=0,
        ),
    )(jnp.reshape(jnp.asarray(me, jnp.int32), (1,)), stacked)


def gather_by_shifts(piece, axis):
    count = lax.axis_size(axis)
    me = lax.axis_index(axis)
    pieces = [piece]
    for shift in range(1, count):
        pairs = [(k, (k + shift) % count) for k in range(count)]
        pieces.append(lax.ppermute(piece, axis, pairs))
    doubled = jnp.stack(pieces[::-1] * 2)
    return lax.dynamic_slice_in_dim(doubled, (count - 1 - me) % count, count, axis=0)


def exchange(sending, axis, rotated=False):
    count = lax.axis_size(axis)
    me = lax.axis_index(axis)

    def entry(shift):
        if rotated:
            return sending[shift]
        return lax.dynamic_index_in_dim(sending, (me + shift) % count, axis=0, keepdims=False)

    pieces = [(me, entry(0))]
    for shift in range(1, count):
        pairs = [(k, (k + shift) % count) for k in range(count)]
        pieces.append(((me - shift) % count, lax.ppermute(entry(shift), axis, pairs)))
    return pieces


def by_source(pieces):
    ordered = []
    for source in range(len(pieces)):
        chosen = pieces[0][1]
        for index, piece in pieces[1:]:
            chosen = jnp.where(index == source, piece, chosen)
        ordered.append(chosen)
    return ordered


def gather_receptor(receptor):
    _, terms, kx_local, ky_local, kz = receptor.shape
    n_ref = lax.axis_size("ref")
    n_rot = lax.axis_size("rot")
    rows = ky_local // n_ref
    block = lax.dynamic_slice_in_dim(receptor, lax.axis_index("ref") * rows, rows, axis=3)
    mine = jnp.concatenate([block[0], block[1]], axis=-1).astype(jnp.bfloat16)
    mine = jnp.swapaxes(mine, 1, 2)
    along_rot = gather_by_shifts(mine, "rot")
    both = gather_by_shifts(along_rot, "ref")
    both = jnp.transpose(both, (2, 0, 3, 1, 4, 5))
    return both.reshape(terms, ky_local, n_rot * kx_local, 2 * kz)


def product_kernel(*refs):
    *spec_refs, rec_ref, out_ref = refs
    lanes = out_ref.shape[-1]
    half = lanes // 2
    total = None
    term = 0
    for spec_ref in spec_refs:
        for inner in range(spec_ref.shape[0]):
            spec = spec_ref[inner].astype(jnp.float32)
            rec = rec_ref[term].astype(jnp.float32)
            term += 1
            low = lax.broadcasted_iota(jnp.int32, (1, lanes), 1) < half
            rec_turned = pltpu.roll(rec, half, 1)
            rec_real = jnp.where(low, rec, rec_turned)
            rec_imag = jnp.where(low, rec_turned, -rec)
            part = rec_real * spec + rec_imag * pltpu.roll(spec, half, 1)
            total = part if total is None else total + part
    out_ref[...] = total


def correlate(spectra, receptor):
    rots, _, kx, ky, lanes = spectra[0].shape
    terms = receptor.shape[0]
    rows = kx * ky
    block = min(rows, 512)
    specs = [part.reshape(rots, part.shape[1], rows, lanes) for part in spectra]
    rec = receptor.reshape(terms, rows, lanes)
    out = pl.pallas_call(
        product_kernel,
        grid=(rots, rows // block),
        in_specs=[
            pl.BlockSpec((None, part.shape[1], block, lanes), lambda r, i: (r, 0, i, 0))
            for part in specs
        ]
        + [pl.BlockSpec((terms, block, lanes), lambda r, i: (0, i, 0))],
        out_specs=pl.BlockSpec((None, block, lanes), lambda r, i: (r, i, 0)),
        out_shape=jax.ShapeDtypeStruct((rots, rows, lanes), jnp.float32),
        cost_estimate=pl.CostEstimate(
            flops=8 * rots * terms * rows * lanes,
            bytes_accessed=2 * (rots + 1) * terms * rows * lanes + 4 * rots * rows * lanes,
            transcendentals=0,
        ),
    )(*specs, rec)
    return out.reshape(rots, kx, ky, lanes)


def local(ligand, receptor, tile_list, tile_owner, refine_weight):
    rots, terms, x_local, ny, nz = ligand.shape
    length = nz
    n_sub = lax.axis_size("sub")
    y_local = ny // n_sub
    cos_table, sin_table = make_tables(length)
    pair = jnp.stack([cos_table, sin_table])

    chunks = 2 if terms % 2 == 0 else 1
    part_terms = terms // chunks
    pair_x = pair.reshape(2, length, n_sub, x_local)
    z_table = jnp.concatenate([cos_table, -sin_table], axis=1)
    values = ligand.astype(jnp.float32)
    spectra = []
    for chunk in range(chunks):
        part = values[:, chunk * part_terms:(chunk + 1) * part_terms]
        along_z = jnp.einsum("rtxyz,zl->rtxyl", part, z_table, precision=highest)
        along_y = jnp.einsum("ejy,rtxyl->rtxejl", pair, along_z, precision=highest)
        sending = combine_call(
            along_y.reshape(-1, 2, ny, 2 * length), 1.0, -1.0, n_sub, jnp.bfloat16,
            lax.axis_index("sub"),
        ).reshape(n_sub, rots, part_terms, x_local, y_local, 2 * length)
        along_x = sum(
            jnp.einsum(
                "ekx,rtxjl->rtjekl", pair_x[:, :, source], piece.astype(jnp.float32),
                precision=highest,
            )
            for source, piece in enumerate(by_source(exchange(sending, "sub", rotated=True)))
        )
        spectrum = combine_call(
            along_x.reshape(-1, 2, length, 2 * length), 1.0, -1.0, 1, jnp.bfloat16
        )
        spectra.append(spectrum.reshape(rots, part_terms, y_local, length, 2 * length))

    whole_receptor = gather_receptor(receptor)
    product = correlate(spectra, whole_receptor)

    back_x = jnp.einsum("exk,rjkl->rjexl", pair, product, precision=highest)
    back_x = combine_call(
        back_x.reshape(-1, 2, length, 2 * length), -1.0, 1.0, n_sub, jnp.float32,
        lax.axis_index("sub"),
    ).reshape(n_sub, rots, y_local, x_local, 2 * length)
    pair_y = pair.reshape(2, length, n_sub, y_local)
    back_y = sum(
        jnp.einsum("eyj,rjxl->reyxl", pair_y[:, :, source], piece, precision=highest)
        for source, piece in enumerate(by_source(exchange(back_x, "sub", rotated=True)))
    )
    back_y = combine_call(
        back_y.reshape(rots, 2, ny * x_local, 2 * length), -1.0, 1.0, 1, jnp.float32
    ).reshape(rots, ny, x_local, 2 * length)
    last_table = jnp.concatenate([cos_table, -sin_table], axis=0)
    scores = jnp.einsum("ryxl,lz->rxyz", back_y, last_table, precision=highest) / float(length**3)

    tile_cells = 8 * length
    tile_rows = scores.reshape(-1, tile_cells)
    listing = tile_list.reshape(-1)
    owners = tile_owner.reshape(-1)
    listed = listing.shape[0]
    chosen = tile_rows[listing]
    owner_count = lax.axis_size(("rot", "ref"))
    order = jnp.arange(listed, dtype=jnp.int32)
    earlier = (owners[:, None] == owners[None, :]) & (order[None, :] < order[:, None])
    slot = jnp.sum(earlier.astype(jnp.int32), axis=1)
    target = owners * CAP + slot
    placing = (jnp.arange(owner_count * CAP, dtype=jnp.int32)[:, None] == target[None, :]).astype(
        jnp.float32
    )
    done = jnp.dot(chosen, refine_weight, precision=highest)
    packed = jnp.dot(placing, done, precision=highest).reshape(owner_count, CAP, tile_cells)
    refined = lax.all_to_all(packed, ("rot", "ref"), split_axis=0, concat_axis=0, tiled=True)
    return (scores, refined.reshape(1, 1, owner_count, CAP, tile_cells))


def solution(mesh):
    in_specs = (
        P(("grp", "rot", "ref"), None, "sub", None, None),
        P("grp", None, "rot", "sub", None),
        P(("grp", "rot"), "sub", "ref", None),
        P(("grp", "rot"), "sub", "ref", None, None),
        P(),
    )
    out_specs = (
        P(("grp", "rot", "ref"), "sub", None, None),
        P(("grp", "rot", "ref"), "sub", None, None, None),
    )
    return jax.shard_map(local, mesh=mesh, in_specs=in_specs, out_specs=out_specs, check_vma=False)
```

```python
import functools
import math

import jax
import jax.numpy as jnp
from jax import lax
from jax.experimental import pallas as pl
from jax.experimental.pallas import tpu as pltpu
from jax.sharding import PartitionSpec as P

CAP = 2


highest = lax.Precision.HIGH


def make_tables(length):
    counter = jnp.arange(length, dtype=jnp.int32)
    phases = counter[:, None] * counter[None, :] % length
    angles = phases.astype(jnp.float32) * (2.0 * math.pi / length)
    return (jnp.cos(angles), jnp.sin(angles))


def combine_kernel(me_ref, in_ref, out_ref, *, first, second):
    batch, _, rows, lanes = in_ref.shape
    split = out_ref.shape[0]
    part = rows // split
    half = lanes // 2
    low = lax.broadcasted_iota(jnp.int32, (1, lanes), 1) < half
    signs = jnp.where(low, first, second).astype(jnp.float32)
    me = me_ref[0]
    for piece in range(split):
        start = pl.multiple_of(((me + piece) % split) * part, 8)
        cos_part = in_ref[:, 0, pl.ds(start, part), :].reshape(batch * part, lanes)
        sin_part = in_ref[:, 1, pl.ds(start, part), :].reshape(batch * part, lanes)
        result = cos_part + pltpu.roll(sin_part, half, 1) * signs
        out_ref[piece] = result.reshape(batch, part, lanes).astype(out_ref.dtype)


def combine_call(stacked, first, second, split, dtype, me=0):
    batch, _, rows, lanes = stacked.shape
    block = max(b for b in range(1, 33) if batch % b == 0)
    part = rows // split
    return pl.pallas_call(
        functools.partial(combine_kernel, first=first, second=second),
        grid_spec=pltpu.PrefetchScalarGridSpec(
            num_scalar_prefetch=1,
            grid=(batch // block,),
            in_specs=[pl.BlockSpec((block, 2, rows, lanes), lambda i, me: (i, 0, 0, 0))],
            out_specs=pl.BlockSpec((split, block, part, lanes), lambda i, me: (0, i, 0, 0)),
        ),
        out_shape=jax.ShapeDtypeStruct((split, batch, part, lanes), dtype),
        cost_estimate=pl.CostEstimate(
            flops=3 * batch * rows * lanes,
            bytes_accessed=(8 + jnp.dtype(dtype).itemsize) * batch * rows * lanes,
            transcendentals=0,
        ),
    )(jnp.reshape(jnp.asarray(me, jnp.int32), (1,)), stacked)


def exchange(sending, axis, rotated=False):
    count = lax.axis_size(axis)
    me = lax.axis_index(axis)

    def entry(shift):
        if rotated:
            return sending[shift]
        return lax.dynamic_index_in_dim(sending, (me + shift) % count, axis=0, keepdims=False)

    pieces = [(me, entry(0))]
    for shift in range(1, count):
        pairs = [(k, (k + shift) % count) for k in range(count)]
        pieces.append(((me - shift) % count, lax.ppermute(entry(shift), axis, pairs)))
    return pieces


def by_source(pieces):
    ordered = []
    for source in range(len(pieces)):
        chosen = pieces[0][1]
        for index, piece in pieces[1:]:
            chosen = jnp.where(index == source, piece, chosen)
        ordered.append(chosen)
    return ordered


def gather_receptor(receptor):
    _, terms, kx_local, ky_local, kz = receptor.shape
    n_ref = lax.axis_size("ref")
    n_rot = lax.axis_size("rot")
    rows = ky_local // n_ref
    block = lax.dynamic_slice_in_dim(receptor, lax.axis_index("ref") * rows, rows, axis=3)
    mine = jnp.concatenate([block[0], block[1]], axis=-1).astype(jnp.bfloat16)
    mine = jnp.swapaxes(mine, 1, 2)
    along_rot = jnp.stack(by_source(exchange(jnp.stack([mine] * n_rot), "rot", rotated=True)))
    both = jnp.stack(by_source(exchange(jnp.stack([along_rot] * n_ref), "ref", rotated=True)))
    both = jnp.transpose(both, (2, 0, 3, 1, 4, 5))
    return both.reshape(terms, ky_local, n_rot * kx_local, 2 * kz)


def product_kernel(*refs):
    *spec_refs, rec_ref, out_ref = refs
    lanes = out_ref.shape[-1]
    half = lanes // 2
    total = None
    term = 0
    for spec_ref in spec_refs:
        for inner in range(spec_ref.shape[0]):
            spec = spec_ref[inner].astype(jnp.float32)
            rec = rec_ref[term].astype(jnp.float32)
            term += 1
            low = lax.broadcasted_iota(jnp.int32, (1, lanes), 1) < half
            rec_turned = pltpu.roll(rec, half, 1)
            rec_real = jnp.where(low, rec, rec_turned)
            rec_imag = jnp.where(low, rec_turned, -rec)
            part = rec_real * spec + rec_imag * pltpu.roll(spec, half, 1)
            total = part if total is None else total + part
    out_ref[...] = total


def correlate(spectra, receptor):
    rots, _, kx, ky, lanes = spectra[0].shape
    terms = receptor.shape[0]
    rows = kx * ky
    block = min(rows, 512)
    specs = [part.reshape(rots, part.shape[1], rows, lanes) for part in spectra]
    rec = receptor.reshape(terms, rows, lanes)
    out = pl.pallas_call(
        product_kernel,
        grid=(rots, rows // block),
        in_specs=[
            pl.BlockSpec((None, part.shape[1], block, lanes), lambda r, i: (r, 0, i, 0))
            for part in specs
        ]
        + [pl.BlockSpec((terms, block, lanes), lambda r, i: (0, i, 0))],
        out_specs=pl.BlockSpec((None, block, lanes), lambda r, i: (r, i, 0)),
        out_shape=jax.ShapeDtypeStruct((rots, rows, lanes), jnp.float32),
        cost_estimate=pl.CostEstimate(
            flops=8 * rots * terms * rows * lanes,
            bytes_accessed=2 * (rots + 1) * terms * rows * lanes + 4 * rots * rows * lanes,
            transcendentals=0,
        ),
    )(*specs, rec)
    return out.reshape(rots, kx, ky, lanes)


def local(ligand, receptor, tile_list, tile_owner, refine_weight):
    rots, terms, x_local, ny, nz = ligand.shape
    length = nz
    n_sub = lax.axis_size("sub")
    y_local = ny // n_sub
    cos_table, sin_table = make_tables(length)
    pair = jnp.stack([cos_table, sin_table])

    chunks = 2 if terms % 2 == 0 else 1
    part_terms = terms // chunks
    pair_x = pair.reshape(2, length, n_sub, x_local)
    z_table = jnp.concatenate([cos_table, -sin_table], axis=1)
    values = ligand.astype(jnp.float32)
    spectra = []
    for chunk in range(chunks):
        part = values[:, chunk * part_terms:(chunk + 1) * part_terms]
        along_z = jnp.einsum("rtxyz,zl->rtxyl", part, z_table, precision=highest)
        along_y = jnp.einsum("ejy,rtxyl->rtxejl", pair, along_z, precision=highest)
        sending = combine_call(
            along_y.reshape(-1, 2, ny, 2 * length), 1.0, -1.0, n_sub, jnp.bfloat16,
            lax.axis_index("sub"),
        ).reshape(n_sub, rots, part_terms, x_local, y_local, 2 * length)
        along_x = sum(
            jnp.einsum(
                "ekx,rtxjl->rtjekl", pair_x[:, :, source], piece.astype(jnp.float32),
                precision=highest,
            )
            for source, piece in enumerate(by_source(exchange(sending, "sub", rotated=True)))
        )
        spectrum = combine_call(
            along_x.reshape(-1, 2, length, 2 * length), 1.0, -1.0, 1, jnp.bfloat16
        )
        spectra.append(spectrum.reshape(rots, part_terms, y_local, length, 2 * length))

    whole_receptor = gather_receptor(receptor)
    product = correlate(spectra, whole_receptor)

    back_x = jnp.einsum("exk,rjkl->xrejl", pair, product, precision=highest)
    back_x = combine_call(back_x.reshape(-1, 2, y_local, 2 * length), -1.0, 1.0, 1, jnp.float32)
    back_x = back_x.reshape(n_sub, x_local, rots, y_local, 2 * length)
    pair_y = pair.reshape(2, length, n_sub, y_local)
    back_y = sum(
        jnp.einsum("eyj,xrjl->rxeyl", pair_y[:, :, source], piece, precision=highest)
        for source, piece in enumerate(by_source(exchange(back_x, "sub")))
    )
    back_y = combine_call(back_y.reshape(-1, 2, ny, 2 * length), -1.0, 1.0, 1, jnp.float32)
    back_y = back_y.reshape(rots, x_local, ny, 2 * length)
    last_table = jnp.concatenate([cos_table, -sin_table], axis=0)
    scores = jnp.einsum("rxyl,lz->rxyz", back_y, last_table, precision=highest) / float(length**3)

    tile_cells = 8 * length
    tile_rows = scores.reshape(-1, tile_cells)
    listing = tile_list.reshape(-1)
    owners = tile_owner.reshape(-1)
    listed = listing.shape[0]
    chosen = tile_rows[listing]
    owner_count = lax.axis_size(("rot", "ref"))
    order = jnp.arange(listed, dtype=jnp.int32)
    earlier = (owners[:, None] == owners[None, :]) & (order[None, :] < order[:, None])
    slot = jnp.sum(earlier.astype(jnp.int32), axis=1)
    target = owners * CAP + slot
    placing = (jnp.arange(owner_count * CAP, dtype=jnp.int32)[:, None] == target[None, :]).astype(
        jnp.float32
    )
    done = jnp.dot(chosen, refine_weight, precision=highest)
    packed = jnp.dot(placing, done, precision=highest).reshape(owner_count, CAP, tile_cells)
    refined = lax.all_to_all(packed, ("rot", "ref"), split_axis=0, concat_axis=0, tiled=True)
    return (scores, refined.reshape(1, 1, owner_count, CAP, tile_cells))


def solution(mesh):
    in_specs = (
        P(("grp", "rot", "ref"), None, "sub", None, None),
        P("grp", None, "rot", "sub", None),
        P(("grp", "rot"), "sub", "ref", None),
        P(("grp", "rot"), "sub", "ref", None, None),
        P(),
    )
    out_specs = (
        P(("grp", "rot", "ref"), "sub", None, None),
        P(("grp", "rot", "ref"), "sub", None, None, None),
    )
    return jax.shard_map(local, mesh=mesh, in_specs=in_specs, out_specs=out_specs, check_vma=False)
```

```python
import functools
import math

import jax
import jax.numpy as jnp
from jax import lax
from jax.experimental import pallas as pl
from jax.experimental.pallas import tpu as pltpu
from jax.sharding import PartitionSpec as P

CAP = 2


highest = lax.Precision.HIGH


def make_tables(length):
    counter = jnp.arange(length, dtype=jnp.int32)
    phases = counter[:, None] * counter[None, :] % length
    angles = phases.astype(jnp.float32) * (2.0 * math.pi / length)
    return (jnp.cos(angles), jnp.sin(angles))


def combine_kernel(me_ref, in_ref, out_ref, *, first, second):
    batch, _, rows, lanes = in_ref.shape
    split = out_ref.shape[0]
    part = rows // split
    half = lanes // 2
    low = lax.broadcasted_iota(jnp.int32, (1, lanes), 1) < half
    signs = jnp.where(low, first, second).astype(jnp.float32)
    me = me_ref[0]
    for piece in range(split):
        start = pl.multiple_of(((me + piece) % split) * part, 8)
        cos_part = in_ref[:, 0, pl.ds(start, part), :].reshape(batch * part, lanes)
        sin_part = in_ref[:, 1, pl.ds(start, part), :].reshape(batch * part, lanes)
        result = cos_part + pltpu.roll(sin_part, half, 1) * signs
        out_ref[piece] = result.reshape(batch, part, lanes).astype(out_ref.dtype)


def combine_call(stacked, first, second, split, dtype, me=0):
    batch, _, rows, lanes = stacked.shape
    block = max(b for b in range(1, 33) if batch % b == 0)
    part = rows // split
    return pl.pallas_call(
        functools.partial(combine_kernel, first=first, second=second),
        grid_spec=pltpu.PrefetchScalarGridSpec(
            num_scalar_prefetch=1,
            grid=(batch // block,),
            in_specs=[pl.BlockSpec((block, 2, rows, lanes), lambda i, me: (i, 0, 0, 0))],
            out_specs=pl.BlockSpec((split, block, part, lanes), lambda i, me: (0, i, 0, 0)),
        ),
        out_shape=jax.ShapeDtypeStruct((split, batch, part, lanes), dtype),
        cost_estimate=pl.CostEstimate(
            flops=3 * batch * rows * lanes,
            bytes_accessed=(8 + jnp.dtype(dtype).itemsize) * batch * rows * lanes,
            transcendentals=0,
        ),
    )(jnp.reshape(jnp.asarray(me, jnp.int32), (1,)), stacked)


def gather_by_shifts(piece, axis):
    count = lax.axis_size(axis)
    me = lax.axis_index(axis)
    pieces = [piece]
    for shift in range(1, count):
        pairs = [(k, (k + shift) % count) for k in range(count)]
        pieces.append(lax.ppermute(piece, axis, pairs))
    doubled = jnp.stack(pieces[::-1] * 2)
    return lax.dynamic_slice_in_dim(doubled, (count - 1 - me) % count, count, axis=0)


def exchange(sending, axis, rotated=False):
    count = lax.axis_size(axis)
    me = lax.axis_index(axis)

    def entry(shift):
        if rotated:
            return sending[shift]
        return lax.dynamic_index_in_dim(sending, (me + shift) % count, axis=0, keepdims=False)

    pieces = [(me, entry(0))]
    for shift in range(1, count):
        pairs = [(k, (k + shift) % count) for k in range(count)]
        pieces.append(((me - shift) % count, lax.ppermute(entry(shift), axis, pairs)))
    return pieces


def by_source(pieces):
    ordered = []
    for source in range(len(pieces)):
        chosen = pieces[0][1]
        for index, piece in pieces[1:]:
            chosen = jnp.where(index == source, piece, chosen)
        ordered.append(chosen)
    return ordered


def gather_receptor(receptor):
    _, terms, kx_local, ky_local, kz = receptor.shape
    n_ref = lax.axis_size("ref")
    n_rot = lax.axis_size("rot")
    rows = ky_local // n_ref
    block = lax.dynamic_slice_in_dim(receptor, lax.axis_index("ref") * rows, rows, axis=3)
    mine = jnp.concatenate([block[0], block[1]], axis=-1).astype(jnp.bfloat16)
    mine = jnp.swapaxes(mine, 1, 2)
    along_rot = gather_by_shifts(mine, "rot")
    both = gather_by_shifts(along_rot, "ref")
    both = jnp.transpose(both, (2, 0, 3, 1, 4, 5))
    return both.reshape(terms, ky_local, n_rot * kx_local, 2 * kz)


def product_kernel(*refs):
    *spec_refs, rec_ref, out_ref = refs
    rows, kx, lanes = out_ref.shape
    half = lanes // 2
    low = lax.broadcasted_iota(jnp.int32, (1, lanes), 1) < half
    signs = jnp.where(low, 1.0, -1.0).astype(jnp.float32)
    total = None
    term = 0
    for spec_ref in spec_refs:
        for inner in range(spec_ref.shape[0]):
            cos_part = spec_ref[inner, :, 0].reshape(rows * kx, lanes)
            sin_part = spec_ref[inner, :, 1].reshape(rows * kx, lanes)
            spec = cos_part + pltpu.roll(sin_part, half, 1) * signs
            spec = spec.astype(jnp.bfloat16).astype(jnp.float32)
            rec = rec_ref[term].reshape(rows * kx, lanes).astype(jnp.float32)
            term += 1
            rec_turned = pltpu.roll(rec, half, 1)
            rec_real = jnp.where(low, rec, rec_turned)
            rec_imag = jnp.where(low, rec_turned, -rec)
            part = rec_real * spec + rec_imag * pltpu.roll(spec, half, 1)
            total = part if total is None else total + part
    out_ref[...] = total.reshape(rows, kx, lanes)


def correlate(parts, receptor):
    rots, _, ky, _, kx, lanes = parts[0].shape
    terms = receptor.shape[0]
    block = 8 if ky % 8 == 0 else ky
    out = pl.pallas_call(
        product_kernel,
        grid=(rots, ky // block),
        in_specs=[
            pl.BlockSpec(
                (None, part.shape[1], block, 2, kx, lanes), lambda r, i: (r, 0, i, 0, 0, 0)
            )
            for part in parts
        ]
        + [pl.BlockSpec((terms, block, kx, lanes), lambda r, i: (0, i, 0, 0))],
        out_specs=pl.BlockSpec((None, block, kx, lanes), lambda r, i: (r, i, 0, 0)),
        out_shape=jax.ShapeDtypeStruct((rots, ky, kx, lanes), jnp.float32),
        cost_estimate=pl.CostEstimate(
            flops=11 * rots * terms * ky * kx * lanes,
            bytes_accessed=(8 * rots + 2) * terms * ky * kx * lanes + 4 * rots * ky * kx * lanes,
            transcendentals=0,
        ),
    )(*parts, receptor)
    return out


def local(ligand, receptor, tile_list, tile_owner, refine_weight):
    rots, terms, x_local, ny, nz = ligand.shape
    length = nz
    n_sub = lax.axis_size("sub")
    y_local = ny // n_sub
    cos_table, sin_table = make_tables(length)
    pair = jnp.stack([cos_table, sin_table])

    chunks = 2 if terms % 2 == 0 else 1
    part_terms = terms // chunks
    pair_x = pair.reshape(2, length, n_sub, x_local)
    z_table = jnp.concatenate([cos_table, -sin_table], axis=1)
    values = ligand.astype(jnp.float32)
    spectra = []
    for chunk in range(chunks):
        part = values[:, chunk * part_terms:(chunk + 1) * part_terms]
        along_z = jnp.einsum("rtxyz,zl->rtxyl", part, z_table, precision=highest)
        along_y = jnp.einsum("ejy,rtxyl->rtxejl", pair, along_z, precision=highest)
        sending = combine_call(
            along_y.reshape(-1, 2, ny, 2 * length), 1.0, -1.0, n_sub, jnp.bfloat16,
            lax.axis_index("sub"),
        ).reshape(n_sub, rots, part_terms, x_local, y_local, 2 * length)
        along_x = sum(
            jnp.einsum(
                "ekx,rtxjl->rtjekl", pair_x[:, :, source], piece.astype(jnp.float32),
                precision=highest,
            )
            for source, piece in enumerate(by_source(exchange(sending, "sub", rotated=True)))
        )
        spectra.append(along_x)

    whole_receptor = gather_receptor(receptor)
    product = correlate(spectra, whole_receptor)

    back_x = jnp.einsum("exk,rjkl->xrejl", pair, product, precision=highest)
    back_x = combine_call(back_x.reshape(-1, 2, y_local, 2 * length), -1.0, 1.0, 1, jnp.float32)
    back_x = back_x.reshape(n_sub, x_local, rots, y_local, 2 * length)
    pair_y = pair.reshape(2, length, n_sub, y_local)
    back_y = sum(
        jnp.einsum("eyj,xrjl->rxeyl", pair_y[:, :, source], piece, precision=highest)
        for source, piece in enumerate(by_source(exchange(back_x, "sub")))
    )
    back_y = combine_call(back_y.reshape(-1, 2, ny, 2 * length), -1.0, 1.0, 1, jnp.float32)
    back_y = back_y.reshape(rots, x_local, ny, 2 * length)
    last_table = jnp.concatenate([cos_table, -sin_table], axis=0)
    scores = jnp.einsum("rxyl,lz->rxyz", back_y, last_table, precision=highest) / float(length**3)

    tile_cells = 8 * length
    tile_rows = scores.reshape(-1, tile_cells)
    listing = tile_list.reshape(-1)
    owners = tile_owner.reshape(-1)
    listed = listing.shape[0]
    chosen = tile_rows[listing]
    owner_count = lax.axis_size(("rot", "ref"))
    order = jnp.arange(listed, dtype=jnp.int32)
    earlier = (owners[:, None] == owners[None, :]) & (order[None, :] < order[:, None])
    slot = jnp.sum(earlier.astype(jnp.int32), axis=1)
    target = owners * CAP + slot
    placing = (jnp.arange(owner_count * CAP, dtype=jnp.int32)[:, None] == target[None, :]).astype(
        jnp.float32
    )
    done = jnp.dot(chosen, refine_weight, precision=highest)
    packed = jnp.dot(placing, done, precision=highest).reshape(owner_count, CAP, tile_cells)
    refined = lax.all_to_all(packed, ("rot", "ref"), split_axis=0, concat_axis=0, tiled=True)
    return (scores, refined.reshape(1, 1, owner_count, CAP, tile_cells))


def solution(mesh):
    in_specs = (
        P(("grp", "rot", "ref"), None, "sub", None, None),
        P("grp", None, "rot", "sub", None),
        P(("grp", "rot"), "sub", "ref", None),
        P(("grp", "rot"), "sub", "ref", None, None),
        P(),
    )
    out_specs = (
        P(("grp", "rot", "ref"), "sub", None, None),
        P(("grp", "rot", "ref"), "sub", None, None, None),
    )
    return jax.shard_map(local, mesh=mesh, in_specs=in_specs, out_specs=out_specs, check_vma=False)
```

```python
import functools
import math

import jax
import jax.numpy as jnp
from jax import lax
from jax.experimental import pallas as pl
from jax.experimental.pallas import tpu as pltpu
from jax.sharding import PartitionSpec as P

CAP = 2


highest = lax.Precision.HIGH


def make_tables(length):
    counter = jnp.arange(length, dtype=jnp.int32)
    phases = counter[:, None] * counter[None, :] % length
    angles = phases.astype(jnp.float32) * (2.0 * math.pi / length)
    return (jnp.cos(angles), jnp.sin(angles))


def combine_kernel(me_ref, in_ref, out_ref, *, first, second):
    batch, _, rows, lanes = in_ref.shape
    split = out_ref.shape[0]
    part = rows // split
    half = lanes // 2
    low = lax.broadcasted_iota(jnp.int32, (1, lanes), 1) < half
    signs = jnp.where(low, first, second).astype(jnp.float32)
    me = me_ref[0]
    for piece in range(split):
        start = pl.multiple_of(((me + piece) % split) * part, 8)
        cos_part = in_ref[:, 0, pl.ds(start, part), :].reshape(batch * part, lanes)
        sin_part = in_ref[:, 1, pl.ds(start, part), :].reshape(batch * part, lanes)
        result = cos_part + pltpu.roll(sin_part, half, 1) * signs
        out_ref[piece] = result.reshape(batch, part, lanes).astype(out_ref.dtype)


def combine_call(stacked, first, second, split, dtype, me=0):
    batch, _, rows, lanes = stacked.shape
    block = max(b for b in range(1, 9) if batch % b == 0)
    part = rows // split
    return pl.pallas_call(
        functools.partial(combine_kernel, first=first, second=second),
        grid_spec=pltpu.PrefetchScalarGridSpec(
            num_scalar_prefetch=1,
            grid=(batch // block,),
            in_specs=[pl.BlockSpec((block, 2, rows, lanes), lambda i, me: (i, 0, 0, 0))],
            out_specs=pl.BlockSpec((split, block, part, lanes), lambda i, me: (0, i, 0, 0)),
        ),
        out_shape=jax.ShapeDtypeStruct((split, batch, part, lanes), dtype),
        cost_estimate=pl.CostEstimate(
            flops=3 * batch * rows * lanes,
            bytes_accessed=(8 + jnp.dtype(dtype).itemsize) * batch * rows * lanes,
            transcendentals=0,
        ),
    )(jnp.reshape(jnp.asarray(me, jnp.int32), (1,)), stacked)


def gather_by_shifts(piece, axis):
    count = lax.axis_size(axis)
    me = lax.axis_index(axis)
    pieces = [piece]
    for shift in range(1, count):
        pairs = [(k, (k + shift) % count) for k in range(count)]
        pieces.append(lax.ppermute(piece, axis, pairs))
    doubled = jnp.stack(pieces[::-1] * 2)
    return lax.dynamic_slice_in_dim(doubled, (count - 1 - me) % count, count, axis=0)


def exchange(sending, axis, rotated=False):
    count = lax.axis_size(axis)
    me = lax.axis_index(axis)

    def entry(shift):
        if rotated:
            return sending[shift]
        return lax.dynamic_index_in_dim(sending, (me + shift) % count, axis=0, keepdims=False)

    pieces = [(me, entry(0))]
    for shift in range(1, count):
        pairs = [(k, (k + shift) % count) for k in range(count)]
        pieces.append(((me - shift) % count, lax.ppermute(entry(shift), axis, pairs)))
    return pieces


def by_source(pieces):
    ordered = []
    for source in range(len(pieces)):
        chosen = pieces[0][1]
        for index, piece in pieces[1:]:
            chosen = jnp.where(index == source, piece, chosen)
        ordered.append(chosen)
    return ordered


def gather_receptor(receptor):
    _, terms, kx_local, ky_local, kz = receptor.shape
    n_ref = lax.axis_size("ref")
    n_rot = lax.axis_size("rot")
    rows = ky_local // n_ref
    block = lax.dynamic_slice_in_dim(receptor, lax.axis_index("ref") * rows, rows, axis=3)
    mine = jnp.concatenate([block[0], block[1]], axis=-1).astype(jnp.bfloat16)
    mine = jnp.swapaxes(mine, 1, 2)
    along_rot = gather_by_shifts(mine, "rot")
    both = gather_by_shifts(along_rot, "ref")
    both = jnp.transpose(both, (2, 0, 3, 1, 4, 5))
    return both.reshape(terms, ky_local, n_rot * kx_local, 2 * kz)


def product_kernel(*refs):
    *spec_refs, rec_ref, out_ref = refs
    lanes = out_ref.shape[-1]
    half = lanes // 2
    total = None
    term = 0
    for spec_ref in spec_refs:
        for inner in range(spec_ref.shape[0]):
            spec = spec_ref[inner].astype(jnp.float32)
            rec = rec_ref[term].astype(jnp.float32)
            term += 1
            low = lax.broadcasted_iota(jnp.int32, (1, lanes), 1) < half
            rec_turned = pltpu.roll(rec, half, 1)
            rec_real = jnp.where(low, rec, rec_turned)
            rec_imag = jnp.where(low, rec_turned, -rec)
            part = rec_real * spec + rec_imag * pltpu.roll(spec, half, 1)
            total = part if total is None else total + part
    out_ref[...] = total


def correlate(spectra, receptor):
    rots, _, kx, ky, lanes = spectra[0].shape
    terms = receptor.shape[0]
    rows = kx * ky
    block = min(rows, 512)
    specs = [part.reshape(rots, part.shape[1], rows, lanes) for part in spectra]
    rec = receptor.reshape(terms, rows, lanes)
    out = pl.pallas_call(
        product_kernel,
        grid=(rots, rows // block),
        in_specs=[
            pl.BlockSpec((None, part.shape[1], block, lanes), lambda r, i: (r, 0, i, 0))
            for part in specs
        ]
        + [pl.BlockSpec((terms, block, lanes), lambda r, i: (0, i, 0))],
        out_specs=pl.BlockSpec((None, block, lanes), lambda r, i: (r, i, 0)),
        out_shape=jax.ShapeDtypeStruct((rots, rows, lanes), jnp.float32),
        cost_estimate=pl.CostEstimate(
            flops=8 * rots * terms * rows * lanes,
            bytes_accessed=2 * (rots + 1) * terms * rows * lanes + 4 * rots * rows * lanes,
            transcendentals=0,
        ),
    )(*specs, rec)
    return out.reshape(rots, kx, ky, lanes)


def local(ligand, receptor, tile_list, tile_owner, refine_weight):
    rots, terms, x_local, ny, nz = ligand.shape
    length = nz
    n_sub = lax.axis_size("sub")
    y_local = ny // n_sub
    cos_table, sin_table = make_tables(length)
    pair = jnp.stack([cos_table, sin_table])

    chunks = 2 if terms % 2 == 0 else 1
    part_terms = terms // chunks
    pair_x = pair.reshape(2, length, n_sub, x_local)
    z_table = jnp.concatenate([cos_table, -sin_table], axis=1)
    values = ligand.astype(jnp.float32)
    spectra = []
    for chunk in range(chunks):
        part = values[:, chunk * part_terms:(chunk + 1) * part_terms]
        along_z = jnp.einsum("rtxyz,zl->rtxyl", part, z_table, precision=highest)
        along_y = jnp.einsum("ejy,rtxyl->rtxejl", pair, along_z, precision=highest)
        sending = combine_call(
            along_y.reshape(-1, 2, ny, 2 * length), 1.0, -1.0, n_sub, jnp.bfloat16,
            lax.axis_index("sub"),
        ).reshape(n_sub, rots, part_terms, x_local, y_local, 2 * length)
        along_x = sum(
            jnp.einsum(
                "ekx,rtxjl->rtjekl", pair_x[:, :, source], piece.astype(jnp.float32),
                precision=highest,
            )
            for source, piece in enumerate(by_source(exchange(sending, "sub", rotated=True)))
        )
        spectrum = combine_call(
            along_x.reshape(-1, 2, length, 2 * length), 1.0, -1.0, 1, jnp.bfloat16
        )
        spectra.append(spectrum.reshape(rots, part_terms, y_local, length, 2 * length))

    whole_receptor = gather_receptor(receptor)
    product = correlate(spectra, whole_receptor)

    back_x = jnp.einsum("exk,rjkl->xrejl", pair, product, precision=highest)
    back_x = combine_call(back_x.reshape(-1, 2, y_local, 2 * length), -1.0, 1.0, 1, jnp.float32)
    back_x = back_x.reshape(n_sub, x_local, rots, y_local, 2 * length)
    pair_y = pair.reshape(2, length, n_sub, y_local)
    back_y = sum(
        jnp.einsum("eyj,xrjl->rxeyl", pair_y[:, :, source], piece, precision=highest)
        for source, piece in enumerate(by_source(exchange(back_x, "sub")))
    )
    back_y = combine_call(back_y.reshape(-1, 2, ny, 2 * length), -1.0, 1.0, 1, jnp.float32)
    back_y = back_y.reshape(rots, x_local, ny, 2 * length)
    last_table = jnp.concatenate([cos_table, -sin_table], axis=0)
    scores = jnp.einsum("rxyl,lz->rxyz", back_y, last_table, precision=highest) / float(length**3)

    tile_cells = 8 * length
    tile_rows = scores.reshape(-1, tile_cells)
    listing = tile_list.reshape(-1)
    owners = tile_owner.reshape(-1)
    listed = listing.shape[0]
    chosen = tile_rows[listing]
    owner_count = lax.axis_size(("rot", "ref"))
    order = jnp.arange(listed, dtype=jnp.int32)
    earlier = (owners[:, None] == owners[None, :]) & (order[None, :] < order[:, None])
    slot = jnp.sum(earlier.astype(jnp.int32), axis=1)
    target = owners * CAP + slot
    placing = (jnp.arange(owner_count * CAP, dtype=jnp.int32)[:, None] == target[None, :]).astype(
        jnp.float32
    )
    done = jnp.dot(chosen, refine_weight, precision=highest)
    packed = jnp.dot(placing, done, precision=highest).reshape(owner_count, CAP, tile_cells)
    refined = lax.all_to_all(packed, ("rot", "ref"), split_axis=0, concat_axis=0, tiled=True)
    return (scores, refined.reshape(1, 1, owner_count, CAP, tile_cells))


def solution(mesh):
    in_specs = (
        P(("grp", "rot", "ref"), None, "sub", None, None),
        P("grp", None, "rot", "sub", None),
        P(("grp", "rot"), "sub", "ref", None),
        P(("grp", "rot"), "sub", "ref", None, None),
        P(),
    )
    out_specs = (
        P(("grp", "rot", "ref"), "sub", None, None),
        P(("grp", "rot", "ref"), "sub", None, None, None),
    )
    return jax.shard_map(local, mesh=mesh, in_specs=in_specs, out_specs=out_specs, check_vma=False)
```

```python
import functools
import math

import jax
import jax.numpy as jnp
from jax import lax
from jax.experimental import pallas as pl
from jax.experimental.pallas import tpu as pltpu
from jax.sharding import PartitionSpec as P

CAP = 2


highest = lax.Precision.HIGH


def make_tables(length):
    counter = jnp.arange(length, dtype=jnp.int32)
    phases = counter[:, None] * counter[None, :] % length
    angles = phases.astype(jnp.float32) * (2.0 * math.pi / length)
    return (jnp.cos(angles), jnp.sin(angles))


def combine_kernel(me_ref, in_ref, out_ref, *, first, second):
    batch, _, rows, lanes = in_ref.shape
    split = out_ref.shape[0]
    part = rows // split
    half = lanes // 2
    low = lax.broadcasted_iota(jnp.int32, (1, lanes), 1) < half
    signs = jnp.where(low, first, second).astype(jnp.float32)
    me = me_ref[0]
    for piece in range(split):
        start = pl.multiple_of(((me + piece) % split) * part, 8)
        cos_part = in_ref[:, 0, pl.ds(start, part), :].reshape(batch * part, lanes)
        sin_part = in_ref[:, 1, pl.ds(start, part), :].reshape(batch * part, lanes)
        result = cos_part + pltpu.roll(sin_part, half, 1) * signs
        out_ref[piece] = result.reshape(batch, part, lanes).astype(out_ref.dtype)


def combine_call(stacked, first, second, split, dtype, me=0):
    batch, _, rows, lanes = stacked.shape
    block = max(b for b in range(1, 65) if batch % b == 0)
    part = rows // split
    return pl.pallas_call(
        functools.partial(combine_kernel, first=first, second=second),
        grid_spec=pltpu.PrefetchScalarGridSpec(
            num_scalar_prefetch=1,
            grid=(batch // block,),
            in_specs=[pl.BlockSpec((block, 2, rows, lanes), lambda i, me: (i, 0, 0, 0))],
            out_specs=pl.BlockSpec((split, block, part, lanes), lambda i, me: (0, i, 0, 0)),
        ),
        out_shape=jax.ShapeDtypeStruct((split, batch, part, lanes), dtype),
        cost_estimate=pl.CostEstimate(
            flops=3 * batch * rows * lanes,
            bytes_accessed=(8 + jnp.dtype(dtype).itemsize) * batch * rows * lanes,
            transcendentals=0,
        ),
    )(jnp.reshape(jnp.asarray(me, jnp.int32), (1,)), stacked)


def gather_by_shifts(piece, axis):
    count = lax.axis_size(axis)
    me = lax.axis_index(axis)
    pieces = [piece]
    for shift in range(1, count):
        pairs = [(k, (k + shift) % count) for k in range(count)]
        pieces.append(lax.ppermute(piece, axis, pairs))
    doubled = jnp.stack(pieces[::-1] * 2)
    return lax.dynamic_slice_in_dim(doubled, (count - 1 - me) % count, count, axis=0)


def exchange(sending, axis, rotated=False):
    count = lax.axis_size(axis)
    me = lax.axis_index(axis)

    def entry(shift):
        if rotated:
            return sending[shift]
        return lax.dynamic_index_in_dim(sending, (me + shift) % count, axis=0, keepdims=False)

    pieces = [(me, entry(0))]
    for shift in range(1, count):
        pairs = [(k, (k + shift) % count) for k in range(count)]
        pieces.append(((me - shift) % count, lax.ppermute(entry(shift), axis, pairs)))
    return pieces


def by_source(pieces):
    ordered = []
    for source in range(len(pieces)):
        chosen = pieces[0][1]
        for index, piece in pieces[1:]:
            chosen = jnp.where(index == source, piece, chosen)
        ordered.append(chosen)
    return ordered


def gather_receptor(receptor):
    _, terms, kx_local, ky_local, kz = receptor.shape
    n_ref = lax.axis_size("ref")
    n_rot = lax.axis_size("rot")
    rows = ky_local // n_ref
    block = lax.dynamic_slice_in_dim(receptor, lax.axis_index("ref") * rows, rows, axis=3)
    mine = jnp.concatenate([block[0], block[1]], axis=-1).astype(jnp.bfloat16)
    mine = jnp.swapaxes(mine, 1, 2)
    along_rot = gather_by_shifts(mine, "rot")
    both = gather_by_shifts(along_rot, "ref")
    both = jnp.transpose(both, (2, 0, 3, 1, 4, 5))
    return both.reshape(terms, ky_local, n_rot * kx_local, 2 * kz)


def product_kernel(*refs):
    *spec_refs, rec_ref, out_ref = refs
    lanes = out_ref.shape[-1]
    half = lanes // 2
    total = None
    term = 0
    for spec_ref in spec_refs:
        for inner in range(spec_ref.shape[0]):
            spec = spec_ref[inner].astype(jnp.float32)
            rec = rec_ref[term].astype(jnp.float32)
            term += 1
            low = lax.broadcasted_iota(jnp.int32, (1, lanes), 1) < half
            rec_turned = pltpu.roll(rec, half, 1)
            rec_real = jnp.where(low, rec, rec_turned)
            rec_imag = jnp.where(low, rec_turned, -rec)
            part = rec_real * spec + rec_imag * pltpu.roll(spec, half, 1)
            total = part if total is None else total + part
    out_ref[...] = total


def correlate(spectra, receptor):
    rots, _, kx, ky, lanes = spectra[0].shape
    terms = receptor.shape[0]
    rows = kx * ky
    block = min(rows, 512)
    specs = [part.reshape(rots, part.shape[1], rows, lanes) for part in spectra]
    rec = receptor.reshape(terms, rows, lanes)
    out = pl.pallas_call(
        product_kernel,
        grid=(rots, rows // block),
        in_specs=[
            pl.BlockSpec((None, part.shape[1], block, lanes), lambda r, i: (r, 0, i, 0))
            for part in specs
        ]
        + [pl.BlockSpec((terms, block, lanes), lambda r, i: (0, i, 0))],
        out_specs=pl.BlockSpec((None, block, lanes), lambda r, i: (r, i, 0)),
        out_shape=jax.ShapeDtypeStruct((rots, rows, lanes), jnp.float32),
        cost_estimate=pl.CostEstimate(
            flops=8 * rots * terms * rows * lanes,
            bytes_accessed=2 * (rots + 1) * terms * rows * lanes + 4 * rots * rows * lanes,
            transcendentals=0,
        ),
    )(*specs, rec)
    return out.reshape(rots, kx, ky, lanes)


def local(ligand, receptor, tile_list, tile_owner, refine_weight):
    rots, terms, x_local, ny, nz = ligand.shape
    length = nz
    n_sub = lax.axis_size("sub")
    y_local = ny // n_sub
    cos_table, sin_table = make_tables(length)
    pair = jnp.stack([cos_table, sin_table])

    chunks = 2 if terms % 2 == 0 else 1
    part_terms = terms // chunks
    pair_x = pair.reshape(2, length, n_sub, x_local)
    z_table = jnp.concatenate([cos_table, -sin_table], axis=1)
    values = ligand.astype(jnp.float32)
    spectra = []
    for chunk in range(chunks):
        part = values[:, chunk * part_terms:(chunk + 1) * part_terms]
        along_z = jnp.einsum("rtxyz,zl->rtxyl", part, z_table, precision=highest)
        along_y = jnp.einsum("ejy,rtxyl->rtxejl", pair, along_z, precision=highest)
        sending = combine_call(
            along_y.reshape(-1, 2, ny, 2 * length), 1.0, -1.0, n_sub, jnp.bfloat16,
            lax.axis_index("sub"),
        ).reshape(n_sub, rots, part_terms, x_local, y_local, 2 * length)
        along_x = sum(
            jnp.einsum(
                "ekx,rtxjl->rtjekl", pair_x[:, :, source], piece.astype(jnp.float32),
                precision=highest,
            )
            for source, piece in enumerate(by_source(exchange(sending, "sub", rotated=True)))
        )
        spectrum = combine_call(
            along_x.reshape(-1, 2, length, 2 * length), 1.0, -1.0, 1, jnp.bfloat16
        )
        spectra.append(spectrum.reshape(rots, part_terms, y_local, length, 2 * length))

    whole_receptor = gather_receptor(receptor)
    product = correlate(spectra, whole_receptor)

    back_x = jnp.einsum("exk,rjkl->xrejl", pair, product, precision=highest)
    back_x = combine_call(back_x.reshape(-1, 2, y_local, 2 * length), -1.0, 1.0, 1, jnp.float32)
    back_x = back_x.reshape(n_sub, x_local, rots, y_local, 2 * length)
    pair_y = pair.reshape(2, length, n_sub, y_local)
    back_y = sum(
        jnp.einsum("eyj,xrjl->rxeyl", pair_y[:, :, source], piece, precision=highest)
        for source, piece in enumerate(by_source(exchange(back_x, "sub")))
    )
    back_y = combine_call(back_y.reshape(-1, 2, ny, 2 * length), -1.0, 1.0, 1, jnp.float32)
    back_y = back_y.reshape(rots, x_local, ny, 2 * length)
    last_table = jnp.concatenate([cos_table, -sin_table], axis=0)
    scores = jnp.einsum("rxyl,lz->rxyz", back_y, last_table, precision=highest) / float(length**3)

    tile_cells = 8 * length
    tile_rows = scores.reshape(-1, tile_cells)
    listing = tile_list.reshape(-1)
    owners = tile_owner.reshape(-1)
    listed = listing.shape[0]
    chosen = tile_rows[listing]
    owner_count = lax.axis_size(("rot", "ref"))
    order = jnp.arange(listed, dtype=jnp.int32)
    earlier = (owners[:, None] == owners[None, :]) & (order[None, :] < order[:, None])
    slot = jnp.sum(earlier.astype(jnp.int32), axis=1)
    target = owners * CAP + slot
    placing = (jnp.arange(owner_count * CAP, dtype=jnp.int32)[:, None] == target[None, :]).astype(
        jnp.float32
    )
    done = jnp.dot(chosen, refine_weight, precision=highest)
    packed = jnp.dot(placing, done, precision=highest).reshape(owner_count, CAP, tile_cells)
    refined = lax.all_to_all(packed, ("rot", "ref"), split_axis=0, concat_axis=0, tiled=True)
    return (scores, refined.reshape(1, 1, owner_count, CAP, tile_cells))


def solution(mesh):
    in_specs = (
        P(("grp", "rot", "ref"), None, "sub", None, None),
        P("grp", None, "rot", "sub", None),
        P(("grp", "rot"), "sub", "ref", None),
        P(("grp", "rot"), "sub", "ref", None, None),
        P(),
    )
    out_specs = (
        P(("grp", "rot", "ref"), "sub", None, None),
        P(("grp", "rot", "ref"), "sub", None, None, None),
    )
    return jax.shard_map(local, mesh=mesh, in_specs=in_specs, out_specs=out_specs, check_vma=False)
```

```python
import functools
import math

import jax
import jax.numpy as jnp
from jax import lax
from jax.experimental import pallas as pl
from jax.experimental.pallas import tpu as pltpu
from jax.sharding import PartitionSpec as P

CAP = 2


highest = lax.Precision.HIGH


def make_tables(length):
    counter = jnp.arange(length, dtype=jnp.int32)
    phases = counter[:, None] * counter[None, :] % length
    angles = phases.astype(jnp.float32) * (2.0 * math.pi / length)
    return (jnp.cos(angles), jnp.sin(angles))


def combine_kernel(me_ref, in_ref, out_ref, *, first, second):
    batch, _, rows, lanes = in_ref.shape
    split = out_ref.shape[0]
    part = rows // split
    half = lanes // 2
    low = lax.broadcasted_iota(jnp.int32, (1, lanes), 1) < half
    signs = jnp.where(low, first, second).astype(jnp.float32)
    me = me_ref[0]
    for piece in range(split):
        start = pl.multiple_of(((me + piece) % split) * part, 8)
        cos_part = in_ref[:, 0, pl.ds(start, part), :].reshape(batch * part, lanes)
        sin_part = in_ref[:, 1, pl.ds(start, part), :].reshape(batch * part, lanes)
        result = cos_part + pltpu.roll(sin_part, half, 1) * signs
        out_ref[piece] = result.reshape(batch, part, lanes).astype(out_ref.dtype)


def combine_call(stacked, first, second, split, dtype, me=0):
    batch, _, rows, lanes = stacked.shape
    block = max(b for b in range(1, 33) if batch % b == 0)
    part = rows // split
    return pl.pallas_call(
        functools.partial(combine_kernel, first=first, second=second),
        grid_spec=pltpu.PrefetchScalarGridSpec(
            num_scalar_prefetch=1,
            grid=(batch // block,),
            in_specs=[pl.BlockSpec((block, 2, rows, lanes), lambda i, me: (i, 0, 0, 0))],
            out_specs=pl.BlockSpec((split, block, part, lanes), lambda i, me: (0, i, 0, 0)),
        ),
        out_shape=jax.ShapeDtypeStruct((split, batch, part, lanes), dtype),
        cost_estimate=pl.CostEstimate(
            flops=3 * batch * rows * lanes,
            bytes_accessed=(8 + jnp.dtype(dtype).itemsize) * batch * rows * lanes,
            transcendentals=0,
        ),
    )(jnp.reshape(jnp.asarray(me, jnp.int32), (1,)), stacked)


def gather_by_shifts(piece, axis):
    count = lax.axis_size(axis)
    me = lax.axis_index(axis)
    pieces = [piece]
    for shift in range(1, count):
        pairs = [(k, (k + shift) % count) for k in range(count)]
        pieces.append(lax.ppermute(piece, axis, pairs))
    doubled = jnp.stack(pieces[::-1] * 2)
    return lax.dynamic_slice_in_dim(doubled, (count - 1 - me) % count, count, axis=0)


def exchange(sending, axis, rotated=False):
    count = lax.axis_size(axis)
    me = lax.axis_index(axis)

    def entry(shift):
        if rotated:
            return sending[shift]
        return lax.dynamic_index_in_dim(sending, (me + shift) % count, axis=0, keepdims=False)

    pieces = [(me, entry(0))]
    for shift in range(1, count):
        pairs = [(k, (k + shift) % count) for k in range(count)]
        pieces.append(((me - shift) % count, lax.ppermute(entry(shift), axis, pairs)))
    return pieces


def by_source(pieces):
    ordered = []
    for source in range(len(pieces)):
        chosen = pieces[0][1]
        for index, piece in pieces[1:]:
            chosen = jnp.where(index == source, piece, chosen)
        ordered.append(chosen)
    return ordered


def gather_receptor(receptor):
    _, terms, kx_local, ky_local, kz = receptor.shape
    n_ref = lax.axis_size("ref")
    n_rot = lax.axis_size("rot")
    rows = ky_local // n_ref
    block = lax.dynamic_slice_in_dim(receptor, lax.axis_index("ref") * rows, rows, axis=3)
    mine = jnp.concatenate([block[0], block[1]], axis=-1).astype(jnp.bfloat16)
    mine = jnp.swapaxes(mine, 1, 2)
    along_rot = gather_by_shifts(mine, "rot")
    both = gather_by_shifts(along_rot, "ref")
    both = jnp.transpose(both, (2, 0, 3, 1, 4, 5))
    return both.reshape(terms, ky_local, n_rot * kx_local, 2 * kz)


def product_kernel(*refs):
    *spec_refs, rec_ref, out_ref = refs
    lanes = out_ref.shape[-1]
    half = lanes // 2
    total = None
    term = 0
    for spec_ref in spec_refs:
        for inner in range(spec_ref.shape[0]):
            spec = spec_ref[inner].astype(jnp.float32)
            rec = rec_ref[term].astype(jnp.float32)
            term += 1
            low = lax.broadcasted_iota(jnp.int32, (1, lanes), 1) < half
            rec_turned = pltpu.roll(rec, half, 1)
            rec_real = jnp.where(low, rec, rec_turned)
            rec_imag = jnp.where(low, rec_turned, -rec)
            part = rec_real * spec + rec_imag * pltpu.roll(spec, half, 1)
            total = part if total is None else total + part
    out_ref[...] = total


def correlate(spectra, receptor):
    rots, _, kx, ky, lanes = spectra[0].shape
    terms = receptor.shape[0]
    rows = kx * ky
    block = min(rows, 1024)
    specs = [part.reshape(rots, part.shape[1], rows, lanes) for part in spectra]
    rec = receptor.reshape(terms, rows, lanes)
    out = pl.pallas_call(
        product_kernel,
        grid=(rots, rows // block),
        in_specs=[
            pl.BlockSpec((None, part.shape[1], block, lanes), lambda r, i: (r, 0, i, 0))
            for part in specs
        ]
        + [pl.BlockSpec((terms, block, lanes), lambda r, i: (0, i, 0))],
        out_specs=pl.BlockSpec((None, block, lanes), lambda r, i: (r, i, 0)),
        out_shape=jax.ShapeDtypeStruct((rots, rows, lanes), jnp.float32),
        cost_estimate=pl.CostEstimate(
            flops=8 * rots * terms * rows * lanes,
            bytes_accessed=2 * (rots + 1) * terms * rows * lanes + 4 * rots * rows * lanes,
            transcendentals=0,
        ),
    )(*specs, rec)
    return out.reshape(rots, kx, ky, lanes)


def local(ligand, receptor, tile_list, tile_owner, refine_weight):
    rots, terms, x_local, ny, nz = ligand.shape
    length = nz
    n_sub = lax.axis_size("sub")
    y_local = ny // n_sub
    cos_table, sin_table = make_tables(length)
    pair = jnp.stack([cos_table, sin_table])

    chunks = 2 if terms % 2 == 0 else 1
    part_terms = terms // chunks
    pair_x = pair.reshape(2, length, n_sub, x_local)
    z_table = jnp.concatenate([cos_table, -sin_table], axis=1)
    values = ligand.astype(jnp.float32)
    spectra = []
    for chunk in range(chunks):
        part = values[:, chunk * part_terms:(chunk + 1) * part_terms]
        along_z = jnp.einsum("rtxyz,zl->rtxyl", part, z_table, precision=highest)
        along_y = jnp.einsum("ejy,rtxyl->rtxejl", pair, along_z, precision=highest)
        sending = combine_call(
            along_y.reshape(-1, 2, ny, 2 * length), 1.0, -1.0, n_sub, jnp.bfloat16,
            lax.axis_index("sub"),
        ).reshape(n_sub, rots, part_terms, x_local, y_local, 2 * length)
        along_x = sum(
            jnp.einsum(
                "ekx,rtxjl->rtjekl", pair_x[:, :, source], piece.astype(jnp.float32),
                precision=highest,
            )
            for source, piece in enumerate(by_source(exchange(sending, "sub", rotated=True)))
        )
        spectrum = combine_call(
            along_x.reshape(-1, 2, length, 2 * length), 1.0, -1.0, 1, jnp.bfloat16
        )
        spectra.append(spectrum.reshape(rots, part_terms, y_local, length, 2 * length))

    whole_receptor = gather_receptor(receptor)
    product = correlate(spectra, whole_receptor)

    back_x = jnp.einsum("exk,rjkl->xrejl", pair, product, precision=highest)
    back_x = combine_call(back_x.reshape(-1, 2, y_local, 2 * length), -1.0, 1.0, 1, jnp.float32)
    back_x = back_x.reshape(n_sub, x_local, rots, y_local, 2 * length)
    pair_y = pair.reshape(2, length, n_sub, y_local)
    back_y = sum(
        jnp.einsum("eyj,xrjl->rxeyl", pair_y[:, :, source], piece, precision=highest)
        for source, piece in enumerate(by_source(exchange(back_x, "sub")))
    )
    back_y = combine_call(back_y.reshape(-1, 2, ny, 2 * length), -1.0, 1.0, 1, jnp.float32)
    back_y = back_y.reshape(rots, x_local, ny, 2 * length)
    last_table = jnp.concatenate([cos_table, -sin_table], axis=0)
    scores = jnp.einsum("rxyl,lz->rxyz", back_y, last_table, precision=highest) / float(length**3)

    tile_cells = 8 * length
    tile_rows = scores.reshape(-1, tile_cells)
    listing = tile_list.reshape(-1)
    owners = tile_owner.reshape(-1)
    listed = listing.shape[0]
    chosen = tile_rows[listing]
    owner_count = lax.axis_size(("rot", "ref"))
    order = jnp.arange(listed, dtype=jnp.int32)
    earlier = (owners[:, None] == owners[None, :]) & (order[None, :] < order[:, None])
    slot = jnp.sum(earlier.astype(jnp.int32), axis=1)
    target = owners * CAP + slot
    placing = (jnp.arange(owner_count * CAP, dtype=jnp.int32)[:, None] == target[None, :]).astype(
        jnp.float32
    )
    done = jnp.dot(chosen, refine_weight, precision=highest)
    packed = jnp.dot(placing, done, precision=highest).reshape(owner_count, CAP, tile_cells)
    refined = lax.all_to_all(packed, ("rot", "ref"), split_axis=0, concat_axis=0, tiled=True)
    return (scores, refined.reshape(1, 1, owner_count, CAP, tile_cells))


def solution(mesh):
    in_specs = (
        P(("grp", "rot", "ref"), None, "sub", None, None),
        P("grp", None, "rot", "sub", None),
        P(("grp", "rot"), "sub", "ref", None),
        P(("grp", "rot"), "sub", "ref", None, None),
        P(),
    )
    out_specs = (
        P(("grp", "rot", "ref"), "sub", None, None),
        P(("grp", "rot", "ref"), "sub", None, None, None),
    )
    return jax.shard_map(local, mesh=mesh, in_specs=in_specs, out_specs=out_specs, check_vma=False)
```

```python
import functools
import math

import jax
import jax.numpy as jnp
from jax import lax
from jax.experimental import pallas as pl
from jax.experimental.pallas import tpu as pltpu
from jax.sharding import PartitionSpec as P

CAP = 2


highest = lax.Precision.HIGH


def make_tables(length):
    counter = jnp.arange(length, dtype=jnp.int32)
    phases = counter[:, None] * counter[None, :] % length
    angles = phases.astype(jnp.float32) * (2.0 * math.pi / length)
    return (jnp.cos(angles), jnp.sin(angles))


def combine_kernel(me_ref, in_ref, out_ref, *, first, second):
    batch, _, rows, lanes = in_ref.shape
    split = out_ref.shape[0]
    part = rows // split
    half = lanes // 2
    low = lax.broadcasted_iota(jnp.int32, (1, lanes), 1) < half
    signs = jnp.where(low, first, second).astype(jnp.float32)
    me = me_ref[0]
    for piece in range(split):
        start = pl.multiple_of(((me + piece) % split) * part, 8)
        cos_part = in_ref[:, 0, pl.ds(start, part), :].reshape(batch * part, lanes)
        sin_part = in_ref[:, 1, pl.ds(start, part), :].reshape(batch * part, lanes)
        result = cos_part + pltpu.roll(sin_part, half, 1) * signs
        out_ref[piece] = result.reshape(batch, part, lanes).astype(out_ref.dtype)


def combine_call(stacked, first, second, split, dtype, me=0):
    batch, _, rows, lanes = stacked.shape
    block = max(b for b in range(1, 33) if batch % b == 0)
    part = rows // split
    return pl.pallas_call(
        functools.partial(combine_kernel, first=first, second=second),
        grid_spec=pltpu.PrefetchScalarGridSpec(
            num_scalar_prefetch=1,
            grid=(batch // block,),
            in_specs=[pl.BlockSpec((block, 2, rows, lanes), lambda i, me: (i, 0, 0, 0))],
            out_specs=pl.BlockSpec((split, block, part, lanes), lambda i, me: (0, i, 0, 0)),
        ),
        out_shape=jax.ShapeDtypeStruct((split, batch, part, lanes), dtype),
        cost_estimate=pl.CostEstimate(
            flops=3 * batch * rows * lanes,
            bytes_accessed=(8 + jnp.dtype(dtype).itemsize) * batch * rows * lanes,
            transcendentals=0,
        ),
    )(jnp.reshape(jnp.asarray(me, jnp.int32), (1,)), stacked)


def gather_by_shifts(piece, axis):
    count = lax.axis_size(axis)
    me = lax.axis_index(axis)
    pieces = [piece]
    for shift in range(1, count):
        pairs = [(k, (k + shift) % count) for k in range(count)]
        pieces.append(lax.ppermute(piece, axis, pairs))
    doubled = jnp.stack(pieces[::-1] * 2)
    return lax.dynamic_slice_in_dim(doubled, (count - 1 - me) % count, count, axis=0)


def exchange(sending, axis, rotated=False):
    count = lax.axis_size(axis)
    me = lax.axis_index(axis)

    def entry(shift):
        if rotated:
            return sending[shift]
        return lax.dynamic_index_in_dim(sending, (me + shift) % count, axis=0, keepdims=False)

    pieces = [(me, entry(0))]
    for shift in range(1, count):
        pairs = [(k, (k + shift) % count) for k in range(count)]
        pieces.append(((me - shift) % count, lax.ppermute(entry(shift), axis, pairs)))
    return pieces


def by_source(pieces):
    ordered = []
    for source in range(len(pieces)):
        chosen = pieces[0][1]
        for index, piece in pieces[1:]:
            chosen = jnp.where(index == source, piece, chosen)
        ordered.append(chosen)
    return ordered


def exact_times(spec, table, values):
    high = table.astype(jnp.bfloat16)
    low = (table - high.astype(jnp.float32)).astype(jnp.bfloat16)
    return jnp.einsum(spec, high, values, preferred_element_type=jnp.float32) + jnp.einsum(
        spec, low, values, preferred_element_type=jnp.float32
    )


def gather_receptor(receptor):
    _, terms, kx_local, ky_local, kz = receptor.shape
    n_ref = lax.axis_size("ref")
    n_rot = lax.axis_size("rot")
    rows = ky_local // n_ref
    block = lax.dynamic_slice_in_dim(receptor, lax.axis_index("ref") * rows, rows, axis=3)
    mine = jnp.concatenate([block[0], block[1]], axis=-1).astype(jnp.bfloat16)
    mine = jnp.swapaxes(mine, 1, 2)
    along_rot = gather_by_shifts(mine, "rot")
    both = gather_by_shifts(along_rot, "ref")
    both = jnp.transpose(both, (2, 0, 3, 1, 4, 5))
    return both.reshape(terms, ky_local, n_rot * kx_local, 2 * kz)


def product_kernel(*refs):
    *spec_refs, rec_ref, out_ref = refs
    lanes = out_ref.shape[-1]
    half = lanes // 2
    total = None
    term = 0
    for spec_ref in spec_refs:
        for inner in range(spec_ref.shape[0]):
            spec = spec_ref[inner].astype(jnp.float32)
            rec = rec_ref[term].astype(jnp.float32)
            term += 1
            low = lax.broadcasted_iota(jnp.int32, (1, lanes), 1) < half
            rec_turned = pltpu.roll(rec, half, 1)
            rec_real = jnp.where(low, rec, rec_turned)
            rec_imag = jnp.where(low, rec_turned, -rec)
            part = rec_real * spec + rec_imag * pltpu.roll(spec, half, 1)
            total = part if total is None else total + part
    out_ref[...] = total


def correlate(spectra, receptor):
    rots, _, kx, ky, lanes = spectra[0].shape
    terms = receptor.shape[0]
    rows = kx * ky
    block = min(rows, 1024)
    specs = [part.reshape(rots, part.shape[1], rows, lanes) for part in spectra]
    rec = receptor.reshape(terms, rows, lanes)
    out = pl.pallas_call(
        product_kernel,
        grid=(rots, rows // block),
        in_specs=[
            pl.BlockSpec((None, part.shape[1], block, lanes), lambda r, i: (r, 0, i, 0))
            for part in specs
        ]
        + [pl.BlockSpec((terms, block, lanes), lambda r, i: (0, i, 0))],
        out_specs=pl.BlockSpec((None, block, lanes), lambda r, i: (r, i, 0)),
        out_shape=jax.ShapeDtypeStruct((rots, rows, lanes), jnp.float32),
        cost_estimate=pl.CostEstimate(
            flops=8 * rots * terms * rows * lanes,
            bytes_accessed=2 * (rots + 1) * terms * rows * lanes + 4 * rots * rows * lanes,
            transcendentals=0,
        ),
    )(*specs, rec)
    return out.reshape(rots, kx, ky, lanes)


def local(ligand, receptor, tile_list, tile_owner, refine_weight):
    rots, terms, x_local, ny, nz = ligand.shape
    length = nz
    n_sub = lax.axis_size("sub")
    y_local = ny // n_sub
    cos_table, sin_table = make_tables(length)
    pair = jnp.stack([cos_table, sin_table])

    chunks = 2 if terms % 2 == 0 else 1
    part_terms = terms // chunks
    pair_x = pair.reshape(2, length, n_sub, x_local)
    z_table = jnp.concatenate([cos_table, -sin_table], axis=1)
    spectra = []
    for chunk in range(chunks):
        part = ligand[:, chunk * part_terms:(chunk + 1) * part_terms]
        along_z = exact_times("zl,rtxyz->rtxyl", z_table, part)
        along_y = jnp.einsum("ejy,rtxyl->rtxejl", pair, along_z, precision=highest)
        sending = combine_call(
            along_y.reshape(-1, 2, ny, 2 * length), 1.0, -1.0, n_sub, jnp.bfloat16,
            lax.axis_index("sub"),
        ).reshape(n_sub, rots, part_terms, x_local, y_local, 2 * length)
        along_x = sum(
            exact_times("ekx,rtxjl->rtjekl", pair_x[:, :, source], piece)
            for source, piece in enumerate(by_source(exchange(sending, "sub", rotated=True)))
        )
        spectrum = combine_call(
            along_x.reshape(-1, 2, length, 2 * length), 1.0, -1.0, 1, jnp.bfloat16
        )
        spectra.append(spectrum.reshape(rots, part_terms, y_local, length, 2 * length))

    whole_receptor = gather_receptor(receptor)
    product = correlate(spectra, whole_receptor)

    back_x = jnp.einsum("exk,rjkl->xrejl", pair, product, precision=highest)
    back_x = combine_call(back_x.reshape(-1, 2, y_local, 2 * length), -1.0, 1.0, 1, jnp.float32)
    back_x = back_x.reshape(n_sub, x_local, rots, y_local, 2 * length)
    pair_y = pair.reshape(2, length, n_sub, y_local)
    back_y = sum(
        jnp.einsum("eyj,xrjl->rxeyl", pair_y[:, :, source], piece, precision=highest)
        for source, piece in enumerate(by_source(exchange(back_x, "sub")))
    )
    back_y = combine_call(back_y.reshape(-1, 2, ny, 2 * length), -1.0, 1.0, 1, jnp.float32)
    back_y = back_y.reshape(rots, x_local, ny, 2 * length)
    last_table = jnp.concatenate([cos_table, -sin_table], axis=0)
    scores = jnp.einsum("rxyl,lz->rxyz", back_y, last_table, precision=highest) / float(length**3)

    tile_cells = 8 * length
    tile_rows = scores.reshape(-1, tile_cells)
    listing = tile_list.reshape(-1)
    owners = tile_owner.reshape(-1)
    listed = listing.shape[0]
    chosen = tile_rows[listing]
    owner_count = lax.axis_size(("rot", "ref"))
    order = jnp.arange(listed, dtype=jnp.int32)
    earlier = (owners[:, None] == owners[None, :]) & (order[None, :] < order[:, None])
    slot = jnp.sum(earlier.astype(jnp.int32), axis=1)
    target = owners * CAP + slot
    placing = (jnp.arange(owner_count * CAP, dtype=jnp.int32)[:, None] == target[None, :]).astype(
        jnp.float32
    )
    done = jnp.dot(chosen, refine_weight, precision=highest)
    packed = jnp.dot(placing, done, precision=highest).reshape(owner_count, CAP, tile_cells)
    refined = lax.all_to_all(packed, ("rot", "ref"), split_axis=0, concat_axis=0, tiled=True)
    return (scores, refined.reshape(1, 1, owner_count, CAP, tile_cells))


def solution(mesh):
    in_specs = (
        P(("grp", "rot", "ref"), None, "sub", None, None),
        P("grp", None, "rot", "sub", None),
        P(("grp", "rot"), "sub", "ref", None),
        P(("grp", "rot"), "sub", "ref", None, None),
        P(),
    )
    out_specs = (
        P(("grp", "rot", "ref"), "sub", None, None),
        P(("grp", "rot", "ref"), "sub", None, None, None),
    )
    return jax.shard_map(local, mesh=mesh, in_specs=in_specs, out_specs=out_specs, check_vma=False)
```

```python
import functools
import math

import jax
import jax.numpy as jnp
from jax import lax
from jax.experimental import pallas as pl
from jax.experimental.pallas import tpu as pltpu
from jax.sharding import PartitionSpec as P

CAP = 2


highest = lax.Precision.HIGH


def make_tables(length):
    counter = jnp.arange(length, dtype=jnp.int32)
    phases = counter[:, None] * counter[None, :] % length
    angles = phases.astype(jnp.float32) * (2.0 * math.pi / length)
    return (jnp.cos(angles), jnp.sin(angles))


def combine_kernel(me_ref, in_ref, out_ref, *, first, second):
    batch, _, rows, lanes = in_ref.shape
    split = out_ref.shape[0]
    part = rows // split
    half = lanes // 2
    low = lax.broadcasted_iota(jnp.int32, (1, lanes), 1) < half
    signs = jnp.where(low, first, second).astype(jnp.float32)
    me = me_ref[0]
    for piece in range(split):
        start = pl.multiple_of(((me + piece) % split) * part, 8)
        cos_part = in_ref[:, 0, pl.ds(start, part), :].reshape(batch * part, lanes)
        sin_part = in_ref[:, 1, pl.ds(start, part), :].reshape(batch * part, lanes)
        result = cos_part + pltpu.roll(sin_part, half, 1) * signs
        out_ref[piece] = result.reshape(batch, part, lanes).astype(out_ref.dtype)


def combine_call(stacked, first, second, split, dtype, me=0):
    batch, _, rows, lanes = stacked.shape
    block = max(b for b in range(1, 33) if batch % b == 0)
    part = rows // split
    return pl.pallas_call(
        functools.partial(combine_kernel, first=first, second=second),
        grid_spec=pltpu.PrefetchScalarGridSpec(
            num_scalar_prefetch=1,
            grid=(batch // block,),
            in_specs=[pl.BlockSpec((block, 2, rows, lanes), lambda i, me: (i, 0, 0, 0))],
            out_specs=pl.BlockSpec((split, block, part, lanes), lambda i, me: (0, i, 0, 0)),
        ),
        out_shape=jax.ShapeDtypeStruct((split, batch, part, lanes), dtype),
        cost_estimate=pl.CostEstimate(
            flops=3 * batch * rows * lanes,
            bytes_accessed=(8 + jnp.dtype(dtype).itemsize) * batch * rows * lanes,
            transcendentals=0,
        ),
    )(jnp.reshape(jnp.asarray(me, jnp.int32), (1,)), stacked)


def gather_by_shifts(piece, axis):
    count = lax.axis_size(axis)
    me = lax.axis_index(axis)
    pieces = [piece]
    for shift in range(1, count):
        pairs = [(k, (k + shift) % count) for k in range(count)]
        pieces.append(lax.ppermute(piece, axis, pairs))
    doubled = jnp.stack(pieces[::-1] * 2)
    return lax.dynamic_slice_in_dim(doubled, (count - 1 - me) % count, count, axis=0)


def exchange(sending, axis, rotated=False):
    count = lax.axis_size(axis)
    me = lax.axis_index(axis)

    def entry(shift):
        if rotated:
            return sending[shift]
        return lax.dynamic_index_in_dim(sending, (me + shift) % count, axis=0, keepdims=False)

    pieces = [(me, entry(0))]
    for shift in range(1, count):
        pairs = [(k, (k + shift) % count) for k in range(count)]
        pieces.append(((me - shift) % count, lax.ppermute(entry(shift), axis, pairs)))
    return pieces


def by_source(pieces):
    ordered = []
    for source in range(len(pieces)):
        chosen = pieces[0][1]
        for index, piece in pieces[1:]:
            chosen = jnp.where(index == source, piece, chosen)
        ordered.append(chosen)
    return ordered


def gather_receptor(receptor):
    _, terms, kx_local, ky_local, kz = receptor.shape
    n_ref = lax.axis_size("ref")
    n_rot = lax.axis_size("rot")
    rows = ky_local // n_ref
    block = lax.dynamic_slice_in_dim(receptor, lax.axis_index("ref") * rows, rows, axis=3)
    mine = jnp.concatenate([block[0], block[1]], axis=-1).astype(jnp.bfloat16)
    mine = jnp.swapaxes(mine, 1, 2)
    along_rot = gather_by_shifts(mine, "rot")
    both = gather_by_shifts(along_rot, "ref")
    both = jnp.transpose(both, (2, 0, 3, 1, 4, 5))
    return both.reshape(terms, ky_local, n_rot * kx_local, 2 * kz)


def product_kernel(*refs):
    *spec_refs, rec_ref, out_ref = refs
    lanes = out_ref.shape[-1]
    half = lanes // 2
    total = None
    term = 0
    for spec_ref in spec_refs:
        for inner in range(spec_ref.shape[0]):
            spec = spec_ref[inner].astype(jnp.float32)
            rec = rec_ref[term].astype(jnp.float32)
            term += 1
            low = lax.broadcasted_iota(jnp.int32, (1, lanes), 1) < half
            rec_turned = pltpu.roll(rec, half, 1)
            rec_real = jnp.where(low, rec, rec_turned)
            rec_imag = jnp.where(low, rec_turned, -rec)
            part = rec_real * spec + rec_imag * pltpu.roll(spec, half, 1)
            total = part if total is None else total + part
    out_ref[...] = total


def correlate(spectra, receptor):
    rots, _, kx, ky, lanes = spectra[0].shape
    terms = receptor.shape[0]
    rows = kx * ky
    block = min(rows, 1024)
    specs = [part.reshape(rots, part.shape[1], rows, lanes) for part in spectra]
    rec = receptor.reshape(terms, rows, lanes)
    out = pl.pallas_call(
        product_kernel,
        grid=(rots, rows // block),
        in_specs=[
            pl.BlockSpec((None, part.shape[1], block, lanes), lambda r, i: (r, 0, i, 0))
            for part in specs
        ]
        + [pl.BlockSpec((terms, block, lanes), lambda r, i: (0, i, 0))],
        out_specs=pl.BlockSpec((None, block, lanes), lambda r, i: (r, i, 0)),
        out_shape=jax.ShapeDtypeStruct((rots, rows, lanes), jnp.float32),
        cost_estimate=pl.CostEstimate(
            flops=8 * rots * terms * rows * lanes,
            bytes_accessed=2 * (rots + 1) * terms * rows * lanes + 4 * rots * rows * lanes,
            transcendentals=0,
        ),
    )(*specs, rec)
    return out.reshape(rots, kx, ky, lanes)


def local(ligand, receptor, tile_list, tile_owner, refine_weight):
    rots, terms, x_local, ny, nz = ligand.shape
    length = nz
    n_sub = lax.axis_size("sub")
    y_local = ny // n_sub
    cos_table, sin_table = make_tables(length)
    pair = jnp.stack([cos_table, sin_table])

    chunks = 4 if terms % 4 == 0 else 1
    part_terms = terms // chunks
    pair_x = pair.reshape(2, length, n_sub, x_local)
    z_table = jnp.concatenate([cos_table, -sin_table], axis=1)
    values = ligand.astype(jnp.float32)
    spectra = []
    for chunk in range(chunks):
        part = values[:, chunk * part_terms:(chunk + 1) * part_terms]
        along_z = jnp.einsum("rtxyz,zl->rtxyl", part, z_table, precision=highest)
        along_y = jnp.einsum("ejy,rtxyl->rtxejl", pair, along_z, precision=highest)
        sending = combine_call(
            along_y.reshape(-1, 2, ny, 2 * length), 1.0, -1.0, n_sub, jnp.bfloat16,
            lax.axis_index("sub"),
        ).reshape(n_sub, rots, part_terms, x_local, y_local, 2 * length)
        along_x = sum(
            jnp.einsum(
                "ekx,rtxjl->rtjekl", pair_x[:, :, source], piece.astype(jnp.float32),
                precision=highest,
            )
            for source, piece in enumerate(by_source(exchange(sending, "sub", rotated=True)))
        )
        spectrum = combine_call(
            along_x.reshape(-1, 2, length, 2 * length), 1.0, -1.0, 1, jnp.bfloat16
        )
        spectra.append(spectrum.reshape(rots, part_terms, y_local, length, 2 * length))

    whole_receptor = gather_receptor(receptor)
    product = correlate(spectra, whole_receptor)

    back_x = jnp.einsum("exk,rjkl->xrejl", pair, product, precision=highest)
    back_x = combine_call(back_x.reshape(-1, 2, y_local, 2 * length), -1.0, 1.0, 1, jnp.float32)
    back_x = back_x.reshape(n_sub, x_local, rots, y_local, 2 * length)
    pair_y = pair.reshape(2, length, n_sub, y_local)
    back_y = sum(
        jnp.einsum("eyj,xrjl->rxeyl", pair_y[:, :, source], piece, precision=highest)
        for source, piece in enumerate(by_source(exchange(back_x, "sub")))
    )
    back_y = combine_call(back_y.reshape(-1, 2, ny, 2 * length), -1.0, 1.0, 1, jnp.float32)
    back_y = back_y.reshape(rots, x_local, ny, 2 * length)
    last_table = jnp.concatenate([cos_table, -sin_table], axis=0)
    scores = jnp.einsum("rxyl,lz->rxyz", back_y, last_table, precision=highest) / float(length**3)

    tile_cells = 8 * length
    tile_rows = scores.reshape(-1, tile_cells)
    listing = tile_list.reshape(-1)
    owners = tile_owner.reshape(-1)
    listed = listing.shape[0]
    chosen = tile_rows[listing]
    owner_count = lax.axis_size(("rot", "ref"))
    order = jnp.arange(listed, dtype=jnp.int32)
    earlier = (owners[:, None] == owners[None, :]) & (order[None, :] < order[:, None])
    slot = jnp.sum(earlier.astype(jnp.int32), axis=1)
    target = owners * CAP + slot
    placing = (jnp.arange(owner_count * CAP, dtype=jnp.int32)[:, None] == target[None, :]).astype(
        jnp.float32
    )
    done = jnp.dot(chosen, refine_weight, precision=highest)
    packed = jnp.dot(placing, done, precision=highest).reshape(owner_count, CAP, tile_cells)
    refined = lax.all_to_all(packed, ("rot", "ref"), split_axis=0, concat_axis=0, tiled=True)
    return (scores, refined.reshape(1, 1, owner_count, CAP, tile_cells))


def solution(mesh):
    in_specs = (
        P(("grp", "rot", "ref"), None, "sub", None, None),
        P("grp", None, "rot", "sub", None),
        P(("grp", "rot"), "sub", "ref", None),
        P(("grp", "rot"), "sub", "ref", None, None),
        P(),
    )
    out_specs = (
        P(("grp", "rot", "ref"), "sub", None, None),
        P(("grp", "rot", "ref"), "sub", None, None, None),
    )
    return jax.shard_map(local, mesh=mesh, in_specs=in_specs, out_specs=out_specs, check_vma=False)
```

```python
import functools
import math

import jax
import jax.numpy as jnp
from jax import lax
from jax.experimental import pallas as pl
from jax.experimental.pallas import tpu as pltpu
from jax.sharding import PartitionSpec as P

CAP = 2


highest = lax.Precision.HIGH


def make_tables(length):
    counter = jnp.arange(length, dtype=jnp.int32)
    phases = counter[:, None] * counter[None, :] % length
    angles = phases.astype(jnp.float32) * (2.0 * math.pi / length)
    return (jnp.cos(angles), jnp.sin(angles))


def combine_kernel(me_ref, in_ref, out_ref, *, first, second):
    batch, _, rows, lanes = in_ref.shape
    split = out_ref.shape[0]
    part = rows // split
    half = lanes // 2
    low = lax.broadcasted_iota(jnp.int32, (1, lanes), 1) < half
    signs = jnp.where(low, first, second).astype(jnp.float32)
    me = me_ref[0]
    for piece in range(split):
        start = pl.multiple_of(((me + piece) % split) * part, 8)
        cos_part = in_ref[:, 0, pl.ds(start, part), :].reshape(batch * part, lanes)
        sin_part = in_ref[:, 1, pl.ds(start, part), :].reshape(batch * part, lanes)
        result = cos_part + pltpu.roll(sin_part, half, 1) * signs
        out_ref[piece] = result.reshape(batch, part, lanes).astype(out_ref.dtype)


def combine_call(stacked, first, second, split, dtype, me=0):
    batch, _, rows, lanes = stacked.shape
    block = max(b for b in range(1, min(32, max(batch // 2, 1)) + 1) if batch % b == 0)
    part = rows // split
    return pl.pallas_call(
        functools.partial(combine_kernel, first=first, second=second),
        grid_spec=pltpu.PrefetchScalarGridSpec(
            num_scalar_prefetch=1,
            grid=(batch // block,),
            in_specs=[pl.BlockSpec((block, 2, rows, lanes), lambda i, me: (i, 0, 0, 0))],
            out_specs=pl.BlockSpec((split, block, part, lanes), lambda i, me: (0, i, 0, 0)),
        ),
        out_shape=jax.ShapeDtypeStruct((split, batch, part, lanes), dtype),
        cost_estimate=pl.CostEstimate(
            flops=3 * batch * rows * lanes,
            bytes_accessed=(8 + jnp.dtype(dtype).itemsize) * batch * rows * lanes,
            transcendentals=0,
        ),
    )(jnp.reshape(jnp.asarray(me, jnp.int32), (1,)), stacked)


def gather_by_shifts(piece, axis):
    count = lax.axis_size(axis)
    me = lax.axis_index(axis)
    pieces = [piece]
    for shift in range(1, count):
        pairs = [(k, (k + shift) % count) for k in range(count)]
        pieces.append(lax.ppermute(piece, axis, pairs))
    doubled = jnp.stack(pieces[::-1] * 2)
    return lax.dynamic_slice_in_dim(doubled, (count - 1 - me) % count, count, axis=0)


def exchange(sending, axis, rotated=False):
    count = lax.axis_size(axis)
    me = lax.axis_index(axis)

    def entry(shift):
        if rotated:
            return sending[shift]
        return lax.dynamic_index_in_dim(sending, (me + shift) % count, axis=0, keepdims=False)

    pieces = [(me, entry(0))]
    for shift in range(1, count):
        pairs = [(k, (k + shift) % count) for k in range(count)]
        pieces.append(((me - shift) % count, lax.ppermute(entry(shift), axis, pairs)))
    return pieces


def by_source(pieces):
    ordered = []
    for source in range(len(pieces)):
        chosen = pieces[0][1]
        for index, piece in pieces[1:]:
            chosen = jnp.where(index == source, piece, chosen)
        ordered.append(chosen)
    return ordered


def gather_receptor(receptor):
    _, terms, kx_local, ky_local, kz = receptor.shape
    n_ref = lax.axis_size("ref")
    n_rot = lax.axis_size("rot")
    rows = ky_local // n_ref
    block = lax.dynamic_slice_in_dim(receptor, lax.axis_index("ref") * rows, rows, axis=3)
    mine = jnp.concatenate([block[0], block[1]], axis=-1).astype(jnp.bfloat16)
    mine = jnp.swapaxes(mine, 1, 2)
    along_rot = gather_by_shifts(mine, "rot")
    both = gather_by_shifts(along_rot, "ref")
    both = jnp.transpose(both, (2, 0, 3, 1, 4, 5))
    return both.reshape(terms, ky_local, n_rot * kx_local, 2 * kz)


def product_kernel(*refs):
    *spec_refs, rec_ref, out_ref = refs
    lanes = out_ref.shape[-1]
    half = lanes // 2
    total = None
    term = 0
    for spec_ref in spec_refs:
        for inner in range(spec_ref.shape[0]):
            spec = spec_ref[inner].astype(jnp.float32)
            rec = rec_ref[term].astype(jnp.float32)
            term += 1
            low = lax.broadcasted_iota(jnp.int32, (1, lanes), 1) < half
            rec_turned = pltpu.roll(rec, half, 1)
            rec_real = jnp.where(low, rec, rec_turned)
            rec_imag = jnp.where(low, rec_turned, -rec)
            part = rec_real * spec + rec_imag * pltpu.roll(spec, half, 1)
            total = part if total is None else total + part
    out_ref[...] = total


def correlate(spectra, receptor):
    rots, _, kx, ky, lanes = spectra[0].shape
    terms = receptor.shape[0]
    rows = kx * ky
    block = min(rows, 1024)
    specs = [part.reshape(rots, part.shape[1], rows, lanes) for part in spectra]
    rec = receptor.reshape(terms, rows, lanes)
    out = pl.pallas_call(
        product_kernel,
        grid=(rots, rows // block),
        in_specs=[
            pl.BlockSpec((None, part.shape[1], block, lanes), lambda r, i: (r, 0, i, 0))
            for part in specs
        ]
        + [pl.BlockSpec((terms, block, lanes), lambda r, i: (0, i, 0))],
        out_specs=pl.BlockSpec((None, block, lanes), lambda r, i: (r, i, 0)),
        out_shape=jax.ShapeDtypeStruct((rots, rows, lanes), jnp.float32),
        cost_estimate=pl.CostEstimate(
            flops=8 * rots * terms * rows * lanes,
            bytes_accessed=2 * (rots + 1) * terms * rows * lanes + 4 * rots * rows * lanes,
            transcendentals=0,
        ),
    )(*specs, rec)
    return out.reshape(rots, kx, ky, lanes)


def local(ligand, receptor, tile_list, tile_owner, refine_weight):
    rots, terms, x_local, ny, nz = ligand.shape
    length = nz
    n_sub = lax.axis_size("sub")
    y_local = ny // n_sub
    cos_table, sin_table = make_tables(length)
    pair = jnp.stack([cos_table, sin_table])

    chunks = 2 if terms % 2 == 0 else 1
    part_terms = terms // chunks
    pair_x = pair.reshape(2, length, n_sub, x_local)
    z_table = jnp.concatenate([cos_table, -sin_table], axis=1)
    values = ligand.astype(jnp.float32)
    spectra = []
    for chunk in range(chunks):
        part = values[:, chunk * part_terms:(chunk + 1) * part_terms]
        along_z = jnp.einsum("rtxyz,zl->rtxyl", part, z_table, precision=highest)
        along_y = jnp.einsum("ejy,rtxyl->rtxejl", pair, along_z, precision=highest)
        sending = combine_call(
            along_y.reshape(-1, 2, ny, 2 * length), 1.0, -1.0, n_sub, jnp.bfloat16,
            lax.axis_index("sub"),
        ).reshape(n_sub, rots, part_terms, x_local, y_local, 2 * length)
        along_x = sum(
            jnp.einsum(
                "ekx,rtxjl->rtjekl", pair_x[:, :, source], piece.astype(jnp.float32),
                precision=highest,
            )
            for source, piece in enumerate(by_source(exchange(sending, "sub", rotated=True)))
        )
        spectrum = combine_call(
            along_x.reshape(-1, 2, length, 2 * length), 1.0, -1.0, 1, jnp.bfloat16
        )
        spectra.append(spectrum.reshape(rots, part_terms, y_local, length, 2 * length))

    whole_receptor = gather_receptor(receptor)
    product = correlate(spectra, whole_receptor)

    back_x = jnp.einsum("exk,rjkl->xrejl", pair, product, precision=highest)
    back_x = combine_call(back_x.reshape(-1, 2, y_local, 2 * length), -1.0, 1.0, 1, jnp.float32)
    back_x = back_x.reshape(n_sub, x_local, rots, y_local, 2 * length)
    pair_y = pair.reshape(2, length, n_sub, y_local)
    back_y = sum(
        jnp.einsum("eyj,xrjl->rxeyl", pair_y[:, :, source], piece, precision=highest)
        for source, piece in enumerate(by_source(exchange(back_x, "sub")))
    )
    back_y = combine_call(back_y.reshape(-1, 2, ny, 2 * length), -1.0, 1.0, 1, jnp.float32)
    back_y = back_y.reshape(rots, x_local, ny, 2 * length)
    last_table = jnp.concatenate([cos_table, -sin_table], axis=0)
    scores = jnp.einsum("rxyl,lz->rxyz", back_y, last_table, precision=highest) / float(length**3)

    tile_cells = 8 * length
    tile_rows = scores.reshape(-1, tile_cells)
    listing = tile_list.reshape(-1)
    owners = tile_owner.reshape(-1)
    listed = listing.shape[0]
    chosen = tile_rows[listing]
    owner_count = lax.axis_size(("rot", "ref"))
    order = jnp.arange(listed, dtype=jnp.int32)
    earlier = (owners[:, None] == owners[None, :]) & (order[None, :] < order[:, None])
    slot = jnp.sum(earlier.astype(jnp.int32), axis=1)
    target = owners * CAP + slot
    placing = (jnp.arange(owner_count * CAP, dtype=jnp.int32)[:, None] == target[None, :]).astype(
        jnp.float32
    )
    done = jnp.dot(chosen, refine_weight, precision=highest)
    packed = jnp.dot(placing, done, precision=highest).reshape(owner_count, CAP, tile_cells)
    refined = lax.all_to_all(packed, ("rot", "ref"), split_axis=0, concat_axis=0, tiled=True)
    return (scores, refined.reshape(1, 1, owner_count, CAP, tile_cells))


def solution(mesh):
    in_specs = (
        P(("grp", "rot", "ref"), None, "sub", None, None),
        P("grp", None, "rot", "sub", None),
        P(("grp", "rot"), "sub", "ref", None),
        P(("grp", "rot"), "sub", "ref", None, None),
        P(),
    )
    out_specs = (
        P(("grp", "rot", "ref"), "sub", None, None),
        P(("grp", "rot", "ref"), "sub", None, None, None),
    )
    return jax.shard_map(local, mesh=mesh, in_specs=in_specs, out_specs=out_specs, check_vma=False)
```

```python
import functools
import math

import jax
import jax.numpy as jnp
from jax import lax
from jax.experimental import pallas as pl
from jax.experimental.pallas import tpu as pltpu
from jax.sharding import PartitionSpec as P

CAP = 2


highest = lax.Precision.HIGH


def make_tables(length):
    counter = jnp.arange(length, dtype=jnp.int32)
    phases = counter[:, None] * counter[None, :] % length
    angles = phases.astype(jnp.float32) * (2.0 * math.pi / length)
    return (jnp.cos(angles), jnp.sin(angles))


def combine_kernel(me_ref, in_ref, out_ref, *, first, second):
    batch, _, rows, lanes = in_ref.shape
    split = out_ref.shape[0]
    part = rows // split
    half = lanes // 2
    low = lax.broadcasted_iota(jnp.int32, (1, lanes), 1) < half
    signs = jnp.where(low, first, second).astype(jnp.float32)
    me = me_ref[0]
    for piece in range(split):
        start = pl.multiple_of(((me + piece) % split) * part, 8)
        cos_part = in_ref[:, 0, pl.ds(start, part), :].reshape(batch * part, lanes)
        sin_part = in_ref[:, 1, pl.ds(start, part), :].reshape(batch * part, lanes)
        result = cos_part + pltpu.roll(sin_part, half, 1) * signs
        out_ref[piece] = result.reshape(batch, part, lanes).astype(out_ref.dtype)


def combine_call(stacked, first, second, split, dtype, me=0):
    batch, _, rows, lanes = stacked.shape
    block = max(b for b in range(1, min(16, max(batch // 2, 1)) + 1) if batch % b == 0)
    part = rows // split
    return pl.pallas_call(
        functools.partial(combine_kernel, first=first, second=second),
        grid_spec=pltpu.PrefetchScalarGridSpec(
            num_scalar_prefetch=1,
            grid=(batch // block,),
            in_specs=[pl.BlockSpec((block, 2, rows, lanes), lambda i, me: (i, 0, 0, 0))],
            out_specs=pl.BlockSpec((split, block, part, lanes), lambda i, me: (0, i, 0, 0)),
        ),
        out_shape=jax.ShapeDtypeStruct((split, batch, part, lanes), dtype),
        cost_estimate=pl.CostEstimate(
            flops=3 * batch * rows * lanes,
            bytes_accessed=(8 + jnp.dtype(dtype).itemsize) * batch * rows * lanes,
            transcendentals=0,
        ),
    )(jnp.reshape(jnp.asarray(me, jnp.int32), (1,)), stacked)


def gather_by_shifts(piece, axis):
    count = lax.axis_size(axis)
    me = lax.axis_index(axis)
    pieces = [piece]
    for shift in range(1, count):
        pairs = [(k, (k + shift) % count) for k in range(count)]
        pieces.append(lax.ppermute(piece, axis, pairs))
    doubled = jnp.stack(pieces[::-1] * 2)
    return lax.dynamic_slice_in_dim(doubled, (count - 1 - me) % count, count, axis=0)


def exchange(sending, axis, rotated=False):
    count = lax.axis_size(axis)
    me = lax.axis_index(axis)

    def entry(shift):
        if rotated:
            return sending[shift]
        return lax.dynamic_index_in_dim(sending, (me + shift) % count, axis=0, keepdims=False)

    pieces = [(me, entry(0))]
    for shift in range(1, count):
        pairs = [(k, (k + shift) % count) for k in range(count)]
        pieces.append(((me - shift) % count, lax.ppermute(entry(shift), axis, pairs)))
    return pieces


def by_source(pieces):
    ordered = []
    for source in range(len(pieces)):
        chosen = pieces[0][1]
        for index, piece in pieces[1:]:
            chosen = jnp.where(index == source, piece, chosen)
        ordered.append(chosen)
    return ordered


def gather_receptor(receptor):
    _, terms, kx_local, ky_local, kz = receptor.shape
    n_ref = lax.axis_size("ref")
    n_rot = lax.axis_size("rot")
    rows = ky_local // n_ref
    block = lax.dynamic_slice_in_dim(receptor, lax.axis_index("ref") * rows, rows, axis=3)
    mine = jnp.concatenate([block[0], block[1]], axis=-1).astype(jnp.bfloat16)
    mine = jnp.swapaxes(mine, 1, 2)
    along_rot = gather_by_shifts(mine, "rot")
    both = gather_by_shifts(along_rot, "ref")
    both = jnp.transpose(both, (2, 0, 3, 1, 4, 5))
    return both.reshape(terms, ky_local, n_rot * kx_local, 2 * kz)


def product_kernel(*refs):
    *spec_refs, rec_ref, out_ref = refs
    lanes = out_ref.shape[-1]
    half = lanes // 2
    total = None
    term = 0
    for spec_ref in spec_refs:
        for inner in range(spec_ref.shape[0]):
            spec = spec_ref[inner].astype(jnp.float32)
            rec = rec_ref[term].astype(jnp.float32)
            term += 1
            low = lax.broadcasted_iota(jnp.int32, (1, lanes), 1) < half
            rec_turned = pltpu.roll(rec, half, 1)
            rec_real = jnp.where(low, rec, rec_turned)
            rec_imag = jnp.where(low, rec_turned, -rec)
            part = rec_real * spec + rec_imag * pltpu.roll(spec, half, 1)
            total = part if total is None else total + part
    out_ref[...] = total


def correlate(spectra, receptor):
    rots, _, kx, ky, lanes = spectra[0].shape
    terms = receptor.shape[0]
    rows = kx * ky
    block = min(rows, 1024)
    specs = [part.reshape(rots, part.shape[1], rows, lanes) for part in spectra]
    rec = receptor.reshape(terms, rows, lanes)
    out = pl.pallas_call(
        product_kernel,
        grid=(rots, rows // block),
        in_specs=[
            pl.BlockSpec((None, part.shape[1], block, lanes), lambda r, i: (r, 0, i, 0))
            for part in specs
        ]
        + [pl.BlockSpec((terms, block, lanes), lambda r, i: (0, i, 0))],
        out_specs=pl.BlockSpec((None, block, lanes), lambda r, i: (r, i, 0)),
        out_shape=jax.ShapeDtypeStruct((rots, rows, lanes), jnp.float32),
        cost_estimate=pl.CostEstimate(
            flops=8 * rots * terms * rows * lanes,
            bytes_accessed=2 * (rots + 1) * terms * rows * lanes + 4 * rots * rows * lanes,
            transcendentals=0,
        ),
    )(*specs, rec)
    return out.reshape(rots, kx, ky, lanes)


def local(ligand, receptor, tile_list, tile_owner, refine_weight):
    rots, terms, x_local, ny, nz = ligand.shape
    length = nz
    n_sub = lax.axis_size("sub")
    y_local = ny // n_sub
    cos_table, sin_table = make_tables(length)
    pair = jnp.stack([cos_table, sin_table])

    chunks = 2 if terms % 2 == 0 else 1
    part_terms = terms // chunks
    pair_x = pair.reshape(2, length, n_sub, x_local)
    z_table = jnp.concatenate([cos_table, -sin_table], axis=1)
    values = ligand.astype(jnp.float32)
    spectra = []
    for chunk in range(chunks):
        part = values[:, chunk * part_terms:(chunk + 1) * part_terms]
        along_z = jnp.einsum("rtxyz,zl->rtxyl", part, z_table, precision=highest)
        along_y = jnp.einsum("ejy,rtxyl->rtxejl", pair, along_z, precision=highest)
        sending = combine_call(
            along_y.reshape(-1, 2, ny, 2 * length), 1.0, -1.0, n_sub, jnp.bfloat16,
            lax.axis_index("sub"),
        ).reshape(n_sub, rots, part_terms, x_local, y_local, 2 * length)
        along_x = sum(
            jnp.einsum(
                "ekx,rtxjl->rtjekl", pair_x[:, :, source], piece.astype(jnp.float32),
                precision=highest,
            )
            for source, piece in enumerate(by_source(exchange(sending, "sub", rotated=True)))
        )
        spectrum = combine_call(
            along_x.reshape(-1, 2, length, 2 * length), 1.0, -1.0, 1, jnp.bfloat16
        )
        spectra.append(spectrum.reshape(rots, part_terms, y_local, length, 2 * length))

    whole_receptor = gather_receptor(receptor)
    product = correlate(spectra, whole_receptor)

    back_x = jnp.einsum("exk,rjkl->xrejl", pair, product, precision=highest)
    back_x = combine_call(back_x.reshape(-1, 2, y_local, 2 * length), -1.0, 1.0, 1, jnp.float32)
    back_x = back_x.reshape(n_sub, x_local, rots, y_local, 2 * length)
    pair_y = pair.reshape(2, length, n_sub, y_local)
    back_y = sum(
        jnp.einsum("eyj,xrjl->rxeyl", pair_y[:, :, source], piece, precision=highest)
        for source, piece in enumerate(by_source(exchange(back_x, "sub")))
    )
    back_y = combine_call(back_y.reshape(-1, 2, ny, 2 * length), -1.0, 1.0, 1, jnp.float32)
    back_y = back_y.reshape(rots, x_local, ny, 2 * length)
    last_table = jnp.concatenate([cos_table, -sin_table], axis=0)
    scores = jnp.einsum("rxyl,lz->rxyz", back_y, last_table, precision=highest) / float(length**3)

    tile_cells = 8 * length
    tile_rows = scores.reshape(-1, tile_cells)
    listing = tile_list.reshape(-1)
    owners = tile_owner.reshape(-1)
    listed = listing.shape[0]
    chosen = tile_rows[listing]
    owner_count = lax.axis_size(("rot", "ref"))
    order = jnp.arange(listed, dtype=jnp.int32)
    earlier = (owners[:, None] == owners[None, :]) & (order[None, :] < order[:, None])
    slot = jnp.sum(earlier.astype(jnp.int32), axis=1)
    target = owners * CAP + slot
    placing = (jnp.arange(owner_count * CAP, dtype=jnp.int32)[:, None] == target[None, :]).astype(
        jnp.float32
    )
    done = jnp.dot(chosen, refine_weight, precision=highest)
    packed = jnp.dot(placing, done, precision=highest).reshape(owner_count, CAP, tile_cells)
    refined = lax.all_to_all(packed, ("rot", "ref"), split_axis=0, concat_axis=0, tiled=True)
    return (scores, refined.reshape(1, 1, owner_count, CAP, tile_cells))


def solution(mesh):
    in_specs = (
        P(("grp", "rot", "ref"), None, "sub", None, None),
        P("grp", None, "rot", "sub", None),
        P(("grp", "rot"), "sub", "ref", None),
        P(("grp", "rot"), "sub", "ref", None, None),
        P(),
    )
    out_specs = (
        P(("grp", "rot", "ref"), "sub", None, None),
        P(("grp", "rot", "ref"), "sub", None, None, None),
    )
    return jax.shard_map(local, mesh=mesh, in_specs=in_specs, out_specs=out_specs, check_vma=False)
```

```python
import functools
import math

import jax
import jax.numpy as jnp
from jax import lax
from jax.experimental import pallas as pl
from jax.experimental.pallas import tpu as pltpu
from jax.sharding import PartitionSpec as P

CAP = 2


highest = lax.Precision.HIGH


def make_tables(length):
    counter = jnp.arange(length, dtype=jnp.int32)
    phases = counter[:, None] * counter[None, :] % length
    angles = phases.astype(jnp.float32) * (2.0 * math.pi / length)
    return (jnp.cos(angles), jnp.sin(angles))


def combine_kernel(me_ref, in_ref, out_ref, *, first, second):
    batch, _, rows, lanes = in_ref.shape
    split = out_ref.shape[0]
    part = rows // split
    half = lanes // 2
    low = lax.broadcasted_iota(jnp.int32, (1, lanes), 1) < half
    signs = jnp.where(low, first, second).astype(jnp.float32)
    me = me_ref[0]
    for piece in range(split):
        start = pl.multiple_of(((me + piece) % split) * part, 8)
        cos_part = in_ref[:, 0, pl.ds(start, part), :].reshape(batch * part, lanes)
        sin_part = in_ref[:, 1, pl.ds(start, part), :].reshape(batch * part, lanes)
        result = cos_part + pltpu.roll(sin_part, half, 1) * signs
        out_ref[piece] = result.reshape(batch, part, lanes).astype(out_ref.dtype)


def combine_call(stacked, first, second, split, dtype, me=0):
    batch, _, rows, lanes = stacked.shape
    block = max(b for b in range(1, min(32, max(batch // 2, 1)) + 1) if batch % b == 0)
    part = rows // split
    return pl.pallas_call(
        functools.partial(combine_kernel, first=first, second=second),
        grid_spec=pltpu.PrefetchScalarGridSpec(
            num_scalar_prefetch=1,
            grid=(batch // block,),
            in_specs=[pl.BlockSpec((block, 2, rows, lanes), lambda i, me: (i, 0, 0, 0))],
            out_specs=pl.BlockSpec((split, block, part, lanes), lambda i, me: (0, i, 0, 0)),
        ),
        out_shape=jax.ShapeDtypeStruct((split, batch, part, lanes), dtype),
        cost_estimate=pl.CostEstimate(
            flops=3 * batch * rows * lanes,
            bytes_accessed=(8 + jnp.dtype(dtype).itemsize) * batch * rows * lanes,
            transcendentals=0,
        ),
    )(jnp.reshape(jnp.asarray(me, jnp.int32), (1,)), stacked)


def gather_by_shifts(piece, axis):
    count = lax.axis_size(axis)
    me = lax.axis_index(axis)
    pieces = [piece]
    for shift in range(1, count):
        pairs = [(k, (k + shift) % count) for k in range(count)]
        pieces.append(lax.ppermute(piece, axis, pairs))
    doubled = jnp.stack(pieces[::-1] * 2)
    return lax.dynamic_slice_in_dim(doubled, (count - 1 - me) % count, count, axis=0)


def exchange(sending, axis, rotated=False):
    count = lax.axis_size(axis)
    me = lax.axis_index(axis)

    def entry(shift):
        if rotated:
            return sending[shift]
        return lax.dynamic_index_in_dim(sending, (me + shift) % count, axis=0, keepdims=False)

    pieces = [(me, entry(0))]
    for shift in range(1, count):
        pairs = [(k, (k + shift) % count) for k in range(count)]
        pieces.append(((me - shift) % count, lax.ppermute(entry(shift), axis, pairs)))
    return pieces


def by_source(pieces):
    ordered = []
    for source in range(len(pieces)):
        chosen = pieces[0][1]
        for index, piece in pieces[1:]:
            chosen = jnp.where(index == source, piece, chosen)
        ordered.append(chosen)
    return ordered


def gather_receptor(receptor):
    _, terms, kx_local, ky_local, kz = receptor.shape
    n_ref = lax.axis_size("ref")
    n_rot = lax.axis_size("rot")
    rows = ky_local // n_ref
    block = lax.dynamic_slice_in_dim(receptor, lax.axis_index("ref") * rows, rows, axis=3)
    mine = jnp.concatenate([block[0], block[1]], axis=-1).astype(jnp.bfloat16)
    mine = jnp.swapaxes(mine, 1, 2)
    along_rot = gather_by_shifts(mine, "rot")
    both = gather_by_shifts(along_rot, "ref")
    both = jnp.transpose(both, (2, 0, 3, 1, 4, 5))
    return both.reshape(terms, ky_local, n_rot * kx_local, 2 * kz)


def product_kernel(*refs):
    *spec_refs, rec_ref, out_ref = refs
    lanes = out_ref.shape[-1]
    half = lanes // 2
    total = None
    term = 0
    for spec_ref in spec_refs:
        for inner in range(spec_ref.shape[0]):
            spec = spec_ref[inner].astype(jnp.float32)
            rec = rec_ref[term].astype(jnp.float32)
            term += 1
            low = lax.broadcasted_iota(jnp.int32, (1, lanes), 1) < half
            rec_turned = pltpu.roll(rec, half, 1)
            rec_real = jnp.where(low, rec, rec_turned)
            rec_imag = jnp.where(low, rec_turned, -rec)
            part = rec_real * spec + rec_imag * pltpu.roll(spec, half, 1)
            total = part if total is None else total + part
    out_ref[...] = total


def correlate(spectra, receptor):
    rots, _, kx, ky, lanes = spectra[0].shape
    terms = receptor.shape[0]
    rows = kx * ky
    block = min(rows, 256)
    specs = [part.reshape(rots, part.shape[1], rows, lanes) for part in spectra]
    rec = receptor.reshape(terms, rows, lanes)
    out = pl.pallas_call(
        product_kernel,
        grid=(rots, rows // block),
        in_specs=[
            pl.BlockSpec((None, part.shape[1], block, lanes), lambda r, i: (r, 0, i, 0))
            for part in specs
        ]
        + [pl.BlockSpec((terms, block, lanes), lambda r, i: (0, i, 0))],
        out_specs=pl.BlockSpec((None, block, lanes), lambda r, i: (r, i, 0)),
        out_shape=jax.ShapeDtypeStruct((rots, rows, lanes), jnp.float32),
        cost_estimate=pl.CostEstimate(
            flops=8 * rots * terms * rows * lanes,
            bytes_accessed=2 * (rots + 1) * terms * rows * lanes + 4 * rots * rows * lanes,
            transcendentals=0,
        ),
    )(*specs, rec)
    return out.reshape(rots, kx, ky, lanes)


def local(ligand, receptor, tile_list, tile_owner, refine_weight):
    rots, terms, x_local, ny, nz = ligand.shape
    length = nz
    n_sub = lax.axis_size("sub")
    y_local = ny // n_sub
    cos_table, sin_table = make_tables(length)
    pair = jnp.stack([cos_table, sin_table])

    chunks = 2 if terms % 2 == 0 else 1
    part_terms = terms // chunks
    pair_x = pair.reshape(2, length, n_sub, x_local)
    z_table = jnp.concatenate([cos_table, -sin_table], axis=1)
    values = ligand.astype(jnp.float32)
    spectra = []
    for chunk in range(chunks):
        part = values[:, chunk * part_terms:(chunk + 1) * part_terms]
        along_z = jnp.einsum("rtxyz,zl->rtxyl", part, z_table, precision=highest)
        along_y = jnp.einsum("ejy,rtxyl->rtxejl", pair, along_z, precision=highest)
        sending = combine_call(
            along_y.reshape(-1, 2, ny, 2 * length), 1.0, -1.0, n_sub, jnp.bfloat16,
            lax.axis_index("sub"),
        ).reshape(n_sub, rots, part_terms, x_local, y_local, 2 * length)
        along_x = sum(
            jnp.einsum(
                "ekx,rtxjl->rtjekl", pair_x[:, :, source], piece.astype(jnp.float32),
                precision=highest,
            )
            for source, piece in enumerate(by_source(exchange(sending, "sub", rotated=True)))
        )
        spectrum = combine_call(
            along_x.reshape(-1, 2, length, 2 * length), 1.0, -1.0, 1, jnp.bfloat16
        )
        spectra.append(spectrum.reshape(rots, part_terms, y_local, length, 2 * length))

    whole_receptor = gather_receptor(receptor)
    product = correlate(spectra, whole_receptor)

    back_x = jnp.einsum("exk,rjkl->xrejl", pair, product, precision=highest)
    back_x = combine_call(back_x.reshape(-1, 2, y_local, 2 * length), -1.0, 1.0, 1, jnp.float32)
    back_x = back_x.reshape(n_sub, x_local, rots, y_local, 2 * length)
    pair_y = pair.reshape(2, length, n_sub, y_local)
    back_y = sum(
        jnp.einsum("eyj,xrjl->rxeyl", pair_y[:, :, source], piece, precision=highest)
        for source, piece in enumerate(by_source(exchange(back_x, "sub")))
    )
    back_y = combine_call(back_y.reshape(-1, 2, ny, 2 * length), -1.0, 1.0, 1, jnp.float32)
    back_y = back_y.reshape(rots, x_local, ny, 2 * length)
    last_table = jnp.concatenate([cos_table, -sin_table], axis=0)
    scores = jnp.einsum("rxyl,lz->rxyz", back_y, last_table, precision=highest) / float(length**3)

    tile_cells = 8 * length
    tile_rows = scores.reshape(-1, tile_cells)
    listing = tile_list.reshape(-1)
    owners = tile_owner.reshape(-1)
    listed = listing.shape[0]
    chosen = tile_rows[listing]
    owner_count = lax.axis_size(("rot", "ref"))
    order = jnp.arange(listed, dtype=jnp.int32)
    earlier = (owners[:, None] == owners[None, :]) & (order[None, :] < order[:, None])
    slot = jnp.sum(earlier.astype(jnp.int32), axis=1)
    target = owners * CAP + slot
    placing = (jnp.arange(owner_count * CAP, dtype=jnp.int32)[:, None] == target[None, :]).astype(
        jnp.float32
    )
    done = jnp.dot(chosen, refine_weight, precision=highest)
    packed = jnp.dot(placing, done, precision=highest).reshape(owner_count, CAP, tile_cells)
    refined = lax.all_to_all(packed, ("rot", "ref"), split_axis=0, concat_axis=0, tiled=True)
    return (scores, refined.reshape(1, 1, owner_count, CAP, tile_cells))


def solution(mesh):
    in_specs = (
        P(("grp", "rot", "ref"), None, "sub", None, None),
        P("grp", None, "rot", "sub", None),
        P(("grp", "rot"), "sub", "ref", None),
        P(("grp", "rot"), "sub", "ref", None, None),
        P(),
    )
    out_specs = (
        P(("grp", "rot", "ref"), "sub", None, None),
        P(("grp", "rot", "ref"), "sub", None, None, None),
    )
    return jax.shard_map(local, mesh=mesh, in_specs=in_specs, out_specs=out_specs, check_vma=False)
```
